256 devices in a mesh: dp: 16 (over z, core), tensor: 16 (over y, x).
Axes of the slice: x: 4, y: 4, z: 8, core: 2. Of those that a mesh axis runs over, the one named last changes fastest.
Arguments:
- tokens: bfloat16 [8192, 2048], P(('dp', 'tensor')), may hold values from -6 to 6
- lengths: int32 [16, 8], P('dp'), may hold values from 1 to 128, 512 in all within a row
- group_prefix: int32 [16], replicated, may hold values from 0 to 15, as said below
- prefix_cache: bfloat16 [65536, 512], P(('dp', 'tensor')), may hold values from -340 to 340
- query_weight: bfloat16 [2048, 1024], P(None, 'tensor'), may hold values from -0.125 to 0.125
- key_weight: bfloat16 [2048, 256], replicated, may hold values from -0.375 to 0.375
- value_weight: bfloat16 [2048, 256], replicated, may hold values from -0.125 to 0.125
- out_weight: bfloat16 [1024, 2048], P('tensor'), may hold values from -0.1875 to 0.1875
- gate_up_weight: bfloat16 [2, 2048, 5120], P(None, None, 'tensor'), may hold values from -0.125 to 0.125
- down_weight: bfloat16 [5120, 2048], P('tensor'), may hold values from -0.078125 to 0.078125
Outputs:
- layer_out: bfloat16 [8192, 2048], P(('dp', 'tensor'))
The draws below stay inside these ranges and needn't reach their ends.
Inputs may be any that keep to these rules, and one draw needn't show every extreme that they name: The 8 lengths of a group sum to 512, and one of them is exactly 128. `group_prefix`: several groups may continue the same slot.
All inputs are finite; a program needn't handle non-finite values.
Results may differ from the reference program's by a relative error of at most 0.023.
Values may be sent and summed in bfloat16 or wider, within the bound.
No kernel may reach another device: no remote copies, remote signals or barrier semaphores. Data moves between devices by JAX's collectives and lax.ppermute only.
A program may use at most 64 MiB of HBM per device.

```python
import math
import jax
import jax.numpy as jnp
import numpy as np
from jax import lax

D = 2048
QH = 16
KVH = 4
HD = 64
FF = 5120
REQS = 8
TOK_G = 512
PLEN = 4096
MOSTLEN = 128
TOKENS = 8192
QW = 1024
KW = 256
N_DP = 16
N_TENSOR = 16


def draw_group_prefix(key, part):
    key_slots, key_order = jax.random.split(key)
    slots = jax.random.randint(key_slots, (N_DP,), 0, N_DP)
    order = jax.random.permutation(key_order, N_DP)
    slots = slots.at[order[0]].set(0)
    slots = slots.at[order[1]].set(N_DP - 1)
    slots = slots.at[order[2]].set((order[2] + N_DP - 1) % N_DP)
    slots = slots.at[order[3]].set((order[3] + 1) % N_DP)
    return slots.astype(jnp.int32)


def draw_prefix_cache(key, part):
    row_total = N_DP * PLEN
    kv_total = KVH * HD
    key_noise = jax.random.fold_in(key, 0)
    key_vals = jax.random.fold_in(key, 3)
    keys_part = jnp.clip(3.0 * jax.random.normal(key_noise, (row_total, kv_total), jnp.float32), -18.0, 18.0)
    values_part = jnp.clip(jax.random.normal(key_vals, (row_total, kv_total), jnp.float32), -6.0, 6.0)
    return jnp.concatenate([keys_part, values_part], axis=1).astype(jnp.bfloat16)


def block_levels(key, dims, shards, least, top_value):
    def one(position, parts):
        draws = jax.random.uniform(jax.random.fold_in(jax.random.fold_in(key, 6), position), (parts,), jnp.float32, least / len(shards), top_value / len(shards))
        return jnp.repeat(jnp.exp(draws), dims[position] // parts).reshape((-1,) + (1,) * (len(dims) - position - 1))

    loudness = one(*shards[0])
    for cut in shards[1:]:
        loudness = loudness * one(*cut)
    return loudness


def length_profile(count, total, limit, skew):
    loads = [(1 << 20) // math.isqrt(standing ** skew) + 1 for standing in range(2, count + 1)]
    spare, counts = total - limit - (count - 1), [1] * (count - 1)
    while spare > 0:
        movable = [i for i in range(count - 1) if counts[i] < limit]
        whole, left = sum([loads[i] for i in movable]), spare
        for i in movable:
            addition = min(limit - counts[i], max(1, left * loads[i] // whole), spare)
            counts[i] = counts[i] + addition
            spare = spare - addition
    return np.array([limit] + counts)


def ragged_sizes(key, number_of, total, reach, skew):
    if number_of == 2:
        one = jax.random.randint(key, (), max(1, total - reach), min(reach, total - 1) + 1)
        return jnp.stack([one, total - one])
    sizes = jnp.asarray(length_profile(number_of, total, reach, skew), jnp.int32)
    pairs = (number_of - 1) // 2
    source_of, taker = sizes[1:1 + 2 * pairs:2], sizes[2:2 + 2 * pairs:2]
    margin = jnp.minimum(source_of - 1, reach - taker)
    passed = jax.random.randint(jax.random.fold_in(key, 1), (pairs,), 0, 1 << 20) % (margin + 1)
    sizes = sizes.at[1:1 + 2 * pairs:2].set(source_of - passed).at[2:2 + 2 * pairs:2].set(taker + passed)
    return sizes[jax.random.permutation(jax.random.fold_in(key, 2), number_of)]


def noise(own_key, dims, width, limit, cuts=(), held_as=jnp.bfloat16):
    result = width * jax.random.normal(own_key, dims, jnp.float32)
    if cuts:
        result = result * block_levels(own_key, dims, cuts, -0.22, 0.18)
    return jnp.clip(result, -limit, limit).astype(held_as)


def setup_inputs(seed: int = 0) -> dict:
    seeds = jax.random.split(jax.random.key(seed), 11)
    tokens = noise(seeds[0], (TOKENS, D), 1.0, 6.0, ((0, 256),))
    lengths = jax.vmap(lambda own: ragged_sizes(own, REQS, TOK_G, MOSTLEN, 2))(jax.random.split(seeds[1], N_DP)).reshape((N_DP, REQS)).astype(jnp.int32)
    group_prefix = draw_group_prefix(jax.random.fold_in(seeds[10], 71), 0)
    prefix_cache = draw_prefix_cache(jax.random.fold_in(seeds[10], 71), 0)
    query_weight = noise(seeds[4], (D, QW), D ** -0.5, 0.125, ((1, 16),))
    key_weight = noise(seeds[5], (D, KW), (D // 9) ** -0.5, 0.375)
    value_weight = noise(seeds[6], (D, KW), D ** -0.5, 0.125)
    out_weight = noise(seeds[7], (QW, D), QW ** -0.5, 0.1875, ((0, 16),))
    gate_up_weight = noise(seeds[8], (2, D, FF), D ** -0.5, 0.125, ((2, 16),))
    down_weight = noise(seeds[9], (FF, D), FF ** -0.5, 0.078125, ((0, 16),))
    return {"tokens": tokens, "lengths": lengths, "group_prefix": group_prefix, "prefix_cache": prefix_cache, "query_weight": query_weight, "key_weight": key_weight, "value_weight": value_weight, "out_weight": out_weight, "gate_up_weight": gate_up_weight, "down_weight": down_weight}


NEG_FILL = -1e+30

def token_layout(lengths, total_rows):
    ends_at = jnp.cumsum(lengths).astype(jnp.int32)
    starts_at = (ends_at - lengths).astype(jnp.int32)
    indices = jnp.arange(total_rows, dtype=jnp.int32)
    request = lax.optimization_barrier(jnp.sum((indices[:, None] >= ends_at[None, :]).astype(jnp.int32), axis=1)).astype(jnp.int32)
    begins = lax.optimization_barrier(jnp.max(jnp.where(starts_at[None, :] <= indices[:, None], starts_at[None, :], 0), axis=1)).astype(jnp.int32)
    return ((PLEN + indices - begins).astype(jnp.float32), request)

def rope_tables(positions):
    halves = HD // 2
    steps_float = jnp.arange(halves, dtype=jnp.float32)
    inverse = jnp.exp(steps_float * (-2.0 * math.log(10000.0) / HD))
    angles = positions[:, None] * inverse[None, :]
    return (jnp.cos(angles), jnp.sin(angles))

def rotate(values, cos_table, sin_table):
    halves = values.shape[-1] // 2
    former = values[..., :halves]
    latter = values[..., halves:]
    cos_rows = cos_table[:, None, :]
    sin_rows = sin_table[:, None, :]
    return jnp.concatenate([former * cos_rows - latter * sin_rows, latter * cos_rows + former * sin_rows], axis=-1)

def norm_rows(inputs):
    floats = inputs.astype(jnp.float32)
    return (floats * lax.rsqrt(lax.optimization_barrier(jnp.mean(floats * floats, axis=-1, keepdims=True)) + 1e-05)).astype(jnp.bfloat16)

def reference(tokens, lengths, group_prefix, prefix_cache, query_weight, key_weight, value_weight, out_weight, gate_up_weight, down_weight):
    scaling = 1.0 / math.sqrt(HD)
    head_ratio = QH // KVH
    token_groups = tokens.reshape(N_DP, TOK_G, D)

    def one_group(inputs):
        group_tokens, group_lengths, slot = inputs
        positions, request = token_layout(group_lengths, TOK_G)
        cos_table, sin_table = rope_tables(positions)
        normed = norm_rows(group_tokens)
        queries = jnp.dot(normed, query_weight, preferred_element_type=jnp.float32).reshape(TOK_G, QH, HD)
        queries = rotate(queries, cos_table, sin_table).astype(jnp.bfloat16)
        new_keys = jnp.dot(normed, key_weight, preferred_element_type=jnp.float32).reshape(TOK_G, KVH, HD)
        new_keys = rotate(new_keys, cos_table, sin_table).astype(jnp.bfloat16)
        new_values = jnp.dot(normed, value_weight, preferred_element_type=jnp.float32).astype(jnp.bfloat16).reshape(TOK_G, KVH, HD)
        cached = lax.dynamic_slice_in_dim(prefix_cache, (slot * PLEN).astype(jnp.int32), PLEN, 0)
        all_keys = jnp.concatenate([cached[:, :KW].reshape(PLEN, KVH, HD), new_keys], axis=0)
        all_values = jnp.concatenate([cached[:, KW:].reshape(PLEN, KVH, HD), new_values], axis=0)
        indices = jnp.arange(TOK_G, dtype=jnp.int32)
        own_seen = (request[:, None] == request[None, :]) & (indices[None, :] <= indices[:, None])
        allowed = jnp.concatenate([jnp.ones((TOK_G, PLEN), dtype=bool), own_seen], axis=1)

        def one_head(head):
            kv_index = (head // head_ratio).astype(jnp.int32)
            query_head = lax.dynamic_index_in_dim(queries, head, axis=1, keepdims=False)
            key_head = lax.dynamic_index_in_dim(all_keys, kv_index, axis=1, keepdims=False)
            value_head = lax.dynamic_index_in_dim(all_values, kv_index, axis=1, keepdims=False)
            scores = jnp.dot(query_head, key_head.T, preferred_element_type=jnp.float32) * scaling
            scores = jnp.where(allowed, scores, NEG_FILL)
            top_score = lax.optimization_barrier(jnp.max(scores, axis=1, keepdims=True))
            exponent = jnp.exp(scores - top_score)
            total_weight = lax.optimization_barrier(jnp.sum(exponent, axis=1, keepdims=True))
            blended = jnp.dot(exponent.astype(jnp.bfloat16), value_head, preferred_element_type=jnp.float32)
            return (blended / total_weight).astype(jnp.bfloat16)
        heads_out = lax.map(one_head, jnp.arange(QH, dtype=jnp.int32))
        attended = jnp.transpose(heads_out, (1, 0, 2)).reshape(TOK_G, QW)
        grouped = attended.reshape(TOK_G, N_TENSOR, QW // N_TENSOR).astype(jnp.float32)
        out_groups = out_weight.reshape(N_TENSOR, QW // N_TENSOR, D).astype(jnp.float32)
        partials = jnp.einsum('tgk,gkd->gtd', grouped, out_groups).astype(jnp.bfloat16)
        partials = lax.optimization_barrier(partials)
        attn_sum = lax.optimization_barrier(jnp.sum(partials.astype(jnp.float32), axis=0))
        middle = (group_tokens.astype(jnp.float32) + attn_sum).astype(jnp.bfloat16)
        middle_normed = norm_rows(middle)
        gate_value = jnp.dot(middle_normed, gate_up_weight[0], preferred_element_type=jnp.float32)
        upward = jnp.dot(middle_normed, gate_up_weight[1], preferred_element_type=jnp.float32)
        hidden = (jax.nn.silu(gate_value) * upward).astype(jnp.bfloat16)
        hidden_groups = hidden.reshape(TOK_G, N_TENSOR, FF // N_TENSOR).astype(jnp.float32)
        down_groups = down_weight.reshape(N_TENSOR, FF // N_TENSOR, D).astype(jnp.float32)
        ffn_parts = jnp.einsum('tgk,gkd->gtd', hidden_groups, down_groups).astype(jnp.bfloat16)
        ffn_parts = lax.optimization_barrier(ffn_parts)
        ffn_sum = lax.optimization_barrier(jnp.sum(ffn_parts.astype(jnp.float32), axis=0))
        return (middle.astype(jnp.float32) + ffn_sum).astype(jnp.bfloat16)
    outputs = lax.map(one_group, (token_groups, lengths, group_prefix))
    return outputs.reshape(TOKENS, D)
```

```python
import math

import jax
import jax.numpy as jnp
from jax import lax
from jax.sharding import PartitionSpec as P

QH = 16
KVH = 4
HD = 64
PLEN = 4096


NEG_FILL = -1e30


def token_layout(lengths, total_rows):
    ends_at = jnp.cumsum(lengths)
    starts_at = ends_at - lengths
    indices = jnp.arange(total_rows, dtype=jnp.int32)
    request = jnp.sum((indices[:, None] >= ends_at[None, :]).astype(jnp.int32), axis=1)
    begins = jnp.max(
        jnp.where(starts_at[None, :] <= indices[:, None], starts_at[None, :], 0), axis=1
    )
    return ((PLEN + indices - begins).astype(jnp.float32), request)


def rope_tables(positions):
    halves = HD // 2
    steps_float = jnp.arange(halves, dtype=jnp.float32)
    inverse = jnp.exp(steps_float * (-2.0 * math.log(10000.0) / HD))
    angles = positions[:, None] * inverse[None, :]
    return (jnp.cos(angles), jnp.sin(angles))


def rotate(values, cos_table, sin_table):
    halves = values.shape[-1] // 2
    former = values[..., :halves]
    latter = values[..., halves:]
    cos_rows = cos_table[:, None, :]
    sin_rows = sin_table[:, None, :]
    return jnp.concatenate(
        [former * cos_rows - latter * sin_rows, latter * cos_rows + former * sin_rows], axis=-1
    )


def norm_rows(inputs):
    floats = inputs.astype(jnp.float32)
    return (floats * lax.rsqrt(jnp.mean(floats * floats, axis=-1, keepdims=True) + 1e-05)).astype(
        jnp.bfloat16
    )


def softmax_block(queries, keys_block, values_block, scaling, allowed):
    scores = (
        jnp.einsum("thd,nhd->thn", queries, keys_block, preferred_element_type=jnp.float32)
        * scaling
    )
    if allowed is not None:
        scores = jnp.where(allowed, scores, NEG_FILL)
    top_score = jnp.max(scores, axis=2)
    exponent = jnp.exp(scores - top_score[:, :, None])
    weight = jnp.sum(exponent, axis=2)
    blended = jnp.einsum(
        "thn,nhd->thd",
        exponent.astype(jnp.bfloat16),
        values_block,
        preferred_element_type=jnp.float32,
    )
    return (top_score, weight, blended)


def merge_states(former, latter):
    top_one, weight_one, blend_one = former
    top_two, weight_two, blend_two = latter
    overall = jnp.maximum(top_one, top_two)
    factor_one = jnp.exp(top_one - overall)
    factor_two = jnp.exp(top_two - overall)
    return (
        overall,
        weight_one * factor_one + weight_two * factor_two,
        blend_one * factor_one[:, :, None] + blend_two * factor_two[:, :, None],
    )


def gather_rows(values, axis):
    count = lax.axis_size(axis)
    copies = jnp.broadcast_to(values[None], (count,) + values.shape)
    received = lax.all_to_all(copies, axis, 0, 0, tiled=True)
    return received.reshape((count * values.shape[0],) + values.shape[1:])


def sum_scatter_rows(values, axis):
    count = lax.axis_size(axis)
    parts = values.reshape((count, values.shape[0] // count) + values.shape[1:])
    received = lax.all_to_all(parts, axis, 0, 0, tiled=True)
    return jnp.sum(received.astype(jnp.float32), axis=0)


def on_device(
    tokens,
    lengths,
    group_prefix,
    prefix_cache,
    query_weight,
    key_weight,
    value_weight,
    out_weight,
    gate_up_weight,
    down_weight,
):
    tensor_count = lax.axis_size("tensor")
    tensor_rank = lax.axis_index("tensor")
    group_rank = lax.axis_index("dp")
    row_count = tokens.shape[0]
    group_tokens = row_count * tensor_count
    local_heads = query_weight.shape[1] // HD
    head_ratio = QH // KVH
    local_kv = max(1, local_heads // head_ratio)
    repeat_by = local_heads // local_kv
    kv_first = tensor_rank * local_heads // head_ratio
    kv_total = KVH * HD
    query_width = local_heads * HD
    kv_width = local_kv * HD
    scaling = 1.0 / math.sqrt(HD)
    positions, request = token_layout(lengths[0], group_tokens)
    cos_table, sin_table = rope_tables(positions)
    key_cols = lax.dynamic_slice_in_dim(key_weight, kv_first * HD, kv_width, 1)
    value_cols = lax.dynamic_slice_in_dim(value_weight, kv_first * HD, kv_width, 1)
    projection = jnp.concatenate([query_weight, key_cols, value_cols], axis=1)

    slot_wanted = group_prefix[group_rank]
    shard_rows = prefix_cache.shape[0]
    every_slot = lax.all_gather(prefix_cache, "dp", axis=0, tiled=True)
    chosen = lax.dynamic_slice_in_dim(every_slot, slot_wanted * shard_rows, shard_rows, 0)
    by_head = chosen.reshape(shard_rows, 2, KVH // local_kv, kv_width)
    by_head = jnp.transpose(by_head, (2, 0, 1, 3)).reshape(KVH // local_kv, shard_rows, 2 * kv_width)
    wanted_by = (jnp.arange(tensor_count) * local_heads // head_ratio) // local_kv
    outgoing = jnp.take(by_head, wanted_by, axis=0)
    incoming = lax.all_to_all(outgoing, "tensor", 0, 0, tiled=True)
    seg_rows = tensor_count * shard_rows
    incoming = incoming.reshape(seg_rows, 2 * kv_width)
    keys_block = jnp.repeat(incoming[:, :kv_width].reshape(seg_rows, local_kv, HD), repeat_by, axis=1)
    values_block = jnp.repeat(incoming[:, kv_width:].reshape(seg_rows, local_kv, HD), repeat_by, axis=1)

    normed = norm_rows(tokens)
    segment = gather_rows(normed, "tensor")
    seg_rows = segment.shape[0]
    mapped = jnp.dot(segment, projection, preferred_element_type=jnp.float32)
    query_part = rotate(
        mapped[:, :query_width].reshape(seg_rows, local_heads, HD), cos_table, sin_table
    )
    key_part = rotate(
        mapped[:, query_width : query_width + kv_width].reshape(seg_rows, local_kv, HD),
        cos_table,
        sin_table,
    )
    projected = jnp.concatenate(
        [
            query_part.reshape(seg_rows, query_width),
            key_part.reshape(seg_rows, kv_width),
            mapped[:, query_width + kv_width :],
        ],
        axis=1,
    ).astype(jnp.bfloat16)
    queries = projected[:, :query_width].reshape(group_tokens, local_heads, HD)
    own_keys = jnp.repeat(
        projected[:, query_width : query_width + kv_width].reshape(group_tokens, local_kv, HD),
        repeat_by,
        axis=1,
    )
    own_values = jnp.repeat(
        projected[:, query_width + kv_width :].reshape(group_tokens, local_kv, HD),
        repeat_by,
        axis=1,
    )
    start_state = (
        jnp.full((group_tokens, local_heads), NEG_FILL, jnp.float32),
        jnp.zeros((group_tokens, local_heads), jnp.float32),
        jnp.zeros((group_tokens, local_heads, HD), jnp.float32),
    )
    prefix_state = merge_states(
        start_state, softmax_block(queries, keys_block, values_block, scaling, None)
    )
    indices = jnp.arange(group_tokens, dtype=jnp.int32)
    allowed = (request[:, None] == request[None, :]) & (indices[None, :] <= indices[:, None])
    suffix_state = softmax_block(queries, own_keys, own_values, scaling, allowed[:, None, :])
    top_score, weight, blended = merge_states(prefix_state, suffix_state)
    attended = (
        (blended / weight[:, :, None]).astype(jnp.bfloat16).reshape(group_tokens, query_width)
    )
    attn_sum = sum_scatter_rows(
        jnp.dot(attended, out_weight, preferred_element_type=jnp.float32).astype(jnp.bfloat16),
        "tensor",
    )
    middle = (tokens.astype(jnp.float32) + attn_sum).astype(jnp.bfloat16)
    segment = gather_rows(norm_rows(middle), "tensor")
    gate_value = jnp.dot(segment, gate_up_weight[0], preferred_element_type=jnp.float32)
    upward = jnp.dot(segment, gate_up_weight[1], preferred_element_type=jnp.float32)
    hidden = (jax.nn.silu(gate_value) * upward).astype(jnp.bfloat16)
    ffn_sum = sum_scatter_rows(
        jnp.dot(hidden, down_weight, preferred_element_type=jnp.float32).astype(jnp.bfloat16),
        "tensor",
    )
    return (middle.astype(jnp.float32) + ffn_sum).astype(jnp.bfloat16)


def solution(mesh):
    return jax.shard_map(
        on_device,
        mesh=mesh,
        in_specs=(
            P(("dp", "tensor"), None),
            P("dp", None),
            P(),
            P(("dp", "tensor"), None),
            P(None, "tensor"),
            P(),
            P(),
            P("tensor", None),
            P(None, None, "tensor"),
            P("tensor", None),
        ),
        out_specs=P(("dp", "tensor"), None),
        check_vma=False,
    )
```

```python
import math

import jax
import jax.numpy as jnp
from jax import lax
from jax.sharding import PartitionSpec as P

QH = 16
KVH = 4
HD = 64
PLEN = 4096


NEG_FILL = -1e30


def token_layout(lengths, total_rows):
    ends_at = jnp.cumsum(lengths)
    starts_at = ends_at - lengths
    indices = jnp.arange(total_rows, dtype=jnp.int32)
    request = jnp.sum((indices[:, None] >= ends_at[None, :]).astype(jnp.int32), axis=1)
    begins = jnp.max(
        jnp.where(starts_at[None, :] <= indices[:, None], starts_at[None, :], 0), axis=1
    )
    return ((PLEN + indices - begins).astype(jnp.float32), request)


def rope_tables(positions):
    halves = HD // 2
    steps_float = jnp.arange(halves, dtype=jnp.float32)
    inverse = jnp.exp(steps_float * (-2.0 * math.log(10000.0) / HD))
    angles = positions[:, None] * inverse[None, :]
    return (jnp.cos(angles), jnp.sin(angles))


def rotate(values, cos_table, sin_table):
    halves = values.shape[-1] // 2
    former = values[..., :halves]
    latter = values[..., halves:]
    cos_rows = cos_table[:, None, :]
    sin_rows = sin_table[:, None, :]
    return jnp.concatenate(
        [former * cos_rows - latter * sin_rows, latter * cos_rows + former * sin_rows], axis=-1
    )


def norm_rows(inputs):
    floats = inputs.astype(jnp.float32)
    return (floats * lax.rsqrt(jnp.mean(floats * floats, axis=-1, keepdims=True) + 1e-05)).astype(
        jnp.bfloat16
    )


def softmax_block(queries, keys_block, values_block, scaling, allowed):
    scores = (
        jnp.einsum("thd,nhd->thn", queries, keys_block, preferred_element_type=jnp.float32)
        * scaling
    )
    if allowed is not None:
        scores = jnp.where(allowed, scores, NEG_FILL)
    top_score = jnp.max(scores, axis=2)
    exponent = jnp.exp(scores - top_score[:, :, None])
    weight = jnp.sum(exponent, axis=2)
    blended = jnp.einsum(
        "thn,nhd->thd",
        exponent.astype(jnp.bfloat16),
        values_block,
        preferred_element_type=jnp.float32,
    )
    return (top_score, weight, blended)


def merge_states(former, latter):
    top_one, weight_one, blend_one = former
    top_two, weight_two, blend_two = latter
    overall = jnp.maximum(top_one, top_two)
    factor_one = jnp.exp(top_one - overall)
    factor_two = jnp.exp(top_two - overall)
    return (
        overall,
        weight_one * factor_one + weight_two * factor_two,
        blend_one * factor_one[:, :, None] + blend_two * factor_two[:, :, None],
    )


def gather_rows(values, axis):
    count = lax.axis_size(axis)
    copies = jnp.broadcast_to(values[None], (count,) + values.shape)
    received = lax.all_to_all(copies, axis, 0, 0, tiled=True)
    return received.reshape((count * values.shape[0],) + values.shape[1:])


def sum_scatter_rows(values, axis):
    count = lax.axis_size(axis)
    parts = values.reshape((count, values.shape[0] // count) + values.shape[1:])
    received = lax.all_to_all(parts, axis, 0, 0, tiled=True)
    return jnp.sum(received.astype(jnp.float32), axis=0)


def on_device(
    tokens,
    lengths,
    group_prefix,
    prefix_cache,
    query_weight,
    key_weight,
    value_weight,
    out_weight,
    gate_up_weight,
    down_weight,
):
    tensor_count = lax.axis_size("tensor")
    tensor_rank = lax.axis_index("tensor")
    group_rank = lax.axis_index("dp")
    row_count = tokens.shape[0]
    group_tokens = row_count * tensor_count
    local_heads = query_weight.shape[1] // HD
    head_ratio = QH // KVH
    local_kv = max(1, local_heads // head_ratio)
    repeat_by = local_heads // local_kv
    kv_first = tensor_rank * local_heads // head_ratio
    kv_total = KVH * HD
    query_width = local_heads * HD
    kv_width = local_kv * HD
    scaling = 1.0 / math.sqrt(HD)
    positions, request = token_layout(lengths[0], group_tokens)
    cos_table, sin_table = rope_tables(positions)
    key_cols = lax.dynamic_slice_in_dim(key_weight, kv_first * HD, kv_width, 1)
    value_cols = lax.dynamic_slice_in_dim(value_weight, kv_first * HD, kv_width, 1)
    projection = jnp.concatenate([query_weight, key_cols, value_cols], axis=1)

    slot_wanted = group_prefix[group_rank]
    shard_rows = prefix_cache.shape[0]
    every_slot = lax.all_gather(prefix_cache, "dp", axis=0, tiled=True)
    every_slot, out_rows = lax.optimization_barrier((every_slot, out_weight))
    out_full = lax.all_gather(out_rows, "tensor", axis=0, tiled=True)
    chosen = lax.dynamic_slice_in_dim(every_slot, slot_wanted * shard_rows, shard_rows, 0)
    by_head = chosen.reshape(shard_rows, 2, KVH // local_kv, kv_width)
    by_head = jnp.transpose(by_head, (2, 0, 1, 3)).reshape(KVH // local_kv, shard_rows, 2 * kv_width)
    wanted_by = (jnp.arange(tensor_count) * local_heads // head_ratio) // local_kv
    outgoing = jnp.take(by_head, wanted_by, axis=0)
    incoming = lax.all_to_all(outgoing, "tensor", 0, 0, tiled=True)
    seg_rows = tensor_count * shard_rows
    incoming = incoming.reshape(seg_rows, 2 * kv_width)
    keys_block = jnp.repeat(incoming[:, :kv_width].reshape(seg_rows, local_kv, HD), repeat_by, axis=1)
    values_block = jnp.repeat(incoming[:, kv_width:].reshape(seg_rows, local_kv, HD), repeat_by, axis=1)

    normed = norm_rows(tokens)
    segment = gather_rows(normed, "tensor")
    seg_rows = segment.shape[0]
    mapped = jnp.dot(segment, projection, preferred_element_type=jnp.float32)
    query_part = rotate(
        mapped[:, :query_width].reshape(seg_rows, local_heads, HD), cos_table, sin_table
    )
    key_part = rotate(
        mapped[:, query_width : query_width + kv_width].reshape(seg_rows, local_kv, HD),
        cos_table,
        sin_table,
    )
    projected = jnp.concatenate(
        [
            query_part.reshape(seg_rows, query_width),
            key_part.reshape(seg_rows, kv_width),
            mapped[:, query_width + kv_width :],
        ],
        axis=1,
    ).astype(jnp.bfloat16)
    queries = projected[:, :query_width].reshape(group_tokens, local_heads, HD)
    own_keys = jnp.repeat(
        projected[:, query_width : query_width + kv_width].reshape(group_tokens, local_kv, HD),
        repeat_by,
        axis=1,
    )
    own_values = jnp.repeat(
        projected[:, query_width + kv_width :].reshape(group_tokens, local_kv, HD),
        repeat_by,
        axis=1,
    )
    start_state = (
        jnp.full((group_tokens, local_heads), NEG_FILL, jnp.float32),
        jnp.zeros((group_tokens, local_heads), jnp.float32),
        jnp.zeros((group_tokens, local_heads, HD), jnp.float32),
    )
    prefix_state = merge_states(
        start_state, softmax_block(queries, keys_block, values_block, scaling, None)
    )
    indices = jnp.arange(group_tokens, dtype=jnp.int32)
    allowed = (request[:, None] == request[None, :]) & (indices[None, :] <= indices[:, None])
    suffix_state = softmax_block(queries, own_keys, own_values, scaling, allowed[:, None, :])
    top_score, weight, blended = merge_states(prefix_state, suffix_state)
    attended = (blended / weight[:, :, None]).astype(jnp.bfloat16)
    attended = lax.all_to_all(
        attended.reshape(tensor_count, row_count, query_width), "tensor", 0, 0, tiled=True
    )
    feature_groups = out_full.shape[0] // query_width
    partials = jnp.einsum(
        "grk,gkd->grd",
        attended,
        out_full.reshape(feature_groups, query_width, out_full.shape[1]),
        preferred_element_type=jnp.float32,
    ).astype(jnp.bfloat16)
    attn_sum = jnp.sum(partials.astype(jnp.float32), axis=0)
    middle = (tokens.astype(jnp.float32) + attn_sum).astype(jnp.bfloat16)
    segment = gather_rows(norm_rows(middle), "tensor")
    gate_value = jnp.dot(segment, gate_up_weight[0], preferred_element_type=jnp.float32)
    upward = jnp.dot(segment, gate_up_weight[1], preferred_element_type=jnp.float32)
    hidden = (jax.nn.silu(gate_value) * upward).astype(jnp.bfloat16)
    ffn_sum = sum_scatter_rows(
        jnp.dot(hidden, down_weight, preferred_element_type=jnp.float32).astype(jnp.bfloat16),
        "tensor",
    )
    return (middle.astype(jnp.float32) + ffn_sum).astype(jnp.bfloat16)


def solution(mesh):
    return jax.shard_map(
        on_device,
        mesh=mesh,
        in_specs=(
            P(("dp", "tensor"), None),
            P("dp", None),
            P(),
            P(("dp", "tensor"), None),
            P(None, "tensor"),
            P(),
            P(),
            P("tensor", None),
            P(None, None, "tensor"),
            P("tensor", None),
        ),
        out_specs=P(("dp", "tensor"), None),
        check_vma=False,
    )
```

```python
import math

import jax
import jax.numpy as jnp
from jax import lax
from jax.sharding import PartitionSpec as P

QH = 16
KVH = 4
HD = 64
PLEN = 4096


NEG_FILL = -1e30


def token_layout(lengths, total_rows):
    ends_at = jnp.cumsum(lengths)
    starts_at = ends_at - lengths
    indices = jnp.arange(total_rows, dtype=jnp.int32)
    request = jnp.sum((indices[:, None] >= ends_at[None, :]).astype(jnp.int32), axis=1)
    begins = jnp.max(
        jnp.where(starts_at[None, :] <= indices[:, None], starts_at[None, :], 0), axis=1
    )
    return ((PLEN + indices - begins).astype(jnp.float32), request)


def rope_tables(positions):
    halves = HD // 2
    steps_float = jnp.arange(halves, dtype=jnp.float32)
    inverse = jnp.exp(steps_float * (-2.0 * math.log(10000.0) / HD))
    angles = positions[:, None] * inverse[None, :]
    return (jnp.cos(angles), jnp.sin(angles))


def rotate(values, cos_table, sin_table):
    halves = values.shape[-1] // 2
    former = values[..., :halves]
    latter = values[..., halves:]
    cos_rows = cos_table[:, None, :]
    sin_rows = sin_table[:, None, :]
    return jnp.concatenate(
        [former * cos_rows - latter * sin_rows, latter * cos_rows + former * sin_rows], axis=-1
    )


def norm_rows(inputs):
    floats = inputs.astype(jnp.float32)
    return (floats * lax.rsqrt(jnp.mean(floats * floats, axis=-1, keepdims=True) + 1e-05)).astype(
        jnp.bfloat16
    )


def softmax_block(queries, keys_block, values_block, scaling, allowed):
    scores = (
        jnp.einsum("thd,nhd->thn", queries, keys_block, preferred_element_type=jnp.float32)
        * scaling
    )
    if allowed is not None:
        scores = jnp.where(allowed, scores, NEG_FILL)
    top_score = jnp.max(scores, axis=2)
    exponent = jnp.exp(scores - top_score[:, :, None])
    weight = jnp.sum(exponent, axis=2)
    blended = jnp.einsum(
        "thn,nhd->thd",
        exponent.astype(jnp.bfloat16),
        values_block,
        preferred_element_type=jnp.float32,
    )
    return (top_score, weight, blended)


def merge_states(former, latter):
    top_one, weight_one, blend_one = former
    top_two, weight_two, blend_two = latter
    overall = jnp.maximum(top_one, top_two)
    factor_one = jnp.exp(top_one - overall)
    factor_two = jnp.exp(top_two - overall)
    return (
        overall,
        weight_one * factor_one + weight_two * factor_two,
        blend_one * factor_one[:, :, None] + blend_two * factor_two[:, :, None],
    )


def gather_rows(values, axis):
    count = lax.axis_size(axis)
    copies = jnp.broadcast_to(values[None], (count,) + values.shape)
    received = lax.all_to_all(copies, axis, 0, 0, tiled=True)
    return received.reshape((count * values.shape[0],) + values.shape[1:])


def sum_scatter_rows(values, axis):
    count = lax.axis_size(axis)
    parts = values.reshape((count, values.shape[0] // count) + values.shape[1:])
    received = lax.all_to_all(parts, axis, 0, 0, tiled=True)
    return jnp.sum(received.astype(jnp.float32), axis=0)


CORES = 2


def fetch_slot(prefix_cache, group_prefix, group_rank):
    group_count = lax.axis_size("dp")
    chips = group_count // CORES
    chip = group_rank // CORES
    core = group_rank % CORES
    onward = [(i, (i + CORES) % group_count) for i in range(group_count)]
    backward = [(i, (i - CORES) % group_count) for i in range(group_count)]
    held = [None] * chips
    held[0] = prefix_cache
    ahead = prefix_cache
    behind = prefix_cache
    for step in range(1, chips // 2 + 1):
        ahead = lax.ppermute(ahead, "dp", onward)
        held[(chips - step) % chips] = ahead
        if step < chips - step:
            behind = lax.ppermute(behind, "dp", backward)
            held[step] = behind
    held = jnp.stack(held)
    slot_wanted = group_prefix[group_rank]
    partner_slot = group_prefix[group_rank ^ 1]
    mine = lax.dynamic_index_in_dim(held, (slot_wanted // CORES - chip) % chips, 0, keepdims=False)
    theirs = lax.dynamic_index_in_dim(held, (partner_slot // CORES - chip) % chips, 0, keepdims=False)
    swapped = lax.ppermute(theirs, "dp", [(i, i ^ 1) for i in range(group_count)])
    return jnp.where(slot_wanted % CORES == core, mine, swapped)


def on_device(
    tokens,
    lengths,
    group_prefix,
    prefix_cache,
    query_weight,
    key_weight,
    value_weight,
    out_weight,
    gate_up_weight,
    down_weight,
):
    tensor_count = lax.axis_size("tensor")
    tensor_rank = lax.axis_index("tensor")
    group_rank = lax.axis_index("dp")
    row_count = tokens.shape[0]
    group_tokens = row_count * tensor_count
    local_heads = query_weight.shape[1] // HD
    head_ratio = QH // KVH
    local_kv = max(1, local_heads // head_ratio)
    repeat_by = local_heads // local_kv
    kv_first = tensor_rank * local_heads // head_ratio
    kv_total = KVH * HD
    query_width = local_heads * HD
    kv_width = local_kv * HD
    scaling = 1.0 / math.sqrt(HD)
    positions, request = token_layout(lengths[0], group_tokens)
    cos_table, sin_table = rope_tables(positions)
    key_cols = lax.dynamic_slice_in_dim(key_weight, kv_first * HD, kv_width, 1)
    value_cols = lax.dynamic_slice_in_dim(value_weight, kv_first * HD, kv_width, 1)
    projection = jnp.concatenate([query_weight, key_cols, value_cols], axis=1)

    shard_rows = prefix_cache.shape[0]
    chosen = fetch_slot(prefix_cache, group_prefix, group_rank)
    out_full = lax.all_gather(out_weight, "tensor", axis=0, tiled=True)
    by_head = chosen.reshape(shard_rows, 2, KVH // local_kv, kv_width)
    by_head = jnp.transpose(by_head, (2, 0, 1, 3)).reshape(KVH // local_kv, shard_rows, 2 * kv_width)
    wanted_by = (jnp.arange(tensor_count) * local_heads // head_ratio) // local_kv
    outgoing = jnp.take(by_head, wanted_by, axis=0)
    incoming = lax.all_to_all(outgoing, "tensor", 0, 0, tiled=True)
    seg_rows = tensor_count * shard_rows
    incoming = incoming.reshape(seg_rows, 2 * kv_width)
    keys_block = jnp.repeat(incoming[:, :kv_width].reshape(seg_rows, local_kv, HD), repeat_by, axis=1)
    values_block = jnp.repeat(incoming[:, kv_width:].reshape(seg_rows, local_kv, HD), repeat_by, axis=1)

    normed = norm_rows(tokens)
    segment = gather_rows(normed, "tensor")
    seg_rows = segment.shape[0]
    mapped = jnp.dot(segment, projection, preferred_element_type=jnp.float32)
    query_part = rotate(
        mapped[:, :query_width].reshape(seg_rows, local_heads, HD), cos_table, sin_table
    )
    key_part = rotate(
        mapped[:, query_width : query_width + kv_width].reshape(seg_rows, local_kv, HD),
        cos_table,
        sin_table,
    )
    projected = jnp.concatenate(
        [
            query_part.reshape(seg_rows, query_width),
            key_part.reshape(seg_rows, kv_width),
            mapped[:, query_width + kv_width :],
        ],
        axis=1,
    ).astype(jnp.bfloat16)
    queries = projected[:, :query_width].reshape(group_tokens, local_heads, HD)
    own_keys = jnp.repeat(
        projected[:, query_width : query_width + kv_width].reshape(group_tokens, local_kv, HD),
        repeat_by,
        axis=1,
    )
    own_values = jnp.repeat(
        projected[:, query_width + kv_width :].reshape(group_tokens, local_kv, HD),
        repeat_by,
        axis=1,
    )
    start_state = (
        jnp.full((group_tokens, local_heads), NEG_FILL, jnp.float32),
        jnp.zeros((group_tokens, local_heads), jnp.float32),
        jnp.zeros((group_tokens, local_heads, HD), jnp.float32),
    )
    prefix_state = merge_states(
        start_state, softmax_block(queries, keys_block, values_block, scaling, None)
    )
    indices = jnp.arange(group_tokens, dtype=jnp.int32)
    allowed = (request[:, None] == request[None, :]) & (indices[None, :] <= indices[:, None])
    suffix_state = softmax_block(queries, own_keys, own_values, scaling, allowed[:, None, :])
    top_score, weight, blended = merge_states(prefix_state, suffix_state)
    attended = (blended / weight[:, :, None]).astype(jnp.bfloat16)
    attended = lax.all_to_all(
        attended.reshape(tensor_count, row_count, query_width), "tensor", 0, 0, tiled=True
    )
    feature_groups = out_full.shape[0] // query_width
    partials = jnp.einsum(
        "grk,gkd->grd",
        attended,
        out_full.reshape(feature_groups, query_width, out_full.shape[1]),
        preferred_element_type=jnp.float32,
    ).astype(jnp.bfloat16)
    attn_sum = jnp.sum(partials.astype(jnp.float32), axis=0)
    middle = (tokens.astype(jnp.float32) + attn_sum).astype(jnp.bfloat16)
    segment = gather_rows(norm_rows(middle), "tensor")
    gate_value = jnp.dot(segment, gate_up_weight[0], preferred_element_type=jnp.float32)
    upward = jnp.dot(segment, gate_up_weight[1], preferred_element_type=jnp.float32)
    hidden = (jax.nn.silu(gate_value) * upward).astype(jnp.bfloat16)
    ffn_sum = sum_scatter_rows(
        jnp.dot(hidden, down_weight, preferred_element_type=jnp.float32).astype(jnp.bfloat16),
        "tensor",
    )
    return (middle.astype(jnp.float32) + ffn_sum).astype(jnp.bfloat16)


def solution(mesh):
    return jax.shard_map(
        on_device,
        mesh=mesh,
        in_specs=(
            P(("dp", "tensor"), None),
            P("dp", None),
            P(),
            P(("dp", "tensor"), None),
            P(None, "tensor"),
            P(),
            P(),
            P("tensor", None),
            P(None, None, "tensor"),
            P("tensor", None),
        ),
        out_specs=P(("dp", "tensor"), None),
        check_vma=False,
    )
```

```python
import math

import jax
import jax.numpy as jnp
from jax import lax
from jax.sharding import PartitionSpec as P

QH = 16
KVH = 4
HD = 64
PLEN = 4096


NEG_FILL = -1e30


def token_layout(lengths, total_rows):
    ends_at = jnp.cumsum(lengths)
    starts_at = ends_at - lengths
    indices = jnp.arange(total_rows, dtype=jnp.int32)
    request = jnp.sum((indices[:, None] >= ends_at[None, :]).astype(jnp.int32), axis=1)
    begins = jnp.max(
        jnp.where(starts_at[None, :] <= indices[:, None], starts_at[None, :], 0), axis=1
    )
    return ((PLEN + indices - begins).astype(jnp.float32), request)


def rope_tables(positions):
    halves = HD // 2
    steps_float = jnp.arange(halves, dtype=jnp.float32)
    inverse = jnp.exp(steps_float * (-2.0 * math.log(10000.0) / HD))
    angles = positions[:, None] * inverse[None, :]
    return (jnp.cos(angles), jnp.sin(angles))


def rotate(values, cos_table, sin_table):
    halves = values.shape[-1] // 2
    former = values[..., :halves]
    latter = values[..., halves:]
    cos_rows = cos_table[:, None, :]
    sin_rows = sin_table[:, None, :]
    return jnp.concatenate(
        [former * cos_rows - latter * sin_rows, latter * cos_rows + former * sin_rows], axis=-1
    )


def norm_rows(inputs):
    floats = inputs.astype(jnp.float32)
    return (floats * lax.rsqrt(jnp.mean(floats * floats, axis=-1, keepdims=True) + 1e-05)).astype(
        jnp.bfloat16
    )


def softmax_block(queries, keys_block, values_block, scaling, allowed):
    scores = (
        jnp.einsum("thd,nhd->thn", queries, keys_block, preferred_element_type=jnp.float32)
        * scaling
    )
    if allowed is not None:
        scores = jnp.where(allowed, scores, NEG_FILL)
    top_score = jnp.max(scores, axis=2)
    exponent = jnp.exp(scores - top_score[:, :, None])
    weight = jnp.sum(exponent, axis=2)
    blended = jnp.einsum(
        "thn,nhd->thd",
        exponent.astype(jnp.bfloat16),
        values_block,
        preferred_element_type=jnp.float32,
    )
    return (top_score, weight, blended)


def merge_states(former, latter):
    top_one, weight_one, blend_one = former
    top_two, weight_two, blend_two = latter
    overall = jnp.maximum(top_one, top_two)
    factor_one = jnp.exp(top_one - overall)
    factor_two = jnp.exp(top_two - overall)
    return (
        overall,
        weight_one * factor_one + weight_two * factor_two,
        blend_one * factor_one[:, :, None] + blend_two * factor_two[:, :, None],
    )


def gather_rows(values, axis):
    count = lax.axis_size(axis)
    copies = jnp.broadcast_to(values[None], (count,) + values.shape)
    received = lax.all_to_all(copies, axis, 0, 0, tiled=True)
    return received.reshape((count * values.shape[0],) + values.shape[1:])


def sum_scatter_rows(values, axis):
    count = lax.axis_size(axis)
    parts = values.reshape((count, values.shape[0] // count) + values.shape[1:])
    received = lax.all_to_all(parts, axis, 0, 0, tiled=True)
    return jnp.sum(received.astype(jnp.float32), axis=0)


CORES = 2


def fetch_slot(prefix_cache, group_prefix, group_rank):
    group_count = lax.axis_size("dp")
    chips = group_count // CORES
    chip = group_rank // CORES
    core = group_rank % CORES
    onward = [(i, (i + CORES) % group_count) for i in range(group_count)]
    backward = [(i, (i - CORES) % group_count) for i in range(group_count)]
    held = [None] * chips
    held[0] = prefix_cache
    ahead = prefix_cache
    behind = prefix_cache
    for step in range(1, chips // 2 + 1):
        ahead = lax.ppermute(ahead, "dp", onward)
        held[(chips - step) % chips] = ahead
        if step < chips - step:
            behind = lax.ppermute(behind, "dp", backward)
            held[step] = behind
    held = jnp.stack(held)
    slot_wanted = group_prefix[group_rank]
    partner_slot = group_prefix[group_rank ^ 1]
    mine = lax.dynamic_index_in_dim(held, (slot_wanted // CORES - chip) % chips, 0, keepdims=False)
    theirs = lax.dynamic_index_in_dim(held, (partner_slot // CORES - chip) % chips, 0, keepdims=False)
    swapped = lax.ppermute(theirs, "dp", [(i, i ^ 1) for i in range(group_count)])
    return jnp.where(slot_wanted % CORES == core, mine, swapped)


def on_device(
    tokens,
    lengths,
    group_prefix,
    prefix_cache,
    query_weight,
    key_weight,
    value_weight,
    out_weight,
    gate_up_weight,
    down_weight,
):
    tensor_count = lax.axis_size("tensor")
    tensor_rank = lax.axis_index("tensor")
    group_rank = lax.axis_index("dp")
    row_count = tokens.shape[0]
    group_tokens = row_count * tensor_count
    local_heads = query_weight.shape[1] // HD
    head_ratio = QH // KVH
    local_kv = max(1, local_heads // head_ratio)
    repeat_by = local_heads // local_kv
    kv_first = tensor_rank * local_heads // head_ratio
    kv_total = KVH * HD
    query_width = local_heads * HD
    kv_width = local_kv * HD
    scaling = 1.0 / math.sqrt(HD)
    positions, request = token_layout(lengths[0], group_tokens)
    cos_table, sin_table = rope_tables(positions)
    key_cols = lax.dynamic_slice_in_dim(key_weight, kv_first * HD, kv_width, 1)
    value_cols = lax.dynamic_slice_in_dim(value_weight, kv_first * HD, kv_width, 1)
    projection = jnp.concatenate([query_weight, key_cols, value_cols], axis=1)

    chosen = fetch_slot(prefix_cache, group_prefix, group_rank)
    out_full = lax.all_gather(out_weight, "tensor", axis=0, tiled=True)
    chunk_rows = chosen.shape[0]
    chunk_keys = jnp.repeat(chosen[:, :kv_total].reshape(chunk_rows, KVH, HD), head_ratio, axis=1)
    chunk_values = jnp.repeat(chosen[:, kv_total:].reshape(chunk_rows, KVH, HD), head_ratio, axis=1)

    normed = norm_rows(tokens)
    segment = gather_rows(normed, "tensor")
    seg_rows = segment.shape[0]
    mapped = jnp.dot(segment, projection, preferred_element_type=jnp.float32)
    query_part = rotate(
        mapped[:, :query_width].reshape(seg_rows, local_heads, HD), cos_table, sin_table
    )
    key_part = rotate(
        mapped[:, query_width : query_width + kv_width].reshape(seg_rows, local_kv, HD),
        cos_table,
        sin_table,
    )
    projected = jnp.concatenate(
        [
            query_part.reshape(seg_rows, query_width),
            key_part.reshape(seg_rows, kv_width),
            mapped[:, query_width + kv_width :],
        ],
        axis=1,
    ).astype(jnp.bfloat16)
    queries = projected[:, :query_width].reshape(group_tokens, local_heads, HD)
    own_keys = jnp.repeat(
        projected[:, query_width : query_width + kv_width].reshape(group_tokens, local_kv, HD),
        repeat_by,
        axis=1,
    )
    own_values = jnp.repeat(
        projected[:, query_width + kv_width :].reshape(group_tokens, local_kv, HD),
        repeat_by,
        axis=1,
    )
    every_query = lax.all_to_all(
        jnp.broadcast_to(queries[None], (tensor_count,) + queries.shape), "tensor", 0, 0, tiled=True
    )
    every_query = jnp.transpose(every_query, (1, 0, 2, 3)).reshape(group_tokens, QH, HD)
    chunk_state = softmax_block(every_query, chunk_keys, chunk_values, scaling, None)

    indices = jnp.arange(group_tokens, dtype=jnp.int32)
    allowed = (request[:, None] == request[None, :]) & (indices[None, :] <= indices[:, None])
    suffix_top, suffix_weight, suffix_blend = softmax_block(
        queries, own_keys, own_values, scaling, allowed[:, None, :]
    )
    head_first = tensor_rank * local_heads
    suffix_state = (
        lax.dynamic_update_slice_in_dim(
            jnp.full((group_tokens, QH), NEG_FILL, jnp.float32), suffix_top, head_first, 1
        ),
        lax.dynamic_update_slice_in_dim(
            jnp.zeros((group_tokens, QH), jnp.float32), suffix_weight, head_first, 1
        ),
        lax.dynamic_update_slice_in_dim(
            jnp.zeros((group_tokens, QH, HD), jnp.float32), suffix_blend, head_first, 1
        ),
    )
    top_score, weight, blended = merge_states(chunk_state, suffix_state)
    packed = jnp.concatenate([blended, top_score[:, :, None], weight[:, :, None]], axis=2)
    packed = lax.all_to_all(
        packed.reshape((tensor_count, row_count) + packed.shape[1:]), "tensor", 0, 0, tiled=True
    )
    part_blend = packed[..., :HD]
    part_top = packed[..., HD]
    part_weight = packed[..., HD + 1]
    overall = jnp.max(part_top, axis=0)
    factor = jnp.exp(part_top - overall[None])
    weight = jnp.sum(part_weight * factor, axis=0)
    blended = jnp.sum(part_blend * factor[..., None], axis=0)
    attended = (blended / weight[:, :, None]).astype(jnp.bfloat16)
    attended = attended.reshape(row_count, tensor_count, query_width).transpose(1, 0, 2)
    feature_groups = out_full.shape[0] // query_width
    partials = jnp.einsum(
        "grk,gkd->grd",
        attended,
        out_full.reshape(feature_groups, query_width, out_full.shape[1]),
        preferred_element_type=jnp.float32,
    ).astype(jnp.bfloat16)
    attn_sum = jnp.sum(partials.astype(jnp.float32), axis=0)
    middle = (tokens.astype(jnp.float32) + attn_sum).astype(jnp.bfloat16)
    segment = gather_rows(norm_rows(middle), "tensor")
    gate_value = jnp.dot(segment, gate_up_weight[0], preferred_element_type=jnp.float32)
    upward = jnp.dot(segment, gate_up_weight[1], preferred_element_type=jnp.float32)
    hidden = (jax.nn.silu(gate_value) * upward).astype(jnp.bfloat16)
    ffn_sum = sum_scatter_rows(
        jnp.dot(hidden, down_weight, preferred_element_type=jnp.float32).astype(jnp.bfloat16),
        "tensor",
    )
    return (middle.astype(jnp.float32) + ffn_sum).astype(jnp.bfloat16)


def solution(mesh):
    return jax.shard_map(
        on_device,
        mesh=mesh,
        in_specs=(
            P(("dp", "tensor"), None),
            P("dp", None),
            P(),
            P(("dp", "tensor"), None),
            P(None, "tensor"),
            P(),
            P(),
            P("tensor", None),
            P(None, None, "tensor"),
            P("tensor", None),
        ),
        out_specs=P(("dp", "tensor"), None),
        check_vma=False,
    )
```

```python
import math

import jax
import jax.numpy as jnp
from jax import lax
from jax.sharding import PartitionSpec as P

QH = 16
KVH = 4
HD = 64
PLEN = 4096


NEG_FILL = -1e30


def token_layout(lengths, total_rows):
    ends_at = jnp.cumsum(lengths)
    starts_at = ends_at - lengths
    indices = jnp.arange(total_rows, dtype=jnp.int32)
    request = jnp.sum((indices[:, None] >= ends_at[None, :]).astype(jnp.int32), axis=1)
    begins = jnp.max(
        jnp.where(starts_at[None, :] <= indices[:, None], starts_at[None, :], 0), axis=1
    )
    return ((PLEN + indices - begins).astype(jnp.float32), request)


def rope_tables(positions):
    halves = HD // 2
    steps_float = jnp.arange(halves, dtype=jnp.float32)
    inverse = jnp.exp(steps_float * (-2.0 * math.log(10000.0) / HD))
    angles = positions[:, None] * inverse[None, :]
    return (jnp.cos(angles), jnp.sin(angles))


def rotate(values, cos_table, sin_table):
    halves = values.shape[-1] // 2
    former = values[..., :halves]
    latter = values[..., halves:]
    cos_rows = cos_table[:, None, :]
    sin_rows = sin_table[:, None, :]
    return jnp.concatenate(
        [former * cos_rows - latter * sin_rows, latter * cos_rows + former * sin_rows], axis=-1
    )


def norm_rows(inputs):
    floats = inputs.astype(jnp.float32)
    return (floats * lax.rsqrt(jnp.mean(floats * floats, axis=-1, keepdims=True) + 1e-05)).astype(
        jnp.bfloat16
    )


def softmax_block(queries, keys_block, values_block, scaling, allowed):
    scores = (
        jnp.einsum("thd,nhd->thn", queries, keys_block, preferred_element_type=jnp.float32)
        * scaling
    )
    if allowed is not None:
        scores = jnp.where(allowed, scores, NEG_FILL)
    top_score = jnp.max(scores, axis=2)
    exponent = jnp.exp(scores - top_score[:, :, None])
    weight = jnp.sum(exponent, axis=2)
    blended = jnp.einsum(
        "thn,nhd->thd",
        exponent.astype(jnp.bfloat16),
        values_block,
        preferred_element_type=jnp.float32,
    )
    return (top_score, weight, blended)


def merge_states(former, latter):
    top_one, weight_one, blend_one = former
    top_two, weight_two, blend_two = latter
    overall = jnp.maximum(top_one, top_two)
    factor_one = jnp.exp(top_one - overall)
    factor_two = jnp.exp(top_two - overall)
    return (
        overall,
        weight_one * factor_one + weight_two * factor_two,
        blend_one * factor_one[:, :, None] + blend_two * factor_two[:, :, None],
    )


def gather_rows(values, axis):
    count = lax.axis_size(axis)
    copies = jnp.broadcast_to(values[None], (count,) + values.shape)
    received = lax.all_to_all(copies, axis, 0, 0, tiled=True)
    return received.reshape((count * values.shape[0],) + values.shape[1:])


def sum_scatter_rows(values, axis):
    count = lax.axis_size(axis)
    parts = values.reshape((count, values.shape[0] // count) + values.shape[1:])
    received = lax.all_to_all(parts, axis, 0, 0, tiled=True)
    return jnp.sum(received.astype(jnp.float32), axis=0)


CORES = 2


def fetch_slot(prefix_cache, group_prefix, group_rank):
    group_count = lax.axis_size("dp")
    chips = group_count // CORES
    chip = group_rank // CORES
    core = group_rank % CORES
    onward = [(i, (i + CORES) % group_count) for i in range(group_count)]
    backward = [(i, (i - CORES) % group_count) for i in range(group_count)]
    held = [None] * chips
    held[0] = prefix_cache
    ahead = prefix_cache
    behind = prefix_cache
    for step in range(1, chips // 2 + 1):
        ahead = lax.ppermute(ahead, "dp", onward)
        held[(chips - step) % chips] = ahead
        if step < chips - step:
            behind = lax.ppermute(behind, "dp", backward)
            held[step] = behind
    held = jnp.stack(held)
    slot_wanted = group_prefix[group_rank]
    partner_slot = group_prefix[group_rank ^ 1]
    mine = lax.dynamic_index_in_dim(held, (slot_wanted // CORES - chip) % chips, 0, keepdims=False)
    theirs = lax.dynamic_index_in_dim(held, (partner_slot // CORES - chip) % chips, 0, keepdims=False)
    swapped = lax.ppermute(theirs, "dp", [(i, i ^ 1) for i in range(group_count)])
    return jnp.where(slot_wanted % CORES == core, mine, swapped)


def on_device(
    tokens,
    lengths,
    group_prefix,
    prefix_cache,
    query_weight,
    key_weight,
    value_weight,
    out_weight,
    gate_up_weight,
    down_weight,
):
    tensor_count = lax.axis_size("tensor")
    tensor_rank = lax.axis_index("tensor")
    group_rank = lax.axis_index("dp")
    row_count = tokens.shape[0]
    group_tokens = row_count * tensor_count
    local_heads = query_weight.shape[1] // HD
    head_ratio = QH // KVH
    local_kv = max(1, local_heads // head_ratio)
    repeat_by = local_heads // local_kv
    kv_first = tensor_rank * local_heads // head_ratio
    kv_total = KVH * HD
    query_width = local_heads * HD
    kv_width = local_kv * HD
    scaling = 1.0 / math.sqrt(HD)
    positions, request = token_layout(lengths[0], group_tokens)
    cos_table, sin_table = rope_tables(positions)
    key_cols = lax.dynamic_slice_in_dim(key_weight, kv_first * HD, kv_width, 1)
    value_cols = lax.dynamic_slice_in_dim(value_weight, kv_first * HD, kv_width, 1)
    projection = jnp.concatenate([query_weight, key_cols, value_cols], axis=1)

    quarters = tensor_count // (KVH // local_kv)
    own_quarter = tensor_rank % quarters
    own_head = tensor_rank // quarters
    shard_rows = prefix_cache.shape[0]
    by_head = prefix_cache.reshape(shard_rows, 2, KVH // local_kv, kv_width)
    spread = []
    for shift in range(quarters):
        head_sent = (own_quarter + shift) % quarters
        block = lax.dynamic_index_in_dim(by_head, head_sent, 2, keepdims=False)
        pairs = [
            (quarters * a + b, quarters * ((b + shift) % quarters) + a)
            for a in range(tensor_count // quarters)
            for b in range(quarters)
        ]
        spread.append(lax.ppermute(block.reshape(shard_rows, 2 * kv_width), "tensor", pairs))
    spread = jnp.stack(spread)
    order = (own_head - jnp.arange(quarters)) % quarters
    spread = jnp.take(spread, order, axis=0).reshape(quarters * shard_rows, 2 * kv_width)
    mine = fetch_slot(spread, group_prefix, group_rank)
    held = [mine]
    for shift in range(1, quarters):
        pairs = [
            (quarters * h + q, quarters * h + (q + shift) % quarters)
            for h in range(tensor_count // quarters)
            for q in range(quarters)
        ]
        held.append(lax.ppermute(mine, "tensor", pairs))
    held = jnp.stack(held)
    order = (own_quarter - jnp.arange(quarters)) % quarters
    incoming = jnp.take(held, order, axis=0)
    seg_rows = tensor_count * shard_rows
    incoming = incoming.reshape(seg_rows, 2 * kv_width)
    out_full = lax.all_gather(out_weight, "tensor", axis=0, tiled=True)
    keys_block = jnp.repeat(incoming[:, :kv_width].reshape(seg_rows, local_kv, HD), repeat_by, axis=1)
    values_block = jnp.repeat(incoming[:, kv_width:].reshape(seg_rows, local_kv, HD), repeat_by, axis=1)

    normed = norm_rows(tokens)
    segment = gather_rows(normed, "tensor")
    seg_rows = segment.shape[0]
    mapped = jnp.dot(segment, projection, preferred_element_type=jnp.float32)
    query_part = rotate(
        mapped[:, :query_width].reshape(seg_rows, local_heads, HD), cos_table, sin_table
    )
    key_part = rotate(
        mapped[:, query_width : query_width + kv_width].reshape(seg_rows, local_kv, HD),
        cos_table,
        sin_table,
    )
    projected = jnp.concatenate(
        [
            query_part.reshape(seg_rows, query_width),
            key_part.reshape(seg_rows, kv_width),
            mapped[:, query_width + kv_width :],
        ],
        axis=1,
    ).astype(jnp.bfloat16)
    queries = projected[:, :query_width].reshape(group_tokens, local_heads, HD)
    own_keys = jnp.repeat(
        projected[:, query_width : query_width + kv_width].reshape(group_tokens, local_kv, HD),
        repeat_by,
        axis=1,
    )
    own_values = jnp.repeat(
        projected[:, query_width + kv_width :].reshape(group_tokens, local_kv, HD),
        repeat_by,
        axis=1,
    )
    start_state = (
        jnp.full((group_tokens, local_heads), NEG_FILL, jnp.float32),
        jnp.zeros((group_tokens, local_heads), jnp.float32),
        jnp.zeros((group_tokens, local_heads, HD), jnp.float32),
    )
    prefix_state = merge_states(
        start_state, softmax_block(queries, keys_block, values_block, scaling, None)
    )
    indices = jnp.arange(group_tokens, dtype=jnp.int32)
    allowed = (request[:, None] == request[None, :]) & (indices[None, :] <= indices[:, None])
    suffix_state = softmax_block(queries, own_keys, own_values, scaling, allowed[:, None, :])
    top_score, weight, blended = merge_states(prefix_state, suffix_state)
    attended = (blended / weight[:, :, None]).astype(jnp.bfloat16)
    attended = lax.all_to_all(
        attended.reshape(tensor_count, row_count, query_width), "tensor", 0, 0, tiled=True
    )
    feature_groups = out_full.shape[0] // query_width
    partials = jnp.einsum(
        "grk,gkd->grd",
        attended,
        out_full.reshape(feature_groups, query_width, out_full.shape[1]),
        preferred_element_type=jnp.float32,
    ).astype(jnp.bfloat16)
    attn_sum = jnp.sum(partials.astype(jnp.float32), axis=0)
    middle = (tokens.astype(jnp.float32) + attn_sum).astype(jnp.bfloat16)
    segment = gather_rows(norm_rows(middle), "tensor")
    gate_value = jnp.dot(segment, gate_up_weight[0], preferred_element_type=jnp.float32)
    upward = jnp.dot(segment, gate_up_weight[1], preferred_element_type=jnp.float32)
    hidden = (jax.nn.silu(gate_value) * upward).astype(jnp.bfloat16)
    ffn_sum = sum_scatter_rows(
        jnp.dot(hidden, down_weight, preferred_element_type=jnp.float32).astype(jnp.bfloat16),
        "tensor",
    )
    return (middle.astype(jnp.float32) + ffn_sum).astype(jnp.bfloat16)


def solution(mesh):
    return jax.shard_map(
        on_device,
        mesh=mesh,
        in_specs=(
            P(("dp", "tensor"), None),
            P("dp", None),
            P(),
            P(("dp", "tensor"), None),
            P(None, "tensor"),
            P(),
            P(),
            P("tensor", None),
            P(None, None, "tensor"),
            P("tensor", None),
        ),
        out_specs=P(("dp", "tensor"), None),
        check_vma=False,
    )
```

```python
import math

import jax
import jax.numpy as jnp
from jax import lax
from jax.sharding import PartitionSpec as P

QH = 16
KVH = 4
HD = 64
PLEN = 4096


NEG_FILL = -1e30


def token_layout(lengths, total_rows):
    ends_at = jnp.cumsum(lengths)
    starts_at = ends_at - lengths
    indices = jnp.arange(total_rows, dtype=jnp.int32)
    request = jnp.sum((indices[:, None] >= ends_at[None, :]).astype(jnp.int32), axis=1)
    begins = jnp.max(
        jnp.where(starts_at[None, :] <= indices[:, None], starts_at[None, :], 0), axis=1
    )
    return ((PLEN + indices - begins).astype(jnp.float32), request)


def rope_tables(positions):
    halves = HD // 2
    steps_float = jnp.arange(halves, dtype=jnp.float32)
    inverse = jnp.exp(steps_float * (-2.0 * math.log(10000.0) / HD))
    angles = positions[:, None] * inverse[None, :]
    return (jnp.cos(angles), jnp.sin(angles))


def rotate(values, cos_table, sin_table):
    halves = values.shape[-1] // 2
    former = values[..., :halves]
    latter = values[..., halves:]
    cos_rows = cos_table[:, None, :]
    sin_rows = sin_table[:, None, :]
    return jnp.concatenate(
        [former * cos_rows - latter * sin_rows, latter * cos_rows + former * sin_rows], axis=-1
    )


def norm_rows(inputs):
    floats = inputs.astype(jnp.float32)
    return (floats * lax.rsqrt(jnp.mean(floats * floats, axis=-1, keepdims=True) + 1e-05)).astype(
        jnp.bfloat16
    )


def softmax_block(queries, keys_block, values_block, scaling, allowed):
    scores = (
        jnp.einsum("thd,nhd->thn", queries, keys_block, preferred_element_type=jnp.float32)
        * scaling
    )
    if allowed is not None:
        scores = jnp.where(allowed, scores, NEG_FILL)
    top_score = jnp.max(scores, axis=2)
    exponent = jnp.exp(scores - top_score[:, :, None])
    weight = jnp.sum(exponent, axis=2)
    blended = jnp.einsum(
        "thn,nhd->thd",
        exponent.astype(jnp.bfloat16),
        values_block,
        preferred_element_type=jnp.float32,
    )
    return (top_score, weight, blended)


def merge_states(former, latter):
    top_one, weight_one, blend_one = former
    top_two, weight_two, blend_two = latter
    overall = jnp.maximum(top_one, top_two)
    factor_one = jnp.exp(top_one - overall)
    factor_two = jnp.exp(top_two - overall)
    return (
        overall,
        weight_one * factor_one + weight_two * factor_two,
        blend_one * factor_one[:, :, None] + blend_two * factor_two[:, :, None],
    )


def gather_rows(values, axis):
    count = lax.axis_size(axis)
    copies = jnp.broadcast_to(values[None], (count,) + values.shape)
    received = lax.all_to_all(copies, axis, 0, 0, tiled=True)
    return received.reshape((count * values.shape[0],) + values.shape[1:])


def sum_scatter_rows(values, axis):
    count = lax.axis_size(axis)
    parts = values.reshape((count, values.shape[0] // count) + values.shape[1:])
    received = lax.all_to_all(parts, axis, 0, 0, tiled=True)
    return jnp.sum(received.astype(jnp.float32), axis=0)


CORES = 2


def merge_states_heads(former, latter):
    top_one, weight_one, blend_one = former
    top_two, weight_two, blend_two = latter
    overall = jnp.maximum(top_one, top_two)
    factor_one = jnp.exp(top_one - overall)
    factor_two = jnp.exp(top_two - overall)
    return (
        overall,
        weight_one * factor_one + weight_two * factor_two,
        blend_one * factor_one[:, :, None] + blend_two * factor_two[:, :, None],
    )


def fetch_slot(prefix_cache, group_prefix, group_rank):
    group_count = lax.axis_size("dp")
    chips = group_count // CORES
    chip = group_rank // CORES
    core = group_rank % CORES
    onward = [(i, (i + CORES) % group_count) for i in range(group_count)]
    backward = [(i, (i - CORES) % group_count) for i in range(group_count)]
    held = [None] * chips
    held[0] = prefix_cache
    ahead = prefix_cache
    behind = prefix_cache
    for step in range(1, chips // 2 + 1):
        ahead = lax.ppermute(ahead, "dp", onward)
        held[(chips - step) % chips] = ahead
        if step < chips - step:
            behind = lax.ppermute(behind, "dp", backward)
            held[step] = behind
    held = jnp.stack(held)
    slot_wanted = group_prefix[group_rank]
    partner_slot = group_prefix[group_rank ^ 1]
    mine = lax.dynamic_index_in_dim(held, (slot_wanted // CORES - chip) % chips, 0, keepdims=False)
    theirs = lax.dynamic_index_in_dim(held, (partner_slot // CORES - chip) % chips, 0, keepdims=False)
    swapped = lax.ppermute(theirs, "dp", [(i, i ^ 1) for i in range(group_count)])
    return jnp.where(slot_wanted % CORES == core, mine, swapped)


def on_device(
    tokens,
    lengths,
    group_prefix,
    prefix_cache,
    query_weight,
    key_weight,
    value_weight,
    out_weight,
    gate_up_weight,
    down_weight,
):
    tensor_count = lax.axis_size("tensor")
    tensor_rank = lax.axis_index("tensor")
    group_rank = lax.axis_index("dp")
    row_count = tokens.shape[0]
    group_tokens = row_count * tensor_count
    local_heads = query_weight.shape[1] // HD
    head_ratio = QH // KVH
    local_kv = max(1, local_heads // head_ratio)
    repeat_by = local_heads // local_kv
    kv_first = tensor_rank * local_heads // head_ratio
    kv_total = KVH * HD
    query_width = local_heads * HD
    kv_width = local_kv * HD
    scaling = 1.0 / math.sqrt(HD)
    positions, request = token_layout(lengths[0], group_tokens)
    cos_table, sin_table = rope_tables(positions)
    key_cols = lax.dynamic_slice_in_dim(key_weight, kv_first * HD, kv_width, 1)
    value_cols = lax.dynamic_slice_in_dim(value_weight, kv_first * HD, kv_width, 1)
    projection = jnp.concatenate([query_weight, key_cols, value_cols], axis=1)

    shard_rows = prefix_cache.shape[0]
    chosen = fetch_slot(prefix_cache, group_prefix, group_rank)
    out_full = lax.all_gather(out_weight, "tensor", axis=0, tiled=True)
    chunk_rows = chosen.shape[0]
    chunk_keys = jnp.transpose(chosen[:, :kv_total].reshape(chunk_rows, KVH, HD), (1, 0, 2))
    chunk_values = jnp.transpose(chosen[:, kv_total:].reshape(chunk_rows, KVH, HD), (1, 0, 2))

    normed = norm_rows(tokens)
    segment = gather_rows(normed, "tensor")
    seg_rows = segment.shape[0]
    mapped = jnp.dot(segment, projection, preferred_element_type=jnp.float32)
    query_part = rotate(
        mapped[:, :query_width].reshape(seg_rows, local_heads, HD), cos_table, sin_table
    )
    key_part = rotate(
        mapped[:, query_width : query_width + kv_width].reshape(seg_rows, local_kv, HD),
        cos_table,
        sin_table,
    )
    projected = jnp.concatenate(
        [
            query_part.reshape(seg_rows, query_width),
            key_part.reshape(seg_rows, kv_width),
            mapped[:, query_width + kv_width :],
        ],
        axis=1,
    ).astype(jnp.bfloat16)
    queries = projected[:, :query_width].reshape(group_tokens, local_heads, HD)
    own_keys = jnp.repeat(
        projected[:, query_width : query_width + kv_width].reshape(group_tokens, local_kv, HD),
        repeat_by,
        axis=1,
    )
    own_values = jnp.repeat(
        projected[:, query_width + kv_width :].reshape(group_tokens, local_kv, HD),
        repeat_by,
        axis=1,
    )
    every_query = lax.all_to_all(
        jnp.broadcast_to(
            jnp.transpose(queries, (1, 0, 2))[None], (tensor_count, local_heads, group_tokens, HD)
        ),
        "tensor",
        0,
        0,
        tiled=True,
    ).reshape(KVH, head_ratio * group_tokens, HD)
    scores = (
        jnp.einsum("gqd,gkd->gqk", every_query, chunk_keys, preferred_element_type=jnp.float32)
        * scaling
    )
    chunk_top = jnp.max(scores, axis=2)
    exponent = jnp.exp(scores - chunk_top[:, :, None])
    chunk_weight = jnp.sum(exponent, axis=2)
    chunk_blend = jnp.einsum(
        "gqk,gkd->gqd", exponent.astype(jnp.bfloat16), chunk_values, preferred_element_type=jnp.float32
    )
    chunk_state = (
        chunk_top.reshape(QH, group_tokens),
        chunk_weight.reshape(QH, group_tokens),
        chunk_blend.reshape(QH, group_tokens, HD),
    )

    indices = jnp.arange(group_tokens, dtype=jnp.int32)
    allowed = (request[:, None] == request[None, :]) & (indices[None, :] <= indices[:, None])
    suffix_top, suffix_weight, suffix_blend = softmax_block(
        queries, own_keys, own_values, scaling, allowed[:, None, :]
    )
    head_first = tensor_rank * local_heads
    suffix_state = (
        lax.dynamic_update_slice_in_dim(
            jnp.full((QH, group_tokens), NEG_FILL, jnp.float32), suffix_top.T, head_first, 0
        ),
        lax.dynamic_update_slice_in_dim(
            jnp.zeros((QH, group_tokens), jnp.float32), suffix_weight.T, head_first, 0
        ),
        lax.dynamic_update_slice_in_dim(
            jnp.zeros((QH, group_tokens, HD), jnp.float32),
            jnp.transpose(suffix_blend, (1, 0, 2)),
            head_first,
            0,
        ),
    )
    top_score, weight, blended = merge_states_heads(chunk_state, suffix_state)
    partial = (blended / weight[:, :, None]).astype(jnp.bfloat16)
    partial = partial.reshape(QH, tensor_count, row_count, HD).transpose(1, 2, 0, 3)
    partial = lax.all_to_all(
        partial.reshape(tensor_count, row_count, QH * HD), "tensor", 0, 0, tiled=True
    )
    stats = jnp.stack([top_score, weight], axis=2).reshape(QH, tensor_count, row_count, 2)
    stats = lax.all_to_all(
        stats.transpose(1, 2, 0, 3).reshape(tensor_count, row_count, QH * 2), "tensor", 0, 0, tiled=True
    ).reshape(tensor_count, row_count, QH, 2)
    part_top = stats[..., 0]
    overall = jnp.max(part_top, axis=0)
    factor = stats[..., 1] * jnp.exp(part_top - overall[None])
    weight = jnp.sum(factor, axis=0)
    blended = jnp.sum(
        partial.reshape(tensor_count, row_count, QH, HD).astype(jnp.float32) * factor[..., None], axis=0
    )
    attended = (blended / weight[:, :, None]).astype(jnp.bfloat16)
    attended = attended.reshape(row_count, tensor_count, query_width).transpose(1, 0, 2)
    feature_groups = out_full.shape[0] // query_width
    partials = jnp.einsum(
        "grk,gkd->grd",
        attended,
        out_full.reshape(feature_groups, query_width, out_full.shape[1]),
        preferred_element_type=jnp.float32,
    ).astype(jnp.bfloat16)
    attn_sum = jnp.sum(partials.astype(jnp.float32), axis=0)
    middle = (tokens.astype(jnp.float32) + attn_sum).astype(jnp.bfloat16)
    segment = gather_rows(norm_rows(middle), "tensor")
    gate_value = jnp.dot(segment, gate_up_weight[0], preferred_element_type=jnp.float32)
    upward = jnp.dot(segment, gate_up_weight[1], preferred_element_type=jnp.float32)
    hidden = (jax.nn.silu(gate_value) * upward).astype(jnp.bfloat16)
    ffn_sum = sum_scatter_rows(
        jnp.dot(hidden, down_weight, preferred_element_type=jnp.float32).astype(jnp.bfloat16),
        "tensor",
    )
    return (middle.astype(jnp.float32) + ffn_sum).astype(jnp.bfloat16)


def solution(mesh):
    return jax.shard_map(
        on_device,
        mesh=mesh,
        in_specs=(
            P(("dp", "tensor"), None),
            P("dp", None),
            P(),
            P(("dp", "tensor"), None),
            P(None, "tensor"),
            P(),
            P(),
            P("tensor", None),
            P(None, None, "tensor"),
            P("tensor", None),
        ),
        out_specs=P(("dp", "tensor"), None),
        check_vma=False,
    )
```

```python
import math

import jax
import jax.numpy as jnp
from jax import lax
from jax.sharding import PartitionSpec as P

QH = 16
KVH = 4
HD = 64
PLEN = 4096


NEG_FILL = -1e30


def token_layout(lengths, total_rows):
    ends_at = jnp.cumsum(lengths)
    starts_at = ends_at - lengths
    indices = jnp.arange(total_rows, dtype=jnp.int32)
    request = jnp.sum((indices[:, None] >= ends_at[None, :]).astype(jnp.int32), axis=1)
    begins = jnp.max(
        jnp.where(starts_at[None, :] <= indices[:, None], starts_at[None, :], 0), axis=1
    )
    return ((PLEN + indices - begins).astype(jnp.float32), request)


def rope_tables(positions):
    halves = HD // 2
    steps_float = jnp.arange(halves, dtype=jnp.float32)
    inverse = jnp.exp(steps_float * (-2.0 * math.log(10000.0) / HD))
    angles = positions[:, None] * inverse[None, :]
    return (jnp.cos(angles), jnp.sin(angles))


def rotate(values, cos_table, sin_table):
    halves = values.shape[-1] // 2
    former = values[..., :halves]
    latter = values[..., halves:]
    cos_rows = cos_table[:, None, :]
    sin_rows = sin_table[:, None, :]
    return jnp.concatenate(
        [former * cos_rows - latter * sin_rows, latter * cos_rows + former * sin_rows], axis=-1
    )


def norm_rows(inputs):
    floats = inputs.astype(jnp.float32)
    return (floats * lax.rsqrt(jnp.mean(floats * floats, axis=-1, keepdims=True) + 1e-05)).astype(
        jnp.bfloat16
    )


def softmax_block(queries, keys_block, values_block, scaling, allowed):
    scores = (
        jnp.einsum("thd,nhd->thn", queries, keys_block, preferred_element_type=jnp.float32)
        * scaling
    )
    if allowed is not None:
        scores = jnp.where(allowed, scores, NEG_FILL)
    top_score = jnp.max(scores, axis=2)
    exponent = jnp.exp(scores - top_score[:, :, None])
    weight = jnp.sum(exponent, axis=2)
    blended = jnp.einsum(
        "thn,nhd->thd",
        exponent.astype(jnp.bfloat16),
        values_block,
        preferred_element_type=jnp.float32,
    )
    return (top_score, weight, blended)


def merge_states(former, latter):
    top_one, weight_one, blend_one = former
    top_two, weight_two, blend_two = latter
    overall = jnp.maximum(top_one, top_two)
    factor_one = jnp.exp(top_one - overall)
    factor_two = jnp.exp(top_two - overall)
    return (
        overall,
        weight_one * factor_one + weight_two * factor_two,
        blend_one * factor_one[:, :, None] + blend_two * factor_two[:, :, None],
    )


def gather_rows(values, axis):
    count = lax.axis_size(axis)
    copies = jnp.broadcast_to(values[None], (count,) + values.shape)
    received = lax.all_to_all(copies, axis, 0, 0, tiled=True)
    return received.reshape((count * values.shape[0],) + values.shape[1:])


def sum_scatter_rows(values, axis):
    count = lax.axis_size(axis)
    parts = values.reshape((count, values.shape[0] // count) + values.shape[1:])
    received = lax.all_to_all(parts, axis, 0, 0, tiled=True)
    return jnp.sum(received.astype(jnp.float32), axis=0)


CORES = 2


def fetch_slot(prefix_cache, group_prefix, group_rank):
    group_count = lax.axis_size("dp")
    chips = group_count // CORES
    chip = group_rank // CORES
    core = group_rank % CORES
    onward = [(i, (i + CORES) % group_count) for i in range(group_count)]
    backward = [(i, (i - CORES) % group_count) for i in range(group_count)]
    held = [None] * chips
    held[0] = prefix_cache
    ahead = prefix_cache
    behind = prefix_cache
    for step in range(1, chips // 2 + 1):
        ahead = lax.ppermute(ahead, "dp", onward)
        held[(chips - step) % chips] = ahead
        if step < chips - step:
            behind = lax.ppermute(behind, "dp", backward)
            held[step] = behind
    held = jnp.stack(held)
    slot_wanted = group_prefix[group_rank]
    partner_slot = group_prefix[group_rank ^ 1]
    mine = lax.dynamic_index_in_dim(held, (slot_wanted // CORES - chip) % chips, 0, keepdims=False)
    theirs = lax.dynamic_index_in_dim(held, (partner_slot // CORES - chip) % chips, 0, keepdims=False)
    swapped = lax.ppermute(theirs, "dp", [(i, i ^ 1) for i in range(group_count)])
    return jnp.where(slot_wanted % CORES == core, mine, swapped)


def on_device(
    tokens,
    lengths,
    group_prefix,
    prefix_cache,
    query_weight,
    key_weight,
    value_weight,
    out_weight,
    gate_up_weight,
    down_weight,
):
    tensor_count = lax.axis_size("tensor")
    tensor_rank = lax.axis_index("tensor")
    group_rank = lax.axis_index("dp")
    row_count = tokens.shape[0]
    group_tokens = row_count * tensor_count
    local_heads = query_weight.shape[1] // HD
    head_ratio = QH // KVH
    local_kv = max(1, local_heads // head_ratio)
    repeat_by = local_heads // local_kv
    kv_first = tensor_rank * local_heads // head_ratio
    kv_total = KVH * HD
    query_width = local_heads * HD
    kv_width = local_kv * HD
    scaling = 1.0 / math.sqrt(HD)
    positions, request = token_layout(lengths[0], group_tokens)
    cos_table, sin_table = rope_tables(positions)
    key_cols = lax.dynamic_slice_in_dim(key_weight, kv_first * HD, kv_width, 1)
    value_cols = lax.dynamic_slice_in_dim(value_weight, kv_first * HD, kv_width, 1)
    projection = jnp.concatenate([query_weight, key_cols, value_cols], axis=1)

    shard_rows = prefix_cache.shape[0]
    chosen = fetch_slot(prefix_cache, group_prefix, group_rank)
    out_full = lax.all_gather(out_weight, "tensor", axis=0, tiled=True)
    by_head = chosen.reshape(shard_rows, 2, KVH // local_kv, kv_width)
    by_head = jnp.transpose(by_head, (2, 0, 1, 3)).reshape(KVH // local_kv, shard_rows, 2 * kv_width)
    wanted_by = (jnp.arange(tensor_count) * local_heads // head_ratio) // local_kv
    outgoing = jnp.take(by_head, wanted_by, axis=0)
    incoming = lax.all_to_all(outgoing, "tensor", 0, 0, tiled=True)
    seg_rows = tensor_count * shard_rows
    incoming = incoming.reshape(seg_rows, 2 * kv_width)
    keys_block = jnp.repeat(incoming[:, :kv_width].reshape(seg_rows, local_kv, HD), repeat_by, axis=1)
    values_block = jnp.repeat(incoming[:, kv_width:].reshape(seg_rows, local_kv, HD), repeat_by, axis=1)

    group_rows = gather_rows(tokens, "tensor")
    segment = norm_rows(group_rows)
    seg_rows = segment.shape[0]
    mapped = jnp.dot(segment, projection, preferred_element_type=jnp.float32)
    query_part = rotate(
        mapped[:, :query_width].reshape(seg_rows, local_heads, HD), cos_table, sin_table
    )
    key_part = rotate(
        mapped[:, query_width : query_width + kv_width].reshape(seg_rows, local_kv, HD),
        cos_table,
        sin_table,
    )
    projected = jnp.concatenate(
        [
            query_part.reshape(seg_rows, query_width),
            key_part.reshape(seg_rows, kv_width),
            mapped[:, query_width + kv_width :],
        ],
        axis=1,
    ).astype(jnp.bfloat16)
    queries = projected[:, :query_width].reshape(group_tokens, local_heads, HD)
    own_keys = jnp.repeat(
        projected[:, query_width : query_width + kv_width].reshape(group_tokens, local_kv, HD),
        repeat_by,
        axis=1,
    )
    own_values = jnp.repeat(
        projected[:, query_width + kv_width :].reshape(group_tokens, local_kv, HD),
        repeat_by,
        axis=1,
    )
    start_state = (
        jnp.full((group_tokens, local_heads), NEG_FILL, jnp.float32),
        jnp.zeros((group_tokens, local_heads), jnp.float32),
        jnp.zeros((group_tokens, local_heads, HD), jnp.float32),
    )
    prefix_state = merge_states(
        start_state, softmax_block(queries, keys_block, values_block, scaling, None)
    )
    indices = jnp.arange(group_tokens, dtype=jnp.int32)
    allowed = (request[:, None] == request[None, :]) & (indices[None, :] <= indices[:, None])
    suffix_state = softmax_block(queries, own_keys, own_values, scaling, allowed[:, None, :])
    top_score, weight, blended = merge_states(prefix_state, suffix_state)
    attended = (blended / weight[:, :, None]).astype(jnp.bfloat16).reshape(group_tokens, query_width)
    every_head = gather_rows(jnp.transpose(attended)[None], "tensor")
    every_head = jnp.transpose(every_head.reshape(tensor_count * query_width, group_tokens))
    attn_sum = jnp.dot(every_head, out_full, preferred_element_type=jnp.float32)
    middle = (group_rows.astype(jnp.float32) + attn_sum).astype(jnp.bfloat16)
    segment = norm_rows(middle)
    gate_value = jnp.dot(segment, gate_up_weight[0], preferred_element_type=jnp.float32)
    upward = jnp.dot(segment, gate_up_weight[1], preferred_element_type=jnp.float32)
    hidden = (jax.nn.silu(gate_value) * upward).astype(jnp.bfloat16)
    ffn_sum = sum_scatter_rows(
        jnp.dot(hidden, down_weight, preferred_element_type=jnp.float32).astype(jnp.bfloat16),
        "tensor",
    )
    own_middle = lax.dynamic_slice_in_dim(middle, tensor_rank * row_count, row_count, 0)
    return (own_middle.astype(jnp.float32) + ffn_sum).astype(jnp.bfloat16)


def solution(mesh):
    return jax.shard_map(
        on_device,
        mesh=mesh,
        in_specs=(
            P(("dp", "tensor"), None),
            P("dp", None),
            P(),
            P(("dp", "tensor"), None),
            P(None, "tensor"),
            P(),
            P(),
            P("tensor", None),
            P(None, None, "tensor"),
            P("tensor", None),
        ),
        out_specs=P(("dp", "tensor"), None),
        check_vma=False,
    )
```

```python
import math

import jax
import jax.numpy as jnp
from jax import lax
from jax.sharding import PartitionSpec as P

QH = 16
KVH = 4
HD = 64
PLEN = 4096


NEG_FILL = -1e30


def token_layout(lengths, total_rows):
    ends_at = jnp.cumsum(lengths)
    starts_at = ends_at - lengths
    indices = jnp.arange(total_rows, dtype=jnp.int32)
    request = jnp.sum((indices[:, None] >= ends_at[None, :]).astype(jnp.int32), axis=1)
    begins = jnp.max(
        jnp.where(starts_at[None, :] <= indices[:, None], starts_at[None, :], 0), axis=1
    )
    return ((PLEN + indices - begins).astype(jnp.float32), request)


def rope_tables(positions):
    halves = HD // 2
    steps_float = jnp.arange(halves, dtype=jnp.float32)
    inverse = jnp.exp(steps_float * (-2.0 * math.log(10000.0) / HD))
    angles = positions[:, None] * inverse[None, :]
    return (jnp.cos(angles), jnp.sin(angles))


def rotate(values, cos_table, sin_table):
    halves = values.shape[-1] // 2
    former = values[..., :halves]
    latter = values[..., halves:]
    cos_rows = cos_table[:, None, :]
    sin_rows = sin_table[:, None, :]
    return jnp.concatenate(
        [former * cos_rows - latter * sin_rows, latter * cos_rows + former * sin_rows], axis=-1
    )


def norm_rows(inputs):
    floats = inputs.astype(jnp.float32)
    return (floats * lax.rsqrt(jnp.mean(floats * floats, axis=-1, keepdims=True) + 1e-05)).astype(
        jnp.bfloat16
    )


def softmax_block(queries, keys_block, values_block, scaling, allowed):
    scores = (
        jnp.einsum("thd,nhd->thn", queries, keys_block, preferred_element_type=jnp.float32)
        * scaling
    )
    if allowed is not None:
        scores = jnp.where(allowed, scores, NEG_FILL)
    top_score = jnp.max(scores, axis=2)
    exponent = jnp.exp(scores - top_score[:, :, None])
    weight = jnp.sum(exponent, axis=2)
    blended = jnp.einsum(
        "thn,nhd->thd",
        exponent.astype(jnp.bfloat16),
        values_block,
        preferred_element_type=jnp.float32,
    )
    return (top_score, weight, blended)


def merge_states(former, latter):
    top_one, weight_one, blend_one = former
    top_two, weight_two, blend_two = latter
    overall = jnp.maximum(top_one, top_two)
    factor_one = jnp.exp(top_one - overall)
    factor_two = jnp.exp(top_two - overall)
    return (
        overall,
        weight_one * factor_one + weight_two * factor_two,
        blend_one * factor_one[:, :, None] + blend_two * factor_two[:, :, None],
    )


def gather_rows(values, axis):
    count = lax.axis_size(axis)
    copies = jnp.broadcast_to(values[None], (count,) + values.shape)
    received = lax.all_to_all(copies, axis, 0, 0, tiled=True)
    return received.reshape((count * values.shape[0],) + values.shape[1:])


def sum_scatter_rows(values, axis):
    count = lax.axis_size(axis)
    parts = values.reshape((count, values.shape[0] // count) + values.shape[1:])
    received = lax.all_to_all(parts, axis, 0, 0, tiled=True)
    return jnp.sum(received.astype(jnp.float32), axis=0)


CORES = 2


def fetch_slot(prefix_cache, group_prefix, group_rank):
    group_count = lax.axis_size("dp")
    chips = group_count // CORES
    chip = group_rank // CORES
    core = group_rank % CORES
    slot_wanted = group_prefix[group_rank]
    partner_slot = group_prefix[group_rank ^ 1]
    mine_at = (slot_wanted // CORES - chip) % chips
    theirs_at = (partner_slot // CORES - chip) % chips
    onward = [(i, (i + CORES) % group_count) for i in range(group_count)]
    backward = [(i, (i - CORES) % group_count) for i in range(group_count)]
    mine = prefix_cache
    theirs = prefix_cache
    ahead = prefix_cache
    behind = prefix_cache
    for step in range(1, chips // 2 + 1):
        ahead = lax.ppermute(ahead, "dp", onward)
        mine = jnp.where(mine_at == (chips - step) % chips, ahead, mine)
        theirs = jnp.where(theirs_at == (chips - step) % chips, ahead, theirs)
        if step < chips - step:
            behind = lax.ppermute(behind, "dp", backward)
            mine = jnp.where(mine_at == step, behind, mine)
            theirs = jnp.where(theirs_at == step, behind, theirs)
    swapped = lax.ppermute(theirs, "dp", [(i, i ^ 1) for i in range(group_count)])
    return jnp.where(slot_wanted % CORES == core, mine, swapped)


def on_device(
    tokens,
    lengths,
    group_prefix,
    prefix_cache,
    query_weight,
    key_weight,
    value_weight,
    out_weight,
    gate_up_weight,
    down_weight,
):
    tensor_count = lax.axis_size("tensor")
    tensor_rank = lax.axis_index("tensor")
    group_rank = lax.axis_index("dp")
    row_count = tokens.shape[0]
    group_tokens = row_count * tensor_count
    local_heads = query_weight.shape[1] // HD
    head_ratio = QH // KVH
    local_kv = max(1, local_heads // head_ratio)
    repeat_by = local_heads // local_kv
    kv_first = tensor_rank * local_heads // head_ratio
    kv_total = KVH * HD
    query_width = local_heads * HD
    kv_width = local_kv * HD
    scaling = 1.0 / math.sqrt(HD)
    positions, request = token_layout(lengths[0], group_tokens)
    cos_table, sin_table = rope_tables(positions)
    key_cols = lax.dynamic_slice_in_dim(key_weight, kv_first * HD, kv_width, 1)
    value_cols = lax.dynamic_slice_in_dim(value_weight, kv_first * HD, kv_width, 1)
    projection = jnp.concatenate([query_weight, key_cols, value_cols], axis=1)

    shard_rows = prefix_cache.shape[0]
    kv_groups = KVH // local_kv
    by_head = prefix_cache.reshape(shard_rows, 2, kv_groups, kv_width)
    by_head = jnp.transpose(by_head, (2, 0, 1, 3)).reshape(kv_groups, shard_rows, 2 * kv_width)
    chosen = fetch_slot(by_head, group_prefix, group_rank)
    out_full = lax.all_gather(out_weight, "tensor", axis=0, tiled=True)
    outgoing = jnp.repeat(chosen, tensor_count // kv_groups, axis=0)
    incoming = lax.all_to_all(outgoing, "tensor", 0, 0, tiled=True)
    seg_rows = tensor_count * shard_rows
    incoming = incoming.reshape(seg_rows, 2 * kv_width)
    keys_block = jnp.repeat(incoming[:, :kv_width].reshape(seg_rows, local_kv, HD), repeat_by, axis=1)
    values_block = jnp.repeat(incoming[:, kv_width:].reshape(seg_rows, local_kv, HD), repeat_by, axis=1)

    group_rows = gather_rows(tokens, "tensor")
    segment = norm_rows(group_rows)
    seg_rows = segment.shape[0]
    mapped = jnp.dot(segment, projection, preferred_element_type=jnp.float32)
    query_part = rotate(
        mapped[:, :query_width].reshape(seg_rows, local_heads, HD), cos_table, sin_table
    )
    key_part = rotate(
        mapped[:, query_width : query_width + kv_width].reshape(seg_rows, local_kv, HD),
        cos_table,
        sin_table,
    )
    projected = jnp.concatenate(
        [
            query_part.reshape(seg_rows, query_width),
            key_part.reshape(seg_rows, kv_width),
            mapped[:, query_width + kv_width :],
        ],
        axis=1,
    ).astype(jnp.bfloat16)
    queries = projected[:, :query_width].reshape(group_tokens, local_heads, HD)
    own_keys = jnp.repeat(
        projected[:, query_width : query_width + kv_width].reshape(group_tokens, local_kv, HD),
        repeat_by,
        axis=1,
    )
    own_values = jnp.repeat(
        projected[:, query_width + kv_width :].reshape(group_tokens, local_kv, HD),
        repeat_by,
        axis=1,
    )
    start_state = (
        jnp.full((group_tokens, local_heads), NEG_FILL, jnp.float32),
        jnp.zeros((group_tokens, local_heads), jnp.float32),
        jnp.zeros((group_tokens, local_heads, HD), jnp.float32),
    )
    prefix_state = merge_states(
        start_state, softmax_block(queries, keys_block, values_block, scaling, None)
    )
    indices = jnp.arange(group_tokens, dtype=jnp.int32)
    allowed = (request[:, None] == request[None, :]) & (indices[None, :] <= indices[:, None])
    suffix_state = softmax_block(queries, own_keys, own_values, scaling, allowed[:, None, :])
    top_score, weight, blended = merge_states(prefix_state, suffix_state)
    attended = (blended / weight[:, :, None]).astype(jnp.bfloat16).reshape(group_tokens, query_width)
    every_head = gather_rows(jnp.transpose(attended)[None], "tensor")
    every_head = jnp.transpose(every_head.reshape(tensor_count * query_width, group_tokens))
    attn_sum = jnp.dot(every_head, out_full, preferred_element_type=jnp.float32)
    middle = (group_rows.astype(jnp.float32) + attn_sum).astype(jnp.bfloat16)
    segment = norm_rows(middle)
    gate_value = jnp.dot(segment, gate_up_weight[0], preferred_element_type=jnp.float32)
    upward = jnp.dot(segment, gate_up_weight[1], preferred_element_type=jnp.float32)
    hidden = (jax.nn.silu(gate_value) * upward).astype(jnp.bfloat16)
    ffn_sum = sum_scatter_rows(
        jnp.dot(hidden, down_weight, preferred_element_type=jnp.float32).astype(jnp.bfloat16),
        "tensor",
    )
    own_middle = lax.dynamic_slice_in_dim(middle, tensor_rank * row_count, row_count, 0)
    return (own_middle.astype(jnp.float32) + ffn_sum).astype(jnp.bfloat16)


def solution(mesh):
    return jax.shard_map(
        on_device,
        mesh=mesh,
        in_specs=(
            P(("dp", "tensor"), None),
            P("dp", None),
            P(),
            P(("dp", "tensor"), None),
            P(None, "tensor"),
            P(),
            P(),
            P("tensor", None),
            P(None, None, "tensor"),
            P("tensor", None),
        ),
        out_specs=P(("dp", "tensor"), None),
        check_vma=False,
    )
```

```python
import math

import jax
import jax.numpy as jnp
from jax import lax
from jax.sharding import PartitionSpec as P

QH = 16
KVH = 4
HD = 64
PLEN = 4096


NEG_FILL = -1e30


def token_layout(lengths, total_rows):
    ends_at = jnp.cumsum(lengths)
    starts_at = ends_at - lengths
    indices = jnp.arange(total_rows, dtype=jnp.int32)
    request = jnp.sum((indices[:, None] >= ends_at[None, :]).astype(jnp.int32), axis=1)
    begins = jnp.max(
        jnp.where(starts_at[None, :] <= indices[:, None], starts_at[None, :], 0), axis=1
    )
    return ((PLEN + indices - begins).astype(jnp.float32), request)


def rope_tables(positions):
    halves = HD // 2
    steps_float = jnp.arange(halves, dtype=jnp.float32)
    inverse = jnp.exp(steps_float * (-2.0 * math.log(10000.0) / HD))
    angles = positions[:, None] * inverse[None, :]
    return (jnp.cos(angles), jnp.sin(angles))


def rotate(values, cos_table, sin_table):
    halves = values.shape[-1] // 2
    former = values[..., :halves]
    latter = values[..., halves:]
    cos_rows = cos_table[:, None, :]
    sin_rows = sin_table[:, None, :]
    return jnp.concatenate(
        [former * cos_rows - latter * sin_rows, latter * cos_rows + former * sin_rows], axis=-1
    )


def norm_rows(inputs):
    floats = inputs.astype(jnp.float32)
    return (floats * lax.rsqrt(jnp.mean(floats * floats, axis=-1, keepdims=True) + 1e-05)).astype(
        jnp.bfloat16
    )


def softmax_block(queries, keys_block, values_block, scaling, allowed):
    scores = (
        jnp.einsum("thd,nhd->thn", queries, keys_block, preferred_element_type=jnp.float32)
        * scaling
    )
    if allowed is not None:
        scores = jnp.where(allowed, scores, NEG_FILL)
    top_score = jnp.max(scores, axis=2)
    exponent = jnp.exp(scores - top_score[:, :, None])
    weight = jnp.sum(exponent, axis=2)
    blended = jnp.einsum(
        "thn,nhd->thd",
        exponent.astype(jnp.bfloat16),
        values_block,
        preferred_element_type=jnp.float32,
    )
    return (top_score, weight, blended)


def merge_states(former, latter):
    top_one, weight_one, blend_one = former
    top_two, weight_two, blend_two = latter
    overall = jnp.maximum(top_one, top_two)
    factor_one = jnp.exp(top_one - overall)
    factor_two = jnp.exp(top_two - overall)
    return (
        overall,
        weight_one * factor_one + weight_two * factor_two,
        blend_one * factor_one[:, :, None] + blend_two * factor_two[:, :, None],
    )


def gather_rows(values, axis):
    count = lax.axis_size(axis)
    copies = jnp.broadcast_to(values[None], (count,) + values.shape)
    received = lax.all_to_all(copies, axis, 0, 0, tiled=True)
    return received.reshape((count * values.shape[0],) + values.shape[1:])


def sum_scatter_rows(values, axis):
    count = lax.axis_size(axis)
    parts = values.reshape((count, values.shape[0] // count) + values.shape[1:])
    received = lax.all_to_all(parts, axis, 0, 0, tiled=True)
    return jnp.sum(received.astype(jnp.float32), axis=0)


CORES = 2


def fetch_slot(prefix_cache, group_prefix, group_rank, rider):
    group_count = lax.axis_size("dp")
    chips = group_count // CORES
    chip = group_rank // CORES
    core = group_rank % CORES
    slot_wanted = group_prefix[group_rank]
    partner_slot = group_prefix[group_rank ^ 1]
    mine_at = (slot_wanted // CORES - chip) % chips
    theirs_at = (partner_slot // CORES - chip) % chips
    onward = [(i, (i + CORES) % group_count) for i in range(group_count)]
    backward = [(i, (i - CORES) % group_count) for i in range(group_count)]
    mine = prefix_cache
    theirs = prefix_cache
    ahead = prefix_cache
    behind = prefix_cache
    for step in range(1, chips // 2 + 1):
        ahead = lax.ppermute(ahead, "dp", onward)
        mine = jnp.where(mine_at == (chips - step) % chips, ahead, mine)
        theirs = jnp.where(theirs_at == (chips - step) % chips, ahead, theirs)
        if step < chips - step:
            behind = lax.ppermute(behind, "dp", backward)
            mine = jnp.where(mine_at == step, behind, mine)
            theirs = jnp.where(theirs_at == step, behind, theirs)
        if step == 1:
            ahead, behind, rider = lax.optimization_barrier((ahead, behind, rider))
        mine, theirs, ahead, behind = lax.optimization_barrier((mine, theirs, ahead, behind))
    swapped = lax.ppermute(theirs, "dp", [(i, i ^ 1) for i in range(group_count)])
    return slot_wanted % CORES == core, mine, swapped, rider


def on_device(
    tokens,
    lengths,
    group_prefix,
    prefix_cache,
    query_weight,
    key_weight,
    value_weight,
    out_weight,
    gate_up_weight,
    down_weight,
):
    tensor_count = lax.axis_size("tensor")
    tensor_rank = lax.axis_index("tensor")
    group_rank = lax.axis_index("dp")
    row_count = tokens.shape[0]
    group_tokens = row_count * tensor_count
    local_heads = query_weight.shape[1] // HD
    head_ratio = QH // KVH
    local_kv = max(1, local_heads // head_ratio)
    repeat_by = local_heads // local_kv
    kv_first = tensor_rank * local_heads // head_ratio
    kv_total = KVH * HD
    query_width = local_heads * HD
    kv_width = local_kv * HD
    scaling = 1.0 / math.sqrt(HD)
    positions, request = token_layout(lengths[0], group_tokens)
    cos_table, sin_table = rope_tables(positions)
    key_cols = lax.dynamic_slice_in_dim(key_weight, kv_first * HD, kv_width, 1)
    value_cols = lax.dynamic_slice_in_dim(value_weight, kv_first * HD, kv_width, 1)
    projection = jnp.concatenate([query_weight, key_cols, value_cols], axis=1)

    shard_rows = prefix_cache.shape[0]
    kv_groups = KVH // local_kv
    by_head = prefix_cache.reshape(shard_rows, 2, kv_groups, kv_width)
    by_head = jnp.transpose(by_head, (2, 0, 1, 3)).reshape(kv_groups, shard_rows, 2 * kv_width)
    on_core, mine, swapped, projection = fetch_slot(by_head, group_prefix, group_rank, projection)
    out_full = lax.all_gather(out_weight, "tensor", axis=0, tiled=True)
    outgoing = jnp.where(
        on_core,
        jnp.repeat(mine, tensor_count // kv_groups, axis=0),
        jnp.repeat(swapped, tensor_count // kv_groups, axis=0),
    )
    incoming = lax.all_to_all(outgoing, "tensor", 0, 0, tiled=True)
    seg_rows = tensor_count * shard_rows
    incoming = incoming.reshape(seg_rows, 2 * kv_width)
    keys_block = jnp.repeat(incoming[:, :kv_width].reshape(seg_rows, local_kv, HD), repeat_by, axis=1)
    values_block = jnp.repeat(incoming[:, kv_width:].reshape(seg_rows, local_kv, HD), repeat_by, axis=1)

    group_rows = gather_rows(tokens, "tensor")
    segment = norm_rows(group_rows)
    seg_rows = segment.shape[0]
    mapped = jnp.dot(segment, projection, preferred_element_type=jnp.float32)
    query_part = rotate(
        mapped[:, :query_width].reshape(seg_rows, local_heads, HD), cos_table, sin_table
    )
    key_part = rotate(
        mapped[:, query_width : query_width + kv_width].reshape(seg_rows, local_kv, HD),
        cos_table,
        sin_table,
    )
    projected = jnp.concatenate(
        [
            query_part.reshape(seg_rows, query_width),
            key_part.reshape(seg_rows, kv_width),
            mapped[:, query_width + kv_width :],
        ],
        axis=1,
    ).astype(jnp.bfloat16)
    queries = projected[:, :query_width].reshape(group_tokens, local_heads, HD)
    own_keys = jnp.repeat(
        projected[:, query_width : query_width + kv_width].reshape(group_tokens, local_kv, HD),
        repeat_by,
        axis=1,
    )
    own_values = jnp.repeat(
        projected[:, query_width + kv_width :].reshape(group_tokens, local_kv, HD),
        repeat_by,
        axis=1,
    )
    start_state = (
        jnp.full((group_tokens, local_heads), NEG_FILL, jnp.float32),
        jnp.zeros((group_tokens, local_heads), jnp.float32),
        jnp.zeros((group_tokens, local_heads, HD), jnp.float32),
    )
    prefix_state = merge_states(
        start_state, softmax_block(queries, keys_block, values_block, scaling, None)
    )
    indices = jnp.arange(group_tokens, dtype=jnp.int32)
    allowed = (request[:, None] == request[None, :]) & (indices[None, :] <= indices[:, None])
    suffix_state = softmax_block(queries, own_keys, own_values, scaling, allowed[:, None, :])
    top_score, weight, blended = merge_states(prefix_state, suffix_state)
    attended = (blended / weight[:, :, None]).astype(jnp.bfloat16).reshape(group_tokens, query_width)
    every_head = gather_rows(jnp.transpose(attended)[None], "tensor")
    every_head = jnp.transpose(every_head.reshape(tensor_count * query_width, group_tokens))
    attn_sum = jnp.dot(every_head, out_full, preferred_element_type=jnp.float32)
    middle = (group_rows.astype(jnp.float32) + attn_sum).astype(jnp.bfloat16)
    segment = norm_rows(middle)
    gate_value = jnp.dot(segment, gate_up_weight[0], preferred_element_type=jnp.float32)
    upward = jnp.dot(segment, gate_up_weight[1], preferred_element_type=jnp.float32)
    hidden = (jax.nn.silu(gate_value) * upward).astype(jnp.bfloat16)
    ffn_sum = sum_scatter_rows(
        jnp.dot(hidden, down_weight, preferred_element_type=jnp.float32).astype(jnp.bfloat16),
        "tensor",
    )
    own_middle = lax.dynamic_slice_in_dim(middle, tensor_rank * row_count, row_count, 0)
    return (own_middle.astype(jnp.float32) + ffn_sum).astype(jnp.bfloat16)


def solution(mesh):
    return jax.shard_map(
        on_device,
        mesh=mesh,
        in_specs=(
            P(("dp", "tensor"), None),
            P("dp", None),
            P(),
            P(("dp", "tensor"), None),
            P(None, "tensor"),
            P(),
            P(),
            P("tensor", None),
            P(None, None, "tensor"),
            P("tensor", None),
        ),
        out_specs=P(("dp", "tensor"), None),
        check_vma=False,
    )
```

```python
import math

import jax
import jax.numpy as jnp
from jax import lax
from jax.sharding import PartitionSpec as P

QH = 16
KVH = 4
HD = 64
PLEN = 4096


NEG_FILL = -1e30


def token_layout(lengths, total_rows):
    ends_at = jnp.cumsum(lengths)
    starts_at = ends_at - lengths
    indices = jnp.arange(total_rows, dtype=jnp.int32)
    request = jnp.sum((indices[:, None] >= ends_at[None, :]).astype(jnp.int32), axis=1)
    begins = jnp.max(
        jnp.where(starts_at[None, :] <= indices[:, None], starts_at[None, :], 0), axis=1
    )
    return ((PLEN + indices - begins).astype(jnp.float32), request)


def rope_tables(positions):
    halves = HD // 2
    steps_float = jnp.arange(halves, dtype=jnp.float32)
    inverse = jnp.exp(steps_float * (-2.0 * math.log(10000.0) / HD))
    angles = positions[:, None] * inverse[None, :]
    return (jnp.cos(angles), jnp.sin(angles))


def rotate(values, cos_table, sin_table):
    halves = values.shape[-1] // 2
    former = values[..., :halves]
    latter = values[..., halves:]
    cos_rows = cos_table[:, None, :]
    sin_rows = sin_table[:, None, :]
    return jnp.concatenate(
        [former * cos_rows - latter * sin_rows, latter * cos_rows + former * sin_rows], axis=-1
    )


def norm_rows(inputs):
    floats = inputs.astype(jnp.float32)
    return (floats * lax.rsqrt(jnp.mean(floats * floats, axis=-1, keepdims=True) + 1e-05)).astype(
        jnp.bfloat16
    )


def softmax_block(queries, keys_block, values_block, scaling, allowed):
    scores = (
        jnp.einsum("thd,nhd->thn", queries, keys_block, preferred_element_type=jnp.float32)
        * scaling
    )
    if allowed is not None:
        scores = jnp.where(allowed, scores, NEG_FILL)
    top_score = jnp.max(scores, axis=2)
    exponent = jnp.exp(scores - top_score[:, :, None])
    weight = jnp.sum(exponent, axis=2)
    blended = jnp.einsum(
        "thn,nhd->thd",
        exponent.astype(jnp.bfloat16),
        values_block,
        preferred_element_type=jnp.float32,
    )
    return (top_score, weight, blended)


def merge_states(former, latter):
    top_one, weight_one, blend_one = former
    top_two, weight_two, blend_two = latter
    overall = jnp.maximum(top_one, top_two)
    factor_one = jnp.exp(top_one - overall)
    factor_two = jnp.exp(top_two - overall)
    return (
        overall,
        weight_one * factor_one + weight_two * factor_two,
        blend_one * factor_one[:, :, None] + blend_two * factor_two[:, :, None],
    )


def gather_rows(values, axis):
    count = lax.axis_size(axis)
    copies = jnp.broadcast_to(values[None], (count,) + values.shape)
    received = lax.all_to_all(copies, axis, 0, 0, tiled=True)
    return received.reshape((count * values.shape[0],) + values.shape[1:])


def sum_scatter_rows(values, axis):
    count = lax.axis_size(axis)
    parts = values.reshape((count, values.shape[0] // count) + values.shape[1:])
    received = lax.all_to_all(parts, axis, 0, 0, tiled=True)
    return jnp.sum(received.astype(jnp.float32), axis=0)


CORES = 2


def fetch_slot(prefix_cache, group_prefix, group_rank, rider):
    group_count = lax.axis_size("dp")
    chips = group_count // CORES
    chip = group_rank // CORES
    core = group_rank % CORES
    slot_wanted = group_prefix[group_rank]
    partner_slot = group_prefix[group_rank ^ 1]
    mine_at = (slot_wanted // CORES - chip) % chips
    theirs_at = (partner_slot // CORES - chip) % chips
    onward = [(i, (i + CORES) % group_count) for i in range(group_count)]
    backward = [(i, (i - CORES) % group_count) for i in range(group_count)]
    mine = prefix_cache
    theirs = prefix_cache
    ahead = prefix_cache
    behind = prefix_cache
    for step in range(1, chips // 2 + 1):
        ahead = lax.ppermute(ahead, "dp", onward)
        mine = jnp.where(mine_at == (chips - step) % chips, ahead, mine)
        theirs = jnp.where(theirs_at == (chips - step) % chips, ahead, theirs)
        if step < chips - step:
            behind = lax.ppermute(behind, "dp", backward)
            mine = jnp.where(mine_at == step, behind, mine)
            theirs = jnp.where(theirs_at == step, behind, theirs)
        if step == 1:
            ahead, behind, rider = lax.optimization_barrier((ahead, behind, rider))
        mine, theirs, ahead, behind = lax.optimization_barrier((mine, theirs, ahead, behind))
    swapped = lax.ppermute(theirs, "dp", [(i, i ^ 1) for i in range(group_count)])
    return slot_wanted % CORES == core, mine, swapped, rider


def on_device(
    tokens,
    lengths,
    group_prefix,
    prefix_cache,
    query_weight,
    key_weight,
    value_weight,
    out_weight,
    gate_up_weight,
    down_weight,
):
    tensor_count = lax.axis_size("tensor")
    tensor_rank = lax.axis_index("tensor")
    group_rank = lax.axis_index("dp")
    row_count = tokens.shape[0]
    group_tokens = row_count * tensor_count
    local_heads = query_weight.shape[1] // HD
    head_ratio = QH // KVH
    local_kv = max(1, local_heads // head_ratio)
    repeat_by = local_heads // local_kv
    kv_first = tensor_rank * local_heads // head_ratio
    kv_total = KVH * HD
    query_width = local_heads * HD
    kv_width = local_kv * HD
    scaling = 1.0 / math.sqrt(HD)
    positions, request = token_layout(lengths[0], group_tokens)
    cos_table, sin_table = rope_tables(positions)
    key_cols = lax.dynamic_slice_in_dim(key_weight, kv_first * HD, kv_width, 1)
    value_cols = lax.dynamic_slice_in_dim(value_weight, kv_first * HD, kv_width, 1)
    projection = jnp.concatenate([query_weight, key_cols, value_cols], axis=1)

    shard_rows = prefix_cache.shape[0]
    kv_groups = KVH // local_kv
    token_copies = jnp.broadcast_to(tokens[None], (tensor_count,) + tokens.shape)
    ring_input, token_copies = lax.optimization_barrier((prefix_cache, token_copies))
    group_rows = lax.all_to_all(token_copies, "tensor", 0, 0, tiled=True).reshape(
        group_tokens, tokens.shape[1]
    )
    on_core, mine, swapped, projection = fetch_slot(ring_input, group_prefix, group_rank, projection)
    out_full = lax.all_gather(out_weight, "tensor", axis=0, tiled=True)
    chosen = jnp.where(on_core, mine, swapped)
    by_head = jnp.stack(
        [
            jnp.concatenate(
                [
                    chosen[:, head * kv_width : (head + 1) * kv_width],
                    chosen[:, kv_total + head * kv_width : kv_total + (head + 1) * kv_width],
                ],
                axis=1,
            )
            for head in range(kv_groups)
        ]
    )
    outgoing = jnp.repeat(by_head, tensor_count // kv_groups, axis=0)
    incoming = lax.all_to_all(outgoing, "tensor", 0, 0, tiled=True)
    seg_rows = tensor_count * shard_rows
    incoming = incoming.reshape(seg_rows, 2 * kv_width)
    keys_block = jnp.repeat(incoming[:, :kv_width].reshape(seg_rows, local_kv, HD), repeat_by, axis=1)
    values_block = jnp.repeat(incoming[:, kv_width:].reshape(seg_rows, local_kv, HD), repeat_by, axis=1)

    segment = norm_rows(group_rows)
    seg_rows = segment.shape[0]
    mapped = jnp.dot(segment, projection, preferred_element_type=jnp.float32)
    query_part = rotate(
        mapped[:, :query_width].reshape(seg_rows, local_heads, HD), cos_table, sin_table
    )
    key_part = rotate(
        mapped[:, query_width : query_width + kv_width].reshape(seg_rows, local_kv, HD),
        cos_table,
        sin_table,
    )
    projected = jnp.concatenate(
        [
            query_part.reshape(seg_rows, query_width),
            key_part.reshape(seg_rows, kv_width),
            mapped[:, query_width + kv_width :],
        ],
        axis=1,
    ).astype(jnp.bfloat16)
    queries = projected[:, :query_width].reshape(group_tokens, local_heads, HD)
    own_keys = jnp.repeat(
        projected[:, query_width : query_width + kv_width].reshape(group_tokens, local_kv, HD),
        repeat_by,
        axis=1,
    )
    own_values = jnp.repeat(
        projected[:, query_width + kv_width :].reshape(group_tokens, local_kv, HD),
        repeat_by,
        axis=1,
    )
    start_state = (
        jnp.full((group_tokens, local_heads), NEG_FILL, jnp.float32),
        jnp.zeros((group_tokens, local_heads), jnp.float32),
        jnp.zeros((group_tokens, local_heads, HD), jnp.float32),
    )
    prefix_state = merge_states(
        start_state, softmax_block(queries, keys_block, values_block, scaling, None)
    )
    indices = jnp.arange(group_tokens, dtype=jnp.int32)
    allowed = (request[:, None] == request[None, :]) & (indices[None, :] <= indices[:, None])
    suffix_state = softmax_block(queries, own_keys, own_values, scaling, allowed[:, None, :])
    top_score, weight, blended = merge_states(prefix_state, suffix_state)
    attended = (blended / weight[:, :, None]).astype(jnp.bfloat16).reshape(group_tokens, query_width)
    every_head = gather_rows(jnp.transpose(attended)[None], "tensor")
    every_head = jnp.transpose(every_head.reshape(tensor_count * query_width, group_tokens))
    attn_sum = jnp.dot(every_head, out_full, preferred_element_type=jnp.float32)
    middle = (group_rows.astype(jnp.float32) + attn_sum).astype(jnp.bfloat16)
    segment = norm_rows(middle)
    gate_value = jnp.dot(segment, gate_up_weight[0], preferred_element_type=jnp.float32)
    upward = jnp.dot(segment, gate_up_weight[1], preferred_element_type=jnp.float32)
    hidden = (jax.nn.silu(gate_value) * upward).astype(jnp.bfloat16)
    ffn_sum = sum_scatter_rows(
        jnp.dot(hidden, down_weight, preferred_element_type=jnp.float32).astype(jnp.bfloat16),
        "tensor",
    )
    own_middle = lax.dynamic_slice_in_dim(middle, tensor_rank * row_count, row_count, 0)
    return (own_middle.astype(jnp.float32) + ffn_sum).astype(jnp.bfloat16)


def solution(mesh):
    return jax.shard_map(
        on_device,
        mesh=mesh,
        in_specs=(
            P(("dp", "tensor"), None),
            P("dp", None),
            P(),
            P(("dp", "tensor"), None),
            P(None, "tensor"),
            P(),
            P(),
            P("tensor", None),
            P(None, None, "tensor"),
            P("tensor", None),
        ),
        out_specs=P(("dp", "tensor"), None),
        check_vma=False,
    )
```

```python
import math

import jax
import jax.numpy as jnp
from jax import lax
from jax.sharding import PartitionSpec as P

QH = 16
KVH = 4
HD = 64
PLEN = 4096


NEG_FILL = -1e30


def token_layout(lengths, total_rows):
    ends_at = jnp.cumsum(lengths)
    starts_at = ends_at - lengths
    indices = jnp.arange(total_rows, dtype=jnp.int32)
    request = jnp.sum((indices[:, None] >= ends_at[None, :]).astype(jnp.int32), axis=1)
    begins = jnp.max(
        jnp.where(starts_at[None, :] <= indices[:, None], starts_at[None, :], 0), axis=1
    )
    return ((PLEN + indices - begins).astype(jnp.float32), request)


def rope_tables(positions):
    halves = HD // 2
    steps_float = jnp.arange(halves, dtype=jnp.float32)
    inverse = jnp.exp(steps_float * (-2.0 * math.log(10000.0) / HD))
    angles = positions[:, None] * inverse[None, :]
    return (jnp.cos(angles), jnp.sin(angles))


def rotate(values, cos_table, sin_table):
    halves = values.shape[-1] // 2
    former = values[..., :halves]
    latter = values[..., halves:]
    cos_rows = cos_table[:, None, :]
    sin_rows = sin_table[:, None, :]
    return jnp.concatenate(
        [former * cos_rows - latter * sin_rows, latter * cos_rows + former * sin_rows], axis=-1
    )


def norm_rows(inputs):
    floats = inputs.astype(jnp.float32)
    return (floats * lax.rsqrt(jnp.mean(floats * floats, axis=-1, keepdims=True) + 1e-05)).astype(
        jnp.bfloat16
    )


def softmax_block(queries, keys_block, values_block, scaling, allowed):
    scores = (
        jnp.einsum("thd,nhd->thn", queries, keys_block, preferred_element_type=jnp.float32)
        * scaling
    )
    if allowed is not None:
        scores = jnp.where(allowed, scores, NEG_FILL)
    top_score = jnp.max(scores, axis=2)
    exponent = jnp.exp(scores - top_score[:, :, None])
    weight = jnp.sum(exponent, axis=2)
    blended = jnp.einsum(
        "thn,nhd->thd",
        exponent.astype(jnp.bfloat16),
        values_block,
        preferred_element_type=jnp.float32,
    )
    return (top_score, weight, blended)


def merge_states(former, latter):
    top_one, weight_one, blend_one = former
    top_two, weight_two, blend_two = latter
    overall = jnp.maximum(top_one, top_two)
    factor_one = jnp.exp(top_one - overall)
    factor_two = jnp.exp(top_two - overall)
    return (
        overall,
        weight_one * factor_one + weight_two * factor_two,
        blend_one * factor_one[:, :, None] + blend_two * factor_two[:, :, None],
    )


def gather_rows(values, axis):
    count = lax.axis_size(axis)
    copies = jnp.broadcast_to(values[None], (count,) + values.shape)
    received = lax.all_to_all(copies, axis, 0, 0, tiled=True)
    return received.reshape((count * values.shape[0],) + values.shape[1:])


def sum_scatter_rows(values, axis):
    count = lax.axis_size(axis)
    parts = values.reshape((count, values.shape[0] // count) + values.shape[1:])
    received = lax.all_to_all(parts, axis, 0, 0, tiled=True)
    return jnp.sum(received.astype(jnp.float32), axis=0)


CORES = 2


def fetch_slot(prefix_cache, group_prefix, group_rank, rider):
    group_count = lax.axis_size("dp")
    chips = group_count // CORES
    chip = group_rank // CORES
    core = group_rank % CORES
    slot_wanted = group_prefix[group_rank]
    partner_slot = group_prefix[group_rank ^ 1]
    mine_at = (slot_wanted // CORES - chip) % chips
    theirs_at = (partner_slot // CORES - chip) % chips
    onward = [(i, (i + CORES) % group_count) for i in range(group_count)]
    backward = [(i, (i - CORES) % group_count) for i in range(group_count)]
    mine = prefix_cache
    theirs = prefix_cache
    ahead = prefix_cache
    behind = prefix_cache
    for step in range(1, chips // 2 + 1):
        ahead = lax.ppermute(ahead, "dp", onward)
        mine = jnp.where(mine_at == (chips - step) % chips, ahead, mine)
        theirs = jnp.where(theirs_at == (chips - step) % chips, ahead, theirs)
        if step < chips - step:
            behind = lax.ppermute(behind, "dp", backward)
            mine = jnp.where(mine_at == step, behind, mine)
            theirs = jnp.where(theirs_at == step, behind, theirs)
        if step == 1:
            ahead, behind, rider = lax.optimization_barrier((ahead, behind, rider))
        mine, theirs, ahead, behind = lax.optimization_barrier((mine, theirs, ahead, behind))
    swapped = lax.ppermute(theirs, "dp", [(i, i ^ 1) for i in range(group_count)])
    return slot_wanted % CORES == core, mine, swapped, rider


def on_device(
    tokens,
    lengths,
    group_prefix,
    prefix_cache,
    query_weight,
    key_weight,
    value_weight,
    out_weight,
    gate_up_weight,
    down_weight,
):
    tensor_count = lax.axis_size("tensor")
    tensor_rank = lax.axis_index("tensor")
    group_rank = lax.axis_index("dp")
    row_count = tokens.shape[0]
    group_tokens = row_count * tensor_count
    local_heads = query_weight.shape[1] // HD
    head_ratio = QH // KVH
    local_kv = max(1, local_heads // head_ratio)
    repeat_by = local_heads // local_kv
    kv_first = tensor_rank * local_heads // head_ratio
    kv_total = KVH * HD
    query_width = local_heads * HD
    kv_width = local_kv * HD
    scaling = 1.0 / math.sqrt(HD)
    positions, request = token_layout(lengths[0], group_tokens)
    cos_table, sin_table = rope_tables(positions)
    key_cols = lax.dynamic_slice_in_dim(key_weight, kv_first * HD, kv_width, 1)
    value_cols = lax.dynamic_slice_in_dim(value_weight, kv_first * HD, kv_width, 1)
    projection = jnp.concatenate([query_weight, key_cols, value_cols], axis=1)

    shard_rows = prefix_cache.shape[0]
    kv_groups = KVH // local_kv
    by_head = prefix_cache.reshape(shard_rows, 2, kv_groups, kv_width)
    by_head = jnp.transpose(by_head, (2, 0, 1, 3)).reshape(kv_groups, shard_rows, 2 * kv_width)
    on_core, mine, swapped, projection = fetch_slot(by_head, group_prefix, group_rank, projection)
    out_full = lax.all_gather(out_weight, "tensor", axis=0, tiled=True)
    outgoing = jnp.where(
        on_core,
        jnp.repeat(mine, tensor_count // kv_groups, axis=0),
        jnp.repeat(swapped, tensor_count // kv_groups, axis=0),
    )
    incoming = lax.all_to_all(outgoing, "tensor", 0, 0, tiled=True)
    seg_rows = tensor_count * shard_rows
    incoming = incoming.reshape(seg_rows, 2 * kv_width)
    keys_block = jnp.repeat(incoming[:, :kv_width].reshape(seg_rows, local_kv, HD), repeat_by, axis=1)
    values_block = jnp.repeat(incoming[:, kv_width:].reshape(seg_rows, local_kv, HD), repeat_by, axis=1)

    group_rows = lax.all_gather(tokens, "tensor", axis=0, tiled=True)
    segment = norm_rows(group_rows)
    seg_rows = segment.shape[0]
    mapped = jnp.dot(segment, projection, preferred_element_type=jnp.float32)
    query_part = rotate(
        mapped[:, :query_width].reshape(seg_rows, local_heads, HD), cos_table, sin_table
    )
    key_part = rotate(
        mapped[:, query_width : query_width + kv_width].reshape(seg_rows, local_kv, HD),
        cos_table,
        sin_table,
    )
    projected = jnp.concatenate(
        [
            query_part.reshape(seg_rows, query_width),
            key_part.reshape(seg_rows, kv_width),
            mapped[:, query_width + kv_width :],
        ],
        axis=1,
    ).astype(jnp.bfloat16)
    queries = projected[:, :query_width].reshape(group_tokens, local_heads, HD)
    own_keys = jnp.repeat(
        projected[:, query_width : query_width + kv_width].reshape(group_tokens, local_kv, HD),
        repeat_by,
        axis=1,
    )
    own_values = jnp.repeat(
        projected[:, query_width + kv_width :].reshape(group_tokens, local_kv, HD),
        repeat_by,
        axis=1,
    )
    start_state = (
        jnp.full((group_tokens, local_heads), NEG_FILL, jnp.float32),
        jnp.zeros((group_tokens, local_heads), jnp.float32),
        jnp.zeros((group_tokens, local_heads, HD), jnp.float32),
    )
    prefix_state = merge_states(
        start_state, softmax_block(queries, keys_block, values_block, scaling, None)
    )
    indices = jnp.arange(group_tokens, dtype=jnp.int32)
    allowed = (request[:, None] == request[None, :]) & (indices[None, :] <= indices[:, None])
    suffix_state = softmax_block(queries, own_keys, own_values, scaling, allowed[:, None, :])
    top_score, weight, blended = merge_states(prefix_state, suffix_state)
    attended = (blended / weight[:, :, None]).astype(jnp.bfloat16).reshape(group_tokens, query_width)
    every_head = gather_rows(jnp.transpose(attended)[None], "tensor")
    every_head = jnp.transpose(every_head.reshape(tensor_count * query_width, group_tokens))
    attn_sum = jnp.dot(every_head, out_full, preferred_element_type=jnp.float32)
    middle = (group_rows.astype(jnp.float32) + attn_sum).astype(jnp.bfloat16)
    segment = norm_rows(middle)
    gate_value = jnp.dot(segment, gate_up_weight[0], preferred_element_type=jnp.float32)
    upward = jnp.dot(segment, gate_up_weight[1], preferred_element_type=jnp.float32)
    hidden = (jax.nn.silu(gate_value) * upward).astype(jnp.bfloat16)
    ffn_sum = sum_scatter_rows(
        jnp.dot(hidden, down_weight, preferred_element_type=jnp.float32).astype(jnp.bfloat16),
        "tensor",
    )
    own_middle = lax.dynamic_slice_in_dim(middle, tensor_rank * row_count, row_count, 0)
    return (own_middle.astype(jnp.float32) + ffn_sum).astype(jnp.bfloat16)


def solution(mesh):
    return jax.shard_map(
        on_device,
        mesh=mesh,
        in_specs=(
            P(("dp", "tensor"), None),
            P("dp", None),
            P(),
            P(("dp", "tensor"), None),
            P(None, "tensor"),
            P(),
            P(),
            P("tensor", None),
            P(None, None, "tensor"),
            P("tensor", None),
        ),
        out_specs=P(("dp", "tensor"), None),
        check_vma=False,
    )
```

```python
import math

import jax
import jax.numpy as jnp
from jax import lax
from jax.sharding import PartitionSpec as P

QH = 16
KVH = 4
HD = 64
PLEN = 4096


NEG_FILL = -1e30


def token_layout(lengths, total_rows):
    ends_at = jnp.cumsum(lengths)
    starts_at = ends_at - lengths
    indices = jnp.arange(total_rows, dtype=jnp.int32)
    request = jnp.sum((indices[:, None] >= ends_at[None, :]).astype(jnp.int32), axis=1)
    begins = jnp.max(
        jnp.where(starts_at[None, :] <= indices[:, None], starts_at[None, :], 0), axis=1
    )
    return ((PLEN + indices - begins).astype(jnp.float32), request)


def rope_tables(positions):
    halves = HD // 2
    steps_float = jnp.arange(halves, dtype=jnp.float32)
    inverse = jnp.exp(steps_float * (-2.0 * math.log(10000.0) / HD))
    angles = positions[:, None] * inverse[None, :]
    return (jnp.cos(angles), jnp.sin(angles))


def rotate(values, cos_table, sin_table):
    halves = values.shape[-1] // 2
    former = values[..., :halves]
    latter = values[..., halves:]
    cos_rows = cos_table[:, None, :]
    sin_rows = sin_table[:, None, :]
    return jnp.concatenate(
        [former * cos_rows - latter * sin_rows, latter * cos_rows + former * sin_rows], axis=-1
    )


def norm_rows(inputs):
    floats = inputs.astype(jnp.float32)
    return (floats * lax.rsqrt(jnp.mean(floats * floats, axis=-1, keepdims=True) + 1e-05)).astype(
        jnp.bfloat16
    )


def softmax_block(queries, keys_block, values_block, scaling, allowed):
    scores = (
        jnp.einsum("thd,nhd->thn", queries, keys_block, preferred_element_type=jnp.float32)
        * scaling
    )
    if allowed is not None:
        scores = jnp.where(allowed, scores, NEG_FILL)
    top_score = jnp.max(scores, axis=2)
    exponent = jnp.exp(scores - top_score[:, :, None])
    weight = jnp.sum(exponent, axis=2)
    blended = jnp.einsum(
        "thn,nhd->thd",
        exponent.astype(jnp.bfloat16),
        values_block,
        preferred_element_type=jnp.float32,
    )
    return (top_score, weight, blended)


def merge_states(former, latter):
    top_one, weight_one, blend_one = former
    top_two, weight_two, blend_two = latter
    overall = jnp.maximum(top_one, top_two)
    factor_one = jnp.exp(top_one - overall)
    factor_two = jnp.exp(top_two - overall)
    return (
        overall,
        weight_one * factor_one + weight_two * factor_two,
        blend_one * factor_one[:, :, None] + blend_two * factor_two[:, :, None],
    )


def gather_rows(values, axis):
    count = lax.axis_size(axis)
    copies = jnp.broadcast_to(values[None], (count,) + values.shape)
    received = lax.all_to_all(copies, axis, 0, 0, tiled=True)
    return received.reshape((count * values.shape[0],) + values.shape[1:])


def sum_scatter_rows(values, axis):
    count = lax.axis_size(axis)
    parts = values.reshape((count, values.shape[0] // count) + values.shape[1:])
    received = lax.all_to_all(parts, axis, 0, 0, tiled=True)
    return jnp.sum(received.astype(jnp.float32), axis=0)


CORES = 2


def fetch_slot(prefix_cache, group_prefix, group_rank, rider):
    group_count = lax.axis_size("dp")
    chips = group_count // CORES
    chip = group_rank // CORES
    core = group_rank % CORES
    slot_wanted = group_prefix[group_rank]
    partner_slot = group_prefix[group_rank ^ 1]
    mine_at = (slot_wanted // CORES - chip) % chips
    theirs_at = (partner_slot // CORES - chip) % chips
    onward = [(i, (i + CORES) % group_count) for i in range(group_count)]
    backward = [(i, (i - CORES) % group_count) for i in range(group_count)]
    mine = prefix_cache
    theirs = prefix_cache
    ahead = prefix_cache
    behind = prefix_cache
    for step in range(1, chips // 2 + 1):
        ahead = lax.ppermute(ahead, "dp", onward)
        mine = jnp.where(mine_at == (chips - step) % chips, ahead, mine)
        theirs = jnp.where(theirs_at == (chips - step) % chips, ahead, theirs)
        if step < chips - step:
            behind = lax.ppermute(behind, "dp", backward)
            mine = jnp.where(mine_at == step, behind, mine)
            theirs = jnp.where(theirs_at == step, behind, theirs)
        if step == 1:
            ahead, behind, rider[0] = lax.optimization_barrier((ahead, behind, rider[0]))
        if step == 3:
            ahead, behind, rider[1] = lax.optimization_barrier((ahead, behind, rider[1]))
        mine, theirs, ahead, behind = lax.optimization_barrier((mine, theirs, ahead, behind))
    swapped = lax.ppermute(theirs, "dp", [(i, i ^ 1) for i in range(group_count)])
    return slot_wanted % CORES == core, mine, swapped, rider


def on_device(
    tokens,
    lengths,
    group_prefix,
    prefix_cache,
    query_weight,
    key_weight,
    value_weight,
    out_weight,
    gate_up_weight,
    down_weight,
):
    tensor_count = lax.axis_size("tensor")
    tensor_rank = lax.axis_index("tensor")
    group_rank = lax.axis_index("dp")
    row_count = tokens.shape[0]
    group_tokens = row_count * tensor_count
    local_heads = query_weight.shape[1] // HD
    head_ratio = QH // KVH
    local_kv = max(1, local_heads // head_ratio)
    repeat_by = local_heads // local_kv
    kv_first = tensor_rank * local_heads // head_ratio
    kv_total = KVH * HD
    query_width = local_heads * HD
    kv_width = local_kv * HD
    scaling = 1.0 / math.sqrt(HD)
    positions, request = token_layout(lengths[0], group_tokens)
    cos_table, sin_table = rope_tables(positions)
    key_cols = lax.dynamic_slice_in_dim(key_weight, kv_first * HD, kv_width, 1)
    value_cols = lax.dynamic_slice_in_dim(value_weight, kv_first * HD, kv_width, 1)
    projection = jnp.concatenate([query_weight, key_cols, value_cols], axis=1)

    shard_rows = prefix_cache.shape[0]
    kv_groups = KVH // local_kv
    by_head = prefix_cache.reshape(shard_rows, 2, kv_groups, kv_width)
    by_head = jnp.transpose(by_head, (2, 0, 1, 3)).reshape(kv_groups, shard_rows, 2 * kv_width)
    half_cols = out_weight.shape[1] // 2
    out_right = gather_rows(out_weight[:, half_cols:], "tensor")
    on_core, mine, swapped, (projection, out_right) = fetch_slot(
        by_head, group_prefix, group_rank, [projection, out_right]
    )
    out_left = lax.all_gather(out_weight[:, :half_cols], "tensor", axis=0, tiled=True)
    outgoing = jnp.where(
        on_core,
        jnp.repeat(mine, tensor_count // kv_groups, axis=0),
        jnp.repeat(swapped, tensor_count // kv_groups, axis=0),
    )
    incoming = lax.all_to_all(outgoing, "tensor", 0, 0, tiled=True)
    seg_rows = tensor_count * shard_rows
    incoming = incoming.reshape(seg_rows, 2 * kv_width)
    keys_block = jnp.repeat(incoming[:, :kv_width].reshape(seg_rows, local_kv, HD), repeat_by, axis=1)
    values_block = jnp.repeat(incoming[:, kv_width:].reshape(seg_rows, local_kv, HD), repeat_by, axis=1)

    group_rows = lax.all_gather(tokens, "tensor", axis=0, tiled=True)
    segment = norm_rows(group_rows)
    seg_rows = segment.shape[0]
    mapped = jnp.dot(segment, projection, preferred_element_type=jnp.float32)
    query_part = rotate(
        mapped[:, :query_width].reshape(seg_rows, local_heads, HD), cos_table, sin_table
    )
    key_part = rotate(
        mapped[:, query_width : query_width + kv_width].reshape(seg_rows, local_kv, HD),
        cos_table,
        sin_table,
    )
    projected = jnp.concatenate(
        [
            query_part.reshape(seg_rows, query_width),
            key_part.reshape(seg_rows, kv_width),
            mapped[:, query_width + kv_width :],
        ],
        axis=1,
    ).astype(jnp.bfloat16)
    queries = projected[:, :query_width].reshape(group_tokens, local_heads, HD)
    own_keys = jnp.repeat(
        projected[:, query_width : query_width + kv_width].reshape(group_tokens, local_kv, HD),
        repeat_by,
        axis=1,
    )
    own_values = jnp.repeat(
        projected[:, query_width + kv_width :].reshape(group_tokens, local_kv, HD),
        repeat_by,
        axis=1,
    )
    start_state = (
        jnp.full((group_tokens, local_heads), NEG_FILL, jnp.float32),
        jnp.zeros((group_tokens, local_heads), jnp.float32),
        jnp.zeros((group_tokens, local_heads, HD), jnp.float32),
    )
    prefix_state = merge_states(
        start_state, softmax_block(queries, keys_block, values_block, scaling, None)
    )
    indices = jnp.arange(group_tokens, dtype=jnp.int32)
    allowed = (request[:, None] == request[None, :]) & (indices[None, :] <= indices[:, None])
    suffix_state = softmax_block(queries, own_keys, own_values, scaling, allowed[:, None, :])
    top_score, weight, blended = merge_states(prefix_state, suffix_state)
    attended = (blended / weight[:, :, None]).astype(jnp.bfloat16).reshape(group_tokens, query_width)
    every_head = gather_rows(jnp.transpose(attended)[None], "tensor")
    every_head = jnp.transpose(every_head.reshape(tensor_count * query_width, group_tokens))
    attn_sum = jnp.concatenate(
        [
            jnp.dot(every_head, out_left, preferred_element_type=jnp.float32),
            jnp.dot(every_head, out_right, preferred_element_type=jnp.float32),
        ],
        axis=1,
    )
    middle = (group_rows.astype(jnp.float32) + attn_sum).astype(jnp.bfloat16)
    segment = norm_rows(middle)
    gate_value = jnp.dot(segment, gate_up_weight[0], preferred_element_type=jnp.float32)
    upward = jnp.dot(segment, gate_up_weight[1], preferred_element_type=jnp.float32)
    hidden = (jax.nn.silu(gate_value) * upward).astype(jnp.bfloat16)
    ffn_sum = sum_scatter_rows(
        jnp.dot(hidden, down_weight, preferred_element_type=jnp.float32).astype(jnp.bfloat16),
        "tensor",
    )
    own_middle = lax.dynamic_slice_in_dim(middle, tensor_rank * row_count, row_count, 0)
    return (own_middle.astype(jnp.float32) + ffn_sum).astype(jnp.bfloat16)


def solution(mesh):
    return jax.shard_map(
        on_device,
        mesh=mesh,
        in_specs=(
            P(("dp", "tensor"), None),
            P("dp", None),
            P(),
            P(("dp", "tensor"), None),
            P(None, "tensor"),
            P(),
            P(),
            P("tensor", None),
            P(None, None, "tensor"),
            P("tensor", None),
        ),
        out_specs=P(("dp", "tensor"), None),
        check_vma=False,
    )
```

```python
import math

import jax
import jax.numpy as jnp
from jax import lax
from jax.sharding import PartitionSpec as P

QH = 16
KVH = 4
HD = 64
PLEN = 4096


NEG_FILL = -1e30


def token_layout(lengths, total_rows):
    ends_at = jnp.cumsum(lengths)
    starts_at = ends_at - lengths
    indices = jnp.arange(total_rows, dtype=jnp.int32)
    request = jnp.sum((indices[:, None] >= ends_at[None, :]).astype(jnp.int32), axis=1)
    begins = jnp.max(
        jnp.where(starts_at[None, :] <= indices[:, None], starts_at[None, :], 0), axis=1
    )
    return ((PLEN + indices - begins).astype(jnp.float32), request)


def rope_tables(positions):
    halves = HD // 2
    steps_float = jnp.arange(halves, dtype=jnp.float32)
    inverse = jnp.exp(steps_float * (-2.0 * math.log(10000.0) / HD))
    angles = positions[:, None] * inverse[None, :]
    return (jnp.cos(angles), jnp.sin(angles))


def rotate(values, cos_table, sin_table):
    halves = values.shape[-1] // 2
    former = values[..., :halves]
    latter = values[..., halves:]
    cos_rows = cos_table[:, None, :]
    sin_rows = sin_table[:, None, :]
    return jnp.concatenate(
        [former * cos_rows - latter * sin_rows, latter * cos_rows + former * sin_rows], axis=-1
    )


def norm_rows(inputs):
    floats = inputs.astype(jnp.float32)
    return (floats * lax.rsqrt(jnp.mean(floats * floats, axis=-1, keepdims=True) + 1e-05)).astype(
        jnp.bfloat16
    )


def softmax_block(queries, keys_block, values_block, scaling, allowed):
    scores = (
        jnp.einsum("thd,nhd->thn", queries, keys_block, preferred_element_type=jnp.float32)
        * scaling
    )
    if allowed is not None:
        scores = jnp.where(allowed, scores, NEG_FILL)
    top_score = jnp.max(scores, axis=2)
    exponent = jnp.exp(scores - top_score[:, :, None])
    weight = jnp.sum(exponent, axis=2)
    blended = jnp.einsum(
        "thn,nhd->thd",
        exponent.astype(jnp.bfloat16),
        values_block,
        preferred_element_type=jnp.float32,
    )
    return (top_score, weight, blended)


def merge_states(former, latter):
    top_one, weight_one, blend_one = former
    top_two, weight_two, blend_two = latter
    overall = jnp.maximum(top_one, top_two)
    factor_one = jnp.exp(top_one - overall)
    factor_two = jnp.exp(top_two - overall)
    return (
        overall,
        weight_one * factor_one + weight_two * factor_two,
        blend_one * factor_one[:, :, None] + blend_two * factor_two[:, :, None],
    )


def gather_rows(values, axis):
    count = lax.axis_size(axis)
    copies = jnp.broadcast_to(values[None], (count,) + values.shape)
    received = lax.all_to_all(copies, axis, 0, 0, tiled=True)
    return received.reshape((count * values.shape[0],) + values.shape[1:])


def sum_scatter_rows(values, axis):
    count = lax.axis_size(axis)
    parts = values.reshape((count, values.shape[0] // count) + values.shape[1:])
    received = lax.all_to_all(parts, axis, 0, 0, tiled=True)
    return jnp.sum(received.astype(jnp.float32), axis=0)


CORES = 2


def fetch_slot(prefix_cache, group_prefix, group_rank, rider):
    group_count = lax.axis_size("dp")
    chips = group_count // CORES
    chip = group_rank // CORES
    core = group_rank % CORES
    slot_wanted = group_prefix[group_rank]
    partner_slot = group_prefix[group_rank ^ 1]
    mine_at = (slot_wanted // CORES - chip) % chips
    theirs_at = (partner_slot // CORES - chip) % chips
    onward = [(i, (i + CORES) % group_count) for i in range(group_count)]
    backward = [(i, (i - CORES) % group_count) for i in range(group_count)]
    mine = prefix_cache
    theirs = prefix_cache
    ahead = prefix_cache
    behind = prefix_cache
    for step in range(1, chips // 2 + 1):
        ahead = lax.ppermute(ahead, "dp", onward)
        mine = jnp.where(mine_at == (chips - step) % chips, ahead, mine)
        theirs = jnp.where(theirs_at == (chips - step) % chips, ahead, theirs)
        if step < chips - step:
            behind = lax.ppermute(behind, "dp", backward)
            mine = jnp.where(mine_at == step, behind, mine)
            theirs = jnp.where(theirs_at == step, behind, theirs)
        if step == 2:
            ahead, behind, rider = lax.optimization_barrier((ahead, behind, rider))
        mine, theirs, ahead, behind = lax.optimization_barrier((mine, theirs, ahead, behind))
    swapped = lax.ppermute(theirs, "dp", [(i, i ^ 1) for i in range(group_count)])
    return slot_wanted % CORES == core, mine, swapped, rider


def on_device(
    tokens,
    lengths,
    group_prefix,
    prefix_cache,
    query_weight,
    key_weight,
    value_weight,
    out_weight,
    gate_up_weight,
    down_weight,
):
    tensor_count = lax.axis_size("tensor")
    tensor_rank = lax.axis_index("tensor")
    group_rank = lax.axis_index("dp")
    row_count = tokens.shape[0]
    group_tokens = row_count * tensor_count
    local_heads = query_weight.shape[1] // HD
    head_ratio = QH // KVH
    local_kv = max(1, local_heads // head_ratio)
    repeat_by = local_heads // local_kv
    kv_first = tensor_rank * local_heads // head_ratio
    kv_total = KVH * HD
    query_width = local_heads * HD
    kv_width = local_kv * HD
    scaling = 1.0 / math.sqrt(HD)
    positions, request = token_layout(lengths[0], group_tokens)
    cos_table, sin_table = rope_tables(positions)
    key_cols = lax.dynamic_slice_in_dim(key_weight, kv_first * HD, kv_width, 1)
    value_cols = lax.dynamic_slice_in_dim(value_weight, kv_first * HD, kv_width, 1)
    projection = jnp.concatenate([query_weight, key_cols, value_cols], axis=1)

    shard_rows = prefix_cache.shape[0]
    kv_groups = KVH // local_kv
    by_head = prefix_cache.reshape(shard_rows, 2, kv_groups, kv_width)
    by_head = jnp.transpose(by_head, (2, 0, 1, 3)).reshape(kv_groups, shard_rows, 2 * kv_width)
    on_core, mine, swapped, projection = fetch_slot(by_head, group_prefix, group_rank, projection)
    out_full = lax.all_gather(out_weight, "tensor", axis=0, tiled=True)
    outgoing = jnp.where(
        on_core,
        jnp.repeat(mine, tensor_count // kv_groups, axis=0),
        jnp.repeat(swapped, tensor_count // kv_groups, axis=0),
    )
    incoming = lax.all_to_all(outgoing, "tensor", 0, 0, tiled=True)
    seg_rows = tensor_count * shard_rows
    incoming = incoming.reshape(seg_rows, 2 * kv_width)
    keys_block = jnp.repeat(incoming[:, :kv_width].reshape(seg_rows, local_kv, HD), repeat_by, axis=1)
    values_block = jnp.repeat(incoming[:, kv_width:].reshape(seg_rows, local_kv, HD), repeat_by, axis=1)

    group_rows = gather_rows(tokens, "tensor")
    segment = norm_rows(group_rows)
    seg_rows = segment.shape[0]
    mapped = jnp.dot(segment, projection, preferred_element_type=jnp.float32)
    query_part = rotate(
        mapped[:, :query_width].reshape(seg_rows, local_heads, HD), cos_table, sin_table
    )
    key_part = rotate(
        mapped[:, query_width : query_width + kv_width].reshape(seg_rows, local_kv, HD),
        cos_table,
        sin_table,
    )
    projected = jnp.concatenate(
        [
            query_part.reshape(seg_rows, query_width),
            key_part.reshape(seg_rows, kv_width),
            mapped[:, query_width + kv_width :],
        ],
        axis=1,
    ).astype(jnp.bfloat16)
    queries = projected[:, :query_width].reshape(group_tokens, local_heads, HD)
    own_keys = jnp.repeat(
        projected[:, query_width : query_width + kv_width].reshape(group_tokens, local_kv, HD),
        repeat_by,
        axis=1,
    )
    own_values = jnp.repeat(
        projected[:, query_width + kv_width :].reshape(group_tokens, local_kv, HD),
        repeat_by,
        axis=1,
    )
    start_state = (
        jnp.full((group_tokens, local_heads), NEG_FILL, jnp.float32),
        jnp.zeros((group_tokens, local_heads), jnp.float32),
        jnp.zeros((group_tokens, local_heads, HD), jnp.float32),
    )
    prefix_state = merge_states(
        start_state, softmax_block(queries, keys_block, values_block, scaling, None)
    )
    indices = jnp.arange(group_tokens, dtype=jnp.int32)
    allowed = (request[:, None] == request[None, :]) & (indices[None, :] <= indices[:, None])
    suffix_state = softmax_block(queries, own_keys, own_values, scaling, allowed[:, None, :])
    top_score, weight, blended = merge_states(prefix_state, suffix_state)
    attended = (blended / weight[:, :, None]).astype(jnp.bfloat16).reshape(group_tokens, query_width)
    every_head = gather_rows(jnp.transpose(attended)[None], "tensor")
    every_head = jnp.transpose(every_head.reshape(tensor_count * query_width, group_tokens))
    attn_sum = jnp.dot(every_head, out_full, preferred_element_type=jnp.float32)
    middle = (group_rows.astype(jnp.float32) + attn_sum).astype(jnp.bfloat16)
    segment = norm_rows(middle)
    gate_value = jnp.dot(segment, gate_up_weight[0], preferred_element_type=jnp.float32)
    upward = jnp.dot(segment, gate_up_weight[1], preferred_element_type=jnp.float32)
    hidden = (jax.nn.silu(gate_value) * upward).astype(jnp.bfloat16)
    ffn_sum = sum_scatter_rows(
        jnp.dot(hidden, down_weight, preferred_element_type=jnp.float32).astype(jnp.bfloat16),
        "tensor",
    )
    own_middle = lax.dynamic_slice_in_dim(middle, tensor_rank * row_count, row_count, 0)
    return (own_middle.astype(jnp.float32) + ffn_sum).astype(jnp.bfloat16)


def solution(mesh):
    return jax.shard_map(
        on_device,
        mesh=mesh,
        in_specs=(
            P(("dp", "tensor"), None),
            P("dp", None),
            P(),
            P(("dp", "tensor"), None),
            P(None, "tensor"),
            P(),
            P(),
            P("tensor", None),
            P(None, None, "tensor"),
            P("tensor", None),
        ),
        out_specs=P(("dp", "tensor"), None),
        check_vma=False,
    )
```

```python
import math

import jax
import jax.numpy as jnp
from jax import lax
from jax.sharding import PartitionSpec as P

QH = 16
KVH = 4
HD = 64
PLEN = 4096


NEG_FILL = -1e30


def token_layout(lengths, total_rows):
    ends_at = jnp.cumsum(lengths)
    starts_at = ends_at - lengths
    indices = jnp.arange(total_rows, dtype=jnp.int32)
    request = jnp.sum((indices[:, None] >= ends_at[None, :]).astype(jnp.int32), axis=1)
    begins = jnp.max(
        jnp.where(starts_at[None, :] <= indices[:, None], starts_at[None, :], 0), axis=1
    )
    return ((PLEN + indices - begins).astype(jnp.float32), request)


def rope_tables(positions):
    halves = HD // 2
    steps_float = jnp.arange(halves, dtype=jnp.float32)
    inverse = jnp.exp(steps_float * (-2.0 * math.log(10000.0) / HD))
    angles = positions[:, None] * inverse[None, :]
    return (jnp.cos(angles), jnp.sin(angles))


def rotate(values, cos_table, sin_table):
    halves = values.shape[-1] // 2
    former = values[..., :halves]
    latter = values[..., halves:]
    cos_rows = cos_table[:, None, :]
    sin_rows = sin_table[:, None, :]
    return jnp.concatenate(
        [former * cos_rows - latter * sin_rows, latter * cos_rows + former * sin_rows], axis=-1
    )


def norm_rows(inputs):
    floats = inputs.astype(jnp.float32)
    return (floats * lax.rsqrt(jnp.mean(floats * floats, axis=-1, keepdims=True) + 1e-05)).astype(
        jnp.bfloat16
    )


def softmax_block(queries, keys_block, values_block, scaling, allowed):
    scores = (
        jnp.einsum("thd,nhd->thn", queries, keys_block, preferred_element_type=jnp.float32)
        * scaling
    )
    if allowed is not None:
        scores = jnp.where(allowed, scores, NEG_FILL)
    top_score = jnp.max(scores, axis=2)
    exponent = jnp.exp(scores - top_score[:, :, None])
    weight = jnp.sum(exponent, axis=2)
    blended = jnp.einsum(
        "thn,nhd->thd",
        exponent.astype(jnp.bfloat16),
        values_block,
        preferred_element_type=jnp.float32,
    )
    return (top_score, weight, blended)


def merge_states(former, latter):
    top_one, weight_one, blend_one = former
    top_two, weight_two, blend_two = latter
    overall = jnp.maximum(top_one, top_two)
    factor_one = jnp.exp(top_one - overall)
    factor_two = jnp.exp(top_two - overall)
    return (
        overall,
        weight_one * factor_one + weight_two * factor_two,
        blend_one * factor_one[:, :, None] + blend_two * factor_two[:, :, None],
    )


def gather_rows(values, axis):
    count = lax.axis_size(axis)
    copies = jnp.broadcast_to(values[None], (count,) + values.shape)
    received = lax.all_to_all(copies, axis, 0, 0, tiled=True)
    return received.reshape((count * values.shape[0],) + values.shape[1:])


def sum_scatter_rows(values, axis):
    count = lax.axis_size(axis)
    parts = values.reshape((count, values.shape[0] // count) + values.shape[1:])
    received = lax.all_to_all(parts, axis, 0, 0, tiled=True)
    return jnp.sum(received.astype(jnp.float32), axis=0)


CORES = 2


def fetch_slot(prefix_cache, group_prefix, group_rank, rider):
    group_count = lax.axis_size("dp")
    chips = group_count // CORES
    chip = group_rank // CORES
    core = group_rank % CORES
    slot_wanted = group_prefix[group_rank]
    partner_slot = group_prefix[group_rank ^ 1]
    mine_at = (slot_wanted // CORES - chip) % chips
    theirs_at = (partner_slot // CORES - chip) % chips
    onward = [(i, (i + CORES) % group_count) for i in range(group_count)]
    backward = [(i, (i - CORES) % group_count) for i in range(group_count)]
    mine = prefix_cache
    theirs = prefix_cache
    ahead = prefix_cache
    behind = prefix_cache
    for step in range(1, chips // 2 + 1):
        ahead = lax.ppermute(ahead, "dp", onward)
        mine = jnp.where(mine_at == (chips - step) % chips, ahead, mine)
        theirs = jnp.where(theirs_at == (chips - step) % chips, ahead, theirs)
        if step < chips - step:
            behind = lax.ppermute(behind, "dp", backward)
            mine = jnp.where(mine_at == step, behind, mine)
            theirs = jnp.where(theirs_at == step, behind, theirs)
        if step == 1:
            ahead, behind, rider = lax.optimization_barrier((ahead, behind, rider))
        mine, theirs, ahead, behind = lax.optimization_barrier((mine, theirs, ahead, behind))
    swapped = lax.ppermute(theirs, "dp", [(i, i ^ 1) for i in range(group_count)])
    return slot_wanted % CORES == core, mine, swapped, rider


def on_device(
    tokens,
    lengths,
    group_prefix,
    prefix_cache,
    query_weight,
    key_weight,
    value_weight,
    out_weight,
    gate_up_weight,
    down_weight,
):
    tensor_count = lax.axis_size("tensor")
    tensor_rank = lax.axis_index("tensor")
    group_rank = lax.axis_index("dp")
    row_count = tokens.shape[0]
    group_tokens = row_count * tensor_count
    local_heads = query_weight.shape[1] // HD
    head_ratio = QH // KVH
    local_kv = max(1, local_heads // head_ratio)
    repeat_by = local_heads // local_kv
    kv_first = tensor_rank * local_heads // head_ratio
    kv_total = KVH * HD
    query_width = local_heads * HD
    kv_width = local_kv * HD
    scaling = 1.0 / math.sqrt(HD)
    positions, request = token_layout(lengths[0], group_tokens)
    cos_table, sin_table = rope_tables(positions)
    key_cols = lax.dynamic_slice_in_dim(key_weight, kv_first * HD, kv_width, 1)
    value_cols = lax.dynamic_slice_in_dim(value_weight, kv_first * HD, kv_width, 1)
    projection = jnp.concatenate([query_weight, key_cols, value_cols], axis=1)

    shard_rows = prefix_cache.shape[0]
    kv_groups = KVH // local_kv
    by_head = prefix_cache.reshape(shard_rows, 2, kv_groups, kv_width)
    by_head = jnp.transpose(by_head, (2, 0, 1, 3)).reshape(kv_groups, shard_rows, 2 * kv_width)
    on_core, mine, swapped, projection = fetch_slot(by_head, group_prefix, group_rank, projection)
    group_count = lax.axis_size("dp")
    core = group_rank % CORES
    half_cols = out_weight.shape[1] // CORES
    own_cols = lax.dynamic_slice_in_dim(out_weight, core * half_cols, half_cols, 1)
    own_cols = lax.all_gather(own_cols, "tensor", axis=0, tiled=True)
    other_cols = lax.ppermute(own_cols, "dp", [(i, i ^ 1) for i in range(group_count)])
    out_full = jnp.zeros((own_cols.shape[0], out_weight.shape[1]), own_cols.dtype)
    out_full = lax.dynamic_update_slice_in_dim(out_full, own_cols, core * half_cols, 1)
    out_full = lax.dynamic_update_slice_in_dim(out_full, other_cols, (1 - core) * half_cols, 1)
    outgoing = jnp.where(
        on_core,
        jnp.repeat(mine, tensor_count // kv_groups, axis=0),
        jnp.repeat(swapped, tensor_count // kv_groups, axis=0),
    )
    incoming = lax.all_to_all(outgoing, "tensor", 0, 0, tiled=True)
    seg_rows = tensor_count * shard_rows
    incoming = incoming.reshape(seg_rows, 2 * kv_width)
    keys_block = jnp.repeat(incoming[:, :kv_width].reshape(seg_rows, local_kv, HD), repeat_by, axis=1)
    values_block = jnp.repeat(incoming[:, kv_width:].reshape(seg_rows, local_kv, HD), repeat_by, axis=1)

    group_rows = gather_rows(tokens, "tensor")
    segment = norm_rows(group_rows)
    seg_rows = segment.shape[0]
    mapped = jnp.dot(segment, projection, preferred_element_type=jnp.float32)
    query_part = rotate(
        mapped[:, :query_width].reshape(seg_rows, local_heads, HD), cos_table, sin_table
    )
    key_part = rotate(
        mapped[:, query_width : query_width + kv_width].reshape(seg_rows, local_kv, HD),
        cos_table,
        sin_table,
    )
    projected = jnp.concatenate(
        [
            query_part.reshape(seg_rows, query_width),
            key_part.reshape(seg_rows, kv_width),
            mapped[:, query_width + kv_width :],
        ],
        axis=1,
    ).astype(jnp.bfloat16)
    queries = projected[:, :query_width].reshape(group_tokens, local_heads, HD)
    own_keys = jnp.repeat(
        projected[:, query_width : query_width + kv_width].reshape(group_tokens, local_kv, HD),
        repeat_by,
        axis=1,
    )
    own_values = jnp.repeat(
        projected[:, query_width + kv_width :].reshape(group_tokens, local_kv, HD),
        repeat_by,
        axis=1,
    )
    start_state = (
        jnp.full((group_tokens, local_heads), NEG_FILL, jnp.float32),
        jnp.zeros((group_tokens, local_heads), jnp.float32),
        jnp.zeros((group_tokens, local_heads, HD), jnp.float32),
    )
    prefix_state = merge_states(
        start_state, softmax_block(queries, keys_block, values_block, scaling, None)
    )
    indices = jnp.arange(group_tokens, dtype=jnp.int32)
    allowed = (request[:, None] == request[None, :]) & (indices[None, :] <= indices[:, None])
    suffix_state = softmax_block(queries, own_keys, own_values, scaling, allowed[:, None, :])
    top_score, weight, blended = merge_states(prefix_state, suffix_state)
    attended = (blended / weight[:, :, None]).astype(jnp.bfloat16).reshape(group_tokens, query_width)
    every_head = gather_rows(jnp.transpose(attended)[None], "tensor")
    every_head = jnp.transpose(every_head.reshape(tensor_count * query_width, group_tokens))
    attn_sum = jnp.dot(every_head, out_full, preferred_element_type=jnp.float32)
    middle = (group_rows.astype(jnp.float32) + attn_sum).astype(jnp.bfloat16)
    segment = norm_rows(middle)
    gate_value = jnp.dot(segment, gate_up_weight[0], preferred_element_type=jnp.float32)
    upward = jnp.dot(segment, gate_up_weight[1], preferred_element_type=jnp.float32)
    hidden = (jax.nn.silu(gate_value) * upward).astype(jnp.bfloat16)
    ffn_sum = sum_scatter_rows(
        jnp.dot(hidden, down_weight, preferred_element_type=jnp.float32).astype(jnp.bfloat16),
        "tensor",
    )
    own_middle = lax.dynamic_slice_in_dim(middle, tensor_rank * row_count, row_count, 0)
    return (own_middle.astype(jnp.float32) + ffn_sum).astype(jnp.bfloat16)


def solution(mesh):
    return jax.shard_map(
        on_device,
        mesh=mesh,
        in_specs=(
            P(("dp", "tensor"), None),
            P("dp", None),
            P(),
            P(("dp", "tensor"), None),
            P(None, "tensor"),
            P(),
            P(),
            P("tensor", None),
            P(None, None, "tensor"),
            P("tensor", None),
        ),
        out_specs=P(("dp", "tensor"), None),
        check_vma=False,
    )
```

```python
import math

import jax
import jax.numpy as jnp
from jax import lax
from jax.sharding import PartitionSpec as P

QH = 16
KVH = 4
HD = 64
PLEN = 4096


NEG_FILL = -1e30


def token_layout(lengths, total_rows):
    ends_at = jnp.cumsum(lengths)
    starts_at = ends_at - lengths
    indices = jnp.arange(total_rows, dtype=jnp.int32)
    request = jnp.sum((indices[:, None] >= ends_at[None, :]).astype(jnp.int32), axis=1)
    begins = jnp.max(
        jnp.where(starts_at[None, :] <= indices[:, None], starts_at[None, :], 0), axis=1
    )
    return ((PLEN + indices - begins).astype(jnp.float32), request)


def rope_tables(positions):
    halves = HD // 2
    steps_float = jnp.arange(halves, dtype=jnp.float32)
    inverse = jnp.exp(steps_float * (-2.0 * math.log(10000.0) / HD))
    angles = positions[:, None] * inverse[None, :]
    return (jnp.cos(angles), jnp.sin(angles))


def rotate(values, cos_table, sin_table):
    halves = values.shape[-1] // 2
    former = values[..., :halves]
    latter = values[..., halves:]
    cos_rows = cos_table[:, None, :]
    sin_rows = sin_table[:, None, :]
    return jnp.concatenate(
        [former * cos_rows - latter * sin_rows, latter * cos_rows + former * sin_rows], axis=-1
    )


def norm_rows(inputs):
    floats = inputs.astype(jnp.float32)
    return (floats * lax.rsqrt(jnp.mean(floats * floats, axis=-1, keepdims=True) + 1e-05)).astype(
        jnp.bfloat16
    )


def softmax_block(queries, keys_block, values_block, scaling, allowed):
    scores = (
        jnp.einsum("thd,nhd->thn", queries, keys_block, preferred_element_type=jnp.float32)
        * scaling
    )
    if allowed is not None:
        scores = jnp.where(allowed, scores, NEG_FILL)
    top_score = jnp.max(scores, axis=2)
    exponent = jnp.exp(scores - top_score[:, :, None])
    weight = jnp.sum(exponent, axis=2)
    blended = jnp.einsum(
        "thn,nhd->thd",
        exponent.astype(jnp.bfloat16),
        values_block,
        preferred_element_type=jnp.float32,
    )
    return (top_score, weight, blended)


def merge_states(former, latter):
    top_one, weight_one, blend_one = former
    top_two, weight_two, blend_two = latter
    overall = jnp.maximum(top_one, top_two)
    factor_one = jnp.exp(top_one - overall)
    factor_two = jnp.exp(top_two - overall)
    return (
        overall,
        weight_one * factor_one + weight_two * factor_two,
        blend_one * factor_one[:, :, None] + blend_two * factor_two[:, :, None],
    )


def gather_rows(values, axis):
    count = lax.axis_size(axis)
    copies = jnp.broadcast_to(values[None], (count,) + values.shape)
    received = lax.all_to_all(copies, axis, 0, 0, tiled=True)
    return received.reshape((count * values.shape[0],) + values.shape[1:])


def sum_scatter_rows(values, axis):
    count = lax.axis_size(axis)
    parts = values.reshape((count, values.shape[0] // count) + values.shape[1:])
    received = lax.all_to_all(parts, axis, 0, 0, tiled=True)
    return jnp.sum(received.astype(jnp.float32), axis=0)


CORES = 2


def fetch_slot(prefix_cache, group_prefix, group_rank, rider):
    group_count = lax.axis_size("dp")
    chips = group_count // CORES
    chip = group_rank // CORES
    core = group_rank % CORES
    slot_wanted = group_prefix[group_rank]
    partner_slot = group_prefix[group_rank ^ 1]
    mine_at = (slot_wanted // CORES - chip) % chips
    theirs_at = (partner_slot // CORES - chip) % chips
    onward = [(i, (i + CORES) % group_count) for i in range(group_count)]
    backward = [(i, (i - CORES) % group_count) for i in range(group_count)]
    mine = prefix_cache
    theirs = prefix_cache
    ahead = prefix_cache
    behind = prefix_cache
    for step in range(1, chips // 2 + 1):
        if step == chips - step:
            rows = ahead.shape[1] // 2
            first = lax.ppermute(ahead[:, :rows], "dp", onward)
            second = lax.ppermute(behind[:, rows:], "dp", backward)
            far = jnp.concatenate([first, second], axis=1)
            mine = jnp.where(mine_at == step, far, mine)
            theirs = jnp.where(theirs_at == step, far, theirs)
            break
        ahead = lax.ppermute(ahead, "dp", onward)
        mine = jnp.where(mine_at == (chips - step) % chips, ahead, mine)
        theirs = jnp.where(theirs_at == (chips - step) % chips, ahead, theirs)
        if step < chips - step:
            behind = lax.ppermute(behind, "dp", backward)
            mine = jnp.where(mine_at == step, behind, mine)
            theirs = jnp.where(theirs_at == step, behind, theirs)
        if step == 1:
            ahead, behind, rider = lax.optimization_barrier((ahead, behind, rider))
        mine, theirs, ahead, behind = lax.optimization_barrier((mine, theirs, ahead, behind))
    swapped = lax.ppermute(theirs, "dp", [(i, i ^ 1) for i in range(group_count)])
    return slot_wanted % CORES == core, mine, swapped, rider


def on_device(
    tokens,
    lengths,
    group_prefix,
    prefix_cache,
    query_weight,
    key_weight,
    value_weight,
    out_weight,
    gate_up_weight,
    down_weight,
):
    tensor_count = lax.axis_size("tensor")
    tensor_rank = lax.axis_index("tensor")
    group_rank = lax.axis_index("dp")
    row_count = tokens.shape[0]
    group_tokens = row_count * tensor_count
    local_heads = query_weight.shape[1] // HD
    head_ratio = QH // KVH
    local_kv = max(1, local_heads // head_ratio)
    repeat_by = local_heads // local_kv
    kv_first = tensor_rank * local_heads // head_ratio
    kv_total = KVH * HD
    query_width = local_heads * HD
    kv_width = local_kv * HD
    scaling = 1.0 / math.sqrt(HD)
    positions, request = token_layout(lengths[0], group_tokens)
    cos_table, sin_table = rope_tables(positions)
    key_cols = lax.dynamic_slice_in_dim(key_weight, kv_first * HD, kv_width, 1)
    value_cols = lax.dynamic_slice_in_dim(value_weight, kv_first * HD, kv_width, 1)
    projection = jnp.concatenate([query_weight, key_cols, value_cols], axis=1)

    shard_rows = prefix_cache.shape[0]
    kv_groups = KVH // local_kv
    by_head = prefix_cache.reshape(shard_rows, 2, kv_groups, kv_width)
    by_head = jnp.transpose(by_head, (2, 0, 1, 3)).reshape(kv_groups, shard_rows, 2 * kv_width)
    on_core, mine, swapped, projection = fetch_slot(by_head, group_prefix, group_rank, projection)
    out_full = lax.all_gather(out_weight, "tensor", axis=0, tiled=True)
    outgoing = jnp.where(
        on_core,
        jnp.repeat(mine, tensor_count // kv_groups, axis=0),
        jnp.repeat(swapped, tensor_count // kv_groups, axis=0),
    )
    incoming = lax.all_to_all(outgoing, "tensor", 0, 0, tiled=True)
    seg_rows = tensor_count * shard_rows
    incoming = incoming.reshape(seg_rows, 2 * kv_width)
    keys_block = jnp.repeat(incoming[:, :kv_width].reshape(seg_rows, local_kv, HD), repeat_by, axis=1)
    values_block = jnp.repeat(incoming[:, kv_width:].reshape(seg_rows, local_kv, HD), repeat_by, axis=1)

    group_rows = gather_rows(tokens, "tensor")
    segment = norm_rows(group_rows)
    seg_rows = segment.shape[0]
    mapped = jnp.dot(segment, projection, preferred_element_type=jnp.float32)
    query_part = rotate(
        mapped[:, :query_width].reshape(seg_rows, local_heads, HD), cos_table, sin_table
    )
    key_part = rotate(
        mapped[:, query_width : query_width + kv_width].reshape(seg_rows, local_kv, HD),
        cos_table,
        sin_table,
    )
    projected = jnp.concatenate(
        [
            query_part.reshape(seg_rows, query_width),
            key_part.reshape(seg_rows, kv_width),
            mapped[:, query_width + kv_width :],
        ],
        axis=1,
    ).astype(jnp.bfloat16)
    queries = projected[:, :query_width].reshape(group_tokens, local_heads, HD)
    own_keys = jnp.repeat(
        projected[:, query_width : query_width + kv_width].reshape(group_tokens, local_kv, HD),
        repeat_by,
        axis=1,
    )
    own_values = jnp.repeat(
        projected[:, query_width + kv_width :].reshape(group_tokens, local_kv, HD),
        repeat_by,
        axis=1,
    )
    start_state = (
        jnp.full((group_tokens, local_heads), NEG_FILL, jnp.float32),
        jnp.zeros((group_tokens, local_heads), jnp.float32),
        jnp.zeros((group_tokens, local_heads, HD), jnp.float32),
    )
    prefix_state = merge_states(
        start_state, softmax_block(queries, keys_block, values_block, scaling, None)
    )
    indices = jnp.arange(group_tokens, dtype=jnp.int32)
    allowed = (request[:, None] == request[None, :]) & (indices[None, :] <= indices[:, None])
    suffix_state = softmax_block(queries, own_keys, own_values, scaling, allowed[:, None, :])
    top_score, weight, blended = merge_states(prefix_state, suffix_state)
    attended = (blended / weight[:, :, None]).astype(jnp.bfloat16).reshape(group_tokens, query_width)
    every_head = gather_rows(jnp.transpose(attended)[None], "tensor")
    every_head = jnp.transpose(every_head.reshape(tensor_count * query_width, group_tokens))
    attn_sum = jnp.dot(every_head, out_full, preferred_element_type=jnp.float32)
    middle = (group_rows.astype(jnp.float32) + attn_sum).astype(jnp.bfloat16)
    segment = norm_rows(middle)
    gate_value = jnp.dot(segment, gate_up_weight[0], preferred_element_type=jnp.float32)
    upward = jnp.dot(segment, gate_up_weight[1], preferred_element_type=jnp.float32)
    hidden = (jax.nn.silu(gate_value) * upward).astype(jnp.bfloat16)
    ffn_sum = sum_scatter_rows(
        jnp.dot(hidden, down_weight, preferred_element_type=jnp.float32).astype(jnp.bfloat16),
        "tensor",
    )
    own_middle = lax.dynamic_slice_in_dim(middle, tensor_rank * row_count, row_count, 0)
    return (own_middle.astype(jnp.float32) + ffn_sum).astype(jnp.bfloat16)


def solution(mesh):
    return jax.shard_map(
        on_device,
        mesh=mesh,
        in_specs=(
            P(("dp", "tensor"), None),
            P("dp", None),
            P(),
            P(("dp", "tensor"), None),
            P(None, "tensor"),
            P(),
            P(),
            P("tensor", None),
            P(None, None, "tensor"),
            P("tensor", None),
        ),
        out_specs=P(("dp", "tensor"), None),
        check_vma=False,
    )
```

```python
import math

import jax
import jax.numpy as jnp
from jax import lax
from jax.sharding import PartitionSpec as P

QH = 16
KVH = 4
HD = 64
PLEN = 4096


NEG_FILL = -1e30


def token_layout(lengths, total_rows):
    ends_at = jnp.cumsum(lengths)
    starts_at = ends_at - lengths
    indices = jnp.arange(total_rows, dtype=jnp.int32)
    request = jnp.sum((indices[:, None] >= ends_at[None, :]).astype(jnp.int32), axis=1)
    begins = jnp.max(
        jnp.where(starts_at[None, :] <= indices[:, None], starts_at[None, :], 0), axis=1
    )
    return ((PLEN + indices - begins).astype(jnp.float32), request)


def rope_tables(positions):
    halves = HD // 2
    steps_float = jnp.arange(halves, dtype=jnp.float32)
    inverse = jnp.exp(steps_float * (-2.0 * math.log(10000.0) / HD))
    angles = positions[:, None] * inverse[None, :]
    return (jnp.cos(angles), jnp.sin(angles))


def rotate(values, cos_table, sin_table):
    halves = values.shape[-1] // 2
    former = values[..., :halves]
    latter = values[..., halves:]
    cos_rows = cos_table[:, None, :]
    sin_rows = sin_table[:, None, :]
    return jnp.concatenate(
        [former * cos_rows - latter * sin_rows, latter * cos_rows + former * sin_rows], axis=-1
    )


def norm_rows(inputs):
    floats = inputs.astype(jnp.float32)
    return (floats * lax.rsqrt(jnp.mean(floats * floats, axis=-1, keepdims=True) + 1e-05)).astype(
        jnp.bfloat16
    )


def softmax_block(queries, keys_block, values_block, scaling, allowed):
    scores = (
        jnp.einsum("thd,nhd->thn", queries, keys_block, preferred_element_type=jnp.float32)
        * scaling
    )
    if allowed is not None:
        scores = jnp.where(allowed, scores, NEG_FILL)
    top_score = jnp.max(scores, axis=2)
    exponent = jnp.exp(scores - top_score[:, :, None])
    weight = jnp.sum(exponent, axis=2)
    blended = jnp.einsum(
        "thn,nhd->thd",
        exponent.astype(jnp.bfloat16),
        values_block,
        preferred_element_type=jnp.float32,
    )
    return (top_score, weight, blended)


def merge_states(former, latter):
    top_one, weight_one, blend_one = former
    top_two, weight_two, blend_two = latter
    overall = jnp.maximum(top_one, top_two)
    factor_one = jnp.exp(top_one - overall)
    factor_two = jnp.exp(top_two - overall)
    return (
        overall,
        weight_one * factor_one + weight_two * factor_two,
        blend_one * factor_one[:, :, None] + blend_two * factor_two[:, :, None],
    )


def gather_rows(values, axis):
    count = lax.axis_size(axis)
    copies = jnp.broadcast_to(values[None], (count,) + values.shape)
    received = lax.all_to_all(copies, axis, 0, 0, tiled=True)
    return received.reshape((count * values.shape[0],) + values.shape[1:])


def sum_scatter_rows(values, axis):
    count = lax.axis_size(axis)
    parts = values.reshape((count, values.shape[0] // count) + values.shape[1:])
    received = lax.all_to_all(parts, axis, 0, 0, tiled=True)
    return jnp.sum(received.astype(jnp.float32), axis=0)


CORES = 2


def fetch_slot(prefix_cache, group_prefix, group_rank, rider):
    group_count = lax.axis_size("dp")
    chips = group_count // CORES
    chip = group_rank // CORES
    core = group_rank % CORES
    slot_wanted = group_prefix[group_rank]
    partner_slot = group_prefix[group_rank ^ 1]
    mine_at = (slot_wanted // CORES - chip) % chips
    theirs_at = (partner_slot // CORES - chip) % chips
    onward = [(i, (i + CORES) % group_count) for i in range(group_count)]
    backward = [(i, (i - CORES) % group_count) for i in range(group_count)]
    mine = prefix_cache
    theirs = prefix_cache
    ahead = prefix_cache
    behind = prefix_cache
    for step in range(1, chips // 2 + 1):
        ahead = lax.ppermute(ahead, "dp", onward)
        mine = jnp.where(mine_at == (chips - step) % chips, ahead, mine)
        theirs = jnp.where(theirs_at == (chips - step) % chips, ahead, theirs)
        if step < chips - step:
            behind = lax.ppermute(behind, "dp", backward)
            mine = jnp.where(mine_at == step, behind, mine)
            theirs = jnp.where(theirs_at == step, behind, theirs)
        if step == 1:
            ahead, behind, rider = lax.optimization_barrier((ahead, behind, rider))
        mine, theirs, ahead, behind = lax.optimization_barrier((mine, theirs, ahead, behind))
    swapped = lax.ppermute(theirs, "dp", [(i, i ^ 1) for i in range(group_count)])
    return slot_wanted % CORES == core, mine, swapped, rider


def on_device(
    tokens,
    lengths,
    group_prefix,
    prefix_cache,
    query_weight,
    key_weight,
    value_weight,
    out_weight,
    gate_up_weight,
    down_weight,
):
    tensor_count = lax.axis_size("tensor")
    tensor_rank = lax.axis_index("tensor")
    group_rank = lax.axis_index("dp")
    row_count = tokens.shape[0]
    group_tokens = row_count * tensor_count
    local_heads = query_weight.shape[1] // HD
    head_ratio = QH // KVH
    local_kv = max(1, local_heads // head_ratio)
    repeat_by = local_heads // local_kv
    kv_first = tensor_rank * local_heads // head_ratio
    kv_total = KVH * HD
    query_width = local_heads * HD
    kv_width = local_kv * HD
    scaling = 1.0 / math.sqrt(HD)
    positions, request = token_layout(lengths[0], group_tokens)
    cos_table, sin_table = rope_tables(positions)
    key_cols = lax.dynamic_slice_in_dim(key_weight, kv_first * HD, kv_width, 1)
    value_cols = lax.dynamic_slice_in_dim(value_weight, kv_first * HD, kv_width, 1)
    projection = jnp.concatenate([query_weight, key_cols, value_cols], axis=1)

    shard_rows = prefix_cache.shape[0]
    kv_groups = KVH // local_kv
    by_head = prefix_cache.reshape(shard_rows, 2, kv_groups, kv_width)
    by_head = jnp.transpose(by_head, (2, 0, 1, 3)).reshape(kv_groups, shard_rows, 2 * kv_width)
    on_core, mine, swapped, projection = fetch_slot(by_head, group_prefix, group_rank, projection)
    out_full = lax.all_gather(out_weight, "tensor", axis=0, tiled=True)
    outgoing = jnp.where(
        on_core,
        jnp.repeat(mine, tensor_count // kv_groups, axis=0),
        jnp.repeat(swapped, tensor_count // kv_groups, axis=0),
    )
    incoming = lax.all_to_all(outgoing, "tensor", 0, 0, tiled=True)
    seg_rows = tensor_count * shard_rows
    incoming = incoming.reshape(seg_rows, 2 * kv_width)
    keys_block = jnp.repeat(incoming[:, :kv_width].reshape(seg_rows, local_kv, HD), repeat_by, axis=1)
    values_block = jnp.repeat(incoming[:, kv_width:].reshape(seg_rows, local_kv, HD), repeat_by, axis=1)

    group_rows = gather_rows(tokens, "tensor")
    segment = norm_rows(group_rows)
    seg_rows = segment.shape[0]
    mapped = jnp.dot(segment, projection, preferred_element_type=jnp.float32)
    query_part = rotate(
        mapped[:, :query_width].reshape(seg_rows, local_heads, HD), cos_table, sin_table
    )
    key_part = rotate(
        mapped[:, query_width : query_width + kv_width].reshape(seg_rows, local_kv, HD),
        cos_table,
        sin_table,
    )
    projected = jnp.concatenate(
        [
            query_part.reshape(seg_rows, query_width),
            key_part.reshape(seg_rows, kv_width),
            mapped[:, query_width + kv_width :],
        ],
        axis=1,
    ).astype(jnp.bfloat16)
    queries = projected[:, :query_width].reshape(group_tokens, local_heads, HD)
    own_keys = jnp.repeat(
        projected[:, query_width : query_width + kv_width].reshape(group_tokens, local_kv, HD),
        repeat_by,
        axis=1,
    )
    own_values = jnp.repeat(
        projected[:, query_width + kv_width :].reshape(group_tokens, local_kv, HD),
        repeat_by,
        axis=1,
    )
    every_key = jnp.concatenate([keys_block, own_keys], axis=0)
    every_value = jnp.concatenate([values_block, own_values], axis=0)
    indices = jnp.arange(group_tokens, dtype=jnp.int32)
    allowed = (request[:, None] == request[None, :]) & (indices[None, :] <= indices[:, None])
    allowed = jnp.concatenate([jnp.ones((group_tokens, keys_block.shape[0]), bool), allowed], axis=1)
    top_score, weight, blended = softmax_block(
        queries, every_key, every_value, scaling, allowed[:, None, :]
    )
    attended = (blended / weight[:, :, None]).astype(jnp.bfloat16).reshape(group_tokens, query_width)
    every_head = gather_rows(jnp.transpose(attended)[None], "tensor")
    every_head = jnp.transpose(every_head.reshape(tensor_count * query_width, group_tokens))
    attn_sum = jnp.dot(every_head, out_full, preferred_element_type=jnp.float32)
    middle = (group_rows.astype(jnp.float32) + attn_sum).astype(jnp.bfloat16)
    segment = norm_rows(middle)
    gate_value = jnp.dot(segment, gate_up_weight[0], preferred_element_type=jnp.float32)
    upward = jnp.dot(segment, gate_up_weight[1], preferred_element_type=jnp.float32)
    hidden = (jax.nn.silu(gate_value) * upward).astype(jnp.bfloat16)
    ffn_sum = sum_scatter_rows(
        jnp.dot(hidden, down_weight, preferred_element_type=jnp.float32).astype(jnp.bfloat16),
        "tensor",
    )
    own_middle = lax.dynamic_slice_in_dim(middle, tensor_rank * row_count, row_count, 0)
    return (own_middle.astype(jnp.float32) + ffn_sum).astype(jnp.bfloat16)


def solution(mesh):
    return jax.shard_map(
        on_device,
        mesh=mesh,
        in_specs=(
            P(("dp", "tensor"), None),
            P("dp", None),
            P(),
            P(("dp", "tensor"), None),
            P(None, "tensor"),
            P(),
            P(),
            P("tensor", None),
            P(None, None, "tensor"),
            P("tensor", None),
        ),
        out_specs=P(("dp", "tensor"), None),
        check_vma=False,
    )
```

```python
import math

import jax
import jax.numpy as jnp
from jax import lax
from jax.sharding import PartitionSpec as P

QH = 16
KVH = 4
HD = 64
PLEN = 4096


NEG_FILL = -1e30


def token_layout(lengths, total_rows):
    ends_at = jnp.cumsum(lengths)
    starts_at = ends_at - lengths
    indices = jnp.arange(total_rows, dtype=jnp.int32)
    request = jnp.sum((indices[:, None] >= ends_at[None, :]).astype(jnp.int32), axis=1)
    begins = jnp.max(
        jnp.where(starts_at[None, :] <= indices[:, None], starts_at[None, :], 0), axis=1
    )
    return ((PLEN + indices - begins).astype(jnp.float32), request)


def rope_tables(positions):
    halves = HD // 2
    steps_float = jnp.arange(halves, dtype=jnp.float32)
    inverse = jnp.exp(steps_float * (-2.0 * math.log(10000.0) / HD))
    angles = positions[:, None] * inverse[None, :]
    return (jnp.cos(angles), jnp.sin(angles))


def rotate(values, cos_table, sin_table):
    halves = values.shape[-1] // 2
    former = values[..., :halves]
    latter = values[..., halves:]
    cos_rows = cos_table[:, None, :]
    sin_rows = sin_table[:, None, :]
    return jnp.concatenate(
        [former * cos_rows - latter * sin_rows, latter * cos_rows + former * sin_rows], axis=-1
    )


def norm_rows(inputs):
    floats = inputs.astype(jnp.float32)
    return (floats * lax.rsqrt(jnp.mean(floats * floats, axis=-1, keepdims=True) + 1e-05)).astype(
        jnp.bfloat16
    )


def softmax_block(queries, keys_block, values_block, scaling, allowed):
    scores = (
        jnp.einsum("thd,nhd->thn", queries, keys_block, preferred_element_type=jnp.float32)
        * scaling
    )
    if allowed is not None:
        scores = jnp.where(allowed, scores, NEG_FILL)
    top_score = jnp.max(scores, axis=2)
    exponent = jnp.exp(scores - top_score[:, :, None])
    weight = jnp.sum(exponent, axis=2)
    blended = jnp.einsum(
        "thn,nhd->thd",
        exponent.astype(jnp.bfloat16),
        values_block,
        preferred_element_type=jnp.float32,
    )
    return (top_score, weight, blended)


def merge_states(former, latter):
    top_one, weight_one, blend_one = former
    top_two, weight_two, blend_two = latter
    overall = jnp.maximum(top_one, top_two)
    factor_one = jnp.exp(top_one - overall)
    factor_two = jnp.exp(top_two - overall)
    return (
        overall,
        weight_one * factor_one + weight_two * factor_two,
        blend_one * factor_one[:, :, None] + blend_two * factor_two[:, :, None],
    )


def gather_rows(values, axis):
    count = lax.axis_size(axis)
    copies = jnp.broadcast_to(values[None], (count,) + values.shape)
    received = lax.all_to_all(copies, axis, 0, 0, tiled=True)
    return received.reshape((count * values.shape[0],) + values.shape[1:])


def sum_scatter_rows(values, axis):
    count = lax.axis_size(axis)
    parts = values.reshape((count, values.shape[0] // count) + values.shape[1:])
    received = lax.all_to_all(parts, axis, 0, 0, tiled=True)
    return jnp.sum(received.astype(jnp.float32), axis=0)


CORES = 2


def fetch_slot(prefix_cache, group_prefix, group_rank, rider):
    group_count = lax.axis_size("dp")
    chips = group_count // CORES
    chip = group_rank // CORES
    core = group_rank % CORES
    slot_wanted = group_prefix[group_rank]
    partner_slot = group_prefix[group_rank ^ 1]
    mine_at = (slot_wanted // CORES - chip) % chips
    theirs_at = (partner_slot // CORES - chip) % chips
    onward = [(i, (i + CORES) % group_count) for i in range(group_count)]
    backward = [(i, (i - CORES) % group_count) for i in range(group_count)]
    mine = prefix_cache
    theirs = prefix_cache
    ahead = prefix_cache
    behind = prefix_cache
    for step in range(1, chips // 2 + 1):
        ahead = lax.ppermute(ahead, "dp", onward)
        mine = jnp.where(mine_at == (chips - step) % chips, ahead, mine)
        theirs = jnp.where(theirs_at == (chips - step) % chips, ahead, theirs)
        if step < chips - step:
            behind = lax.ppermute(behind, "dp", backward)
            mine = jnp.where(mine_at == step, behind, mine)
            theirs = jnp.where(theirs_at == step, behind, theirs)
        if step == 1:
            ahead, behind, rider = lax.optimization_barrier((ahead, behind, rider))
        mine, theirs, ahead, behind = lax.optimization_barrier((mine, theirs, ahead, behind))
    swapped = lax.ppermute(theirs, "dp", [(i, i ^ 1) for i in range(group_count)])
    return slot_wanted % CORES == core, mine, swapped, rider


def on_device(
    tokens,
    lengths,
    group_prefix,
    prefix_cache,
    query_weight,
    key_weight,
    value_weight,
    out_weight,
    gate_up_weight,
    down_weight,
):
    tensor_count = lax.axis_size("tensor")
    tensor_rank = lax.axis_index("tensor")
    group_rank = lax.axis_index("dp")
    row_count = tokens.shape[0]
    group_tokens = row_count * tensor_count
    local_heads = query_weight.shape[1] // HD
    head_ratio = QH // KVH
    local_kv = max(1, local_heads // head_ratio)
    repeat_by = local_heads // local_kv
    kv_first = tensor_rank * local_heads // head_ratio
    kv_total = KVH * HD
    query_width = local_heads * HD
    kv_width = local_kv * HD
    scaling = 1.0 / math.sqrt(HD)
    positions, request = token_layout(lengths[0], group_tokens)
    cos_table, sin_table = rope_tables(positions)
    key_cols = lax.dynamic_slice_in_dim(key_weight, kv_first * HD, kv_width, 1)
    value_cols = lax.dynamic_slice_in_dim(value_weight, kv_first * HD, kv_width, 1)
    projection = jnp.concatenate([query_weight, key_cols, value_cols], axis=1)

    shard_rows = prefix_cache.shape[0]
    kv_groups = KVH // local_kv
    on_core, mine, swapped, projection = fetch_slot(prefix_cache, group_prefix, group_rank, projection)
    out_full = lax.all_gather(out_weight, "tensor", axis=0, tiled=True)
    chosen = jnp.where(on_core, mine, swapped)
    by_head = jnp.stack(
        [
            jnp.concatenate(
                [
                    chosen[:, head * kv_width : (head + 1) * kv_width],
                    chosen[:, kv_total + head * kv_width : kv_total + (head + 1) * kv_width],
                ],
                axis=1,
            )
            for head in range(kv_groups)
        ]
    )
    outgoing = jnp.repeat(by_head, tensor_count // kv_groups, axis=0)
    incoming = lax.all_to_all(outgoing, "tensor", 0, 0, tiled=True)
    seg_rows = tensor_count * shard_rows
    incoming = incoming.reshape(seg_rows, 2 * kv_width)
    keys_block = jnp.repeat(incoming[:, :kv_width].reshape(seg_rows, local_kv, HD), repeat_by, axis=1)
    values_block = jnp.repeat(incoming[:, kv_width:].reshape(seg_rows, local_kv, HD), repeat_by, axis=1)

    group_rows = gather_rows(tokens, "tensor")
    segment = norm_rows(group_rows)
    seg_rows = segment.shape[0]
    mapped = jnp.dot(segment, projection, preferred_element_type=jnp.float32)
    query_part = rotate(
        mapped[:, :query_width].reshape(seg_rows, local_heads, HD), cos_table, sin_table
    )
    key_part = rotate(
        mapped[:, query_width : query_width + kv_width].reshape(seg_rows, local_kv, HD),
        cos_table,
        sin_table,
    )
    projected = jnp.concatenate(
        [
            query_part.reshape(seg_rows, query_width),
            key_part.reshape(seg_rows, kv_width),
            mapped[:, query_width + kv_width :],
        ],
        axis=1,
    ).astype(jnp.bfloat16)
    queries = projected[:, :query_width].reshape(group_tokens, local_heads, HD)
    own_keys = jnp.repeat(
        projected[:, query_width : query_width + kv_width].reshape(group_tokens, local_kv, HD),
        repeat_by,
        axis=1,
    )
    own_values = jnp.repeat(
        projected[:, query_width + kv_width :].reshape(group_tokens, local_kv, HD),
        repeat_by,
        axis=1,
    )
    every_key = jnp.concatenate([keys_block, own_keys], axis=0)
    every_value = jnp.concatenate([values_block, own_values], axis=0)
    indices = jnp.arange(group_tokens, dtype=jnp.int32)
    allowed = (request[:, None] == request[None, :]) & (indices[None, :] <= indices[:, None])
    allowed = jnp.concatenate([jnp.ones((group_tokens, keys_block.shape[0]), bool), allowed], axis=1)
    top_score, weight, blended = softmax_block(
        queries, every_key, every_value, scaling, allowed[:, None, :]
    )
    attended = (blended / weight[:, :, None]).astype(jnp.bfloat16).reshape(group_tokens, query_width)
    every_head = gather_rows(jnp.transpose(attended)[None], "tensor")
    every_head = jnp.transpose(every_head.reshape(tensor_count * query_width, group_tokens))
    attn_sum = jnp.dot(every_head, out_full, preferred_element_type=jnp.float32)
    middle = (group_rows.astype(jnp.float32) + attn_sum).astype(jnp.bfloat16)
    segment = norm_rows(middle)
    gate_value = jnp.dot(segment, gate_up_weight[0], preferred_element_type=jnp.float32)
    upward = jnp.dot(segment, gate_up_weight[1], preferred_element_type=jnp.float32)
    hidden = (jax.nn.silu(gate_value) * upward).astype(jnp.bfloat16)
    ffn_sum = sum_scatter_rows(
        jnp.dot(hidden, down_weight, preferred_element_type=jnp.float32).astype(jnp.bfloat16),
        "tensor",
    )
    own_middle = lax.dynamic_slice_in_dim(middle, tensor_rank * row_count, row_count, 0)
    return (own_middle.astype(jnp.float32) + ffn_sum).astype(jnp.bfloat16)


def solution(mesh):
    return jax.shard_map(
        on_device,
        mesh=mesh,
        in_specs=(
            P(("dp", "tensor"), None),
            P("dp", None),
            P(),
            P(("dp", "tensor"), None),
            P(None, "tensor"),
            P(),
            P(),
            P("tensor", None),
            P(None, None, "tensor"),
            P("tensor", None),
        ),
        out_specs=P(("dp", "tensor"), None),
        check_vma=False,
    )
```

```python
import math

import jax
import jax.numpy as jnp
from jax import lax
from jax.sharding import PartitionSpec as P

QH = 16
KVH = 4
HD = 64
PLEN = 4096


NEG_FILL = -1e30


def token_layout(lengths, total_rows):
    ends_at = jnp.cumsum(lengths)
    starts_at = ends_at - lengths
    indices = jnp.arange(total_rows, dtype=jnp.int32)
    request = jnp.sum((indices[:, None] >= ends_at[None, :]).astype(jnp.int32), axis=1)
    begins = jnp.max(
        jnp.where(starts_at[None, :] <= indices[:, None], starts_at[None, :], 0), axis=1
    )
    return ((PLEN + indices - begins).astype(jnp.float32), request)


def rope_tables(positions):
    halves = HD // 2
    steps_float = jnp.arange(halves, dtype=jnp.float32)
    inverse = jnp.exp(steps_float * (-2.0 * math.log(10000.0) / HD))
    angles = positions[:, None] * inverse[None, :]
    return (jnp.cos(angles), jnp.sin(angles))


def rotate(values, cos_table, sin_table):
    halves = values.shape[-1] // 2
    former = values[..., :halves]
    latter = values[..., halves:]
    cos_rows = cos_table[:, None, :]
    sin_rows = sin_table[:, None, :]
    return jnp.concatenate(
        [former * cos_rows - latter * sin_rows, latter * cos_rows + former * sin_rows], axis=-1
    )


def norm_rows(inputs):
    floats = inputs.astype(jnp.float32)
    return (floats * lax.rsqrt(jnp.mean(floats * floats, axis=-1, keepdims=True) + 1e-05)).astype(
        jnp.bfloat16
    )


def softmax_block(queries, keys_block, values_block, scaling, allowed):
    scores = (
        jnp.einsum("thd,nhd->thn", queries, keys_block, preferred_element_type=jnp.float32)
        * scaling
    )
    if allowed is not None:
        scores = jnp.where(allowed, scores, NEG_FILL)
    top_score = jnp.max(scores, axis=2)
    exponent = jnp.exp(scores - top_score[:, :, None])
    weight = jnp.sum(exponent, axis=2)
    blended = jnp.einsum(
        "thn,nhd->thd",
        exponent.astype(jnp.bfloat16),
        values_block,
        preferred_element_type=jnp.float32,
    )
    return (top_score, weight, blended)


def merge_states(former, latter):
    top_one, weight_one, blend_one = former
    top_two, weight_two, blend_two = latter
    overall = jnp.maximum(top_one, top_two)
    factor_one = jnp.exp(top_one - overall)
    factor_two = jnp.exp(top_two - overall)
    return (
        overall,
        weight_one * factor_one + weight_two * factor_two,
        blend_one * factor_one[:, :, None] + blend_two * factor_two[:, :, None],
    )


def gather_rows(values, axis):
    count = lax.axis_size(axis)
    copies = jnp.broadcast_to(values[None], (count,) + values.shape)
    received = lax.all_to_all(copies, axis, 0, 0, tiled=True)
    return received.reshape((count * values.shape[0],) + values.shape[1:])


def sum_scatter_rows(values, axis):
    count = lax.axis_size(axis)
    parts = values.reshape((count, values.shape[0] // count) + values.shape[1:])
    received = lax.all_to_all(parts, axis, 0, 0, tiled=True)
    return jnp.sum(received.astype(jnp.float32), axis=0)


CORES = 2


def fetch_slot(prefix_cache, group_prefix, group_rank, rider):
    group_count = lax.axis_size("dp")
    chips = group_count // CORES
    chip = group_rank // CORES
    core = group_rank % CORES
    slot_wanted = group_prefix[group_rank]
    partner_slot = group_prefix[group_rank ^ 1]
    mine_at = (slot_wanted // CORES - chip) % chips
    theirs_at = (partner_slot // CORES - chip) % chips
    onward = [(i, (i + CORES) % group_count) for i in range(group_count)]
    backward = [(i, (i - CORES) % group_count) for i in range(group_count)]
    mine = prefix_cache
    theirs = prefix_cache
    ahead = prefix_cache
    behind = prefix_cache
    for step in range(1, chips // 2 + 1):
        ahead = lax.ppermute(ahead, "dp", onward)
        mine = jnp.where(mine_at == (chips - step) % chips, ahead, mine)
        theirs = jnp.where(theirs_at == (chips - step) % chips, ahead, theirs)
        if step < chips - step:
            behind = lax.ppermute(behind, "dp", backward)
            mine = jnp.where(mine_at == step, behind, mine)
            theirs = jnp.where(theirs_at == step, behind, theirs)
        if step == 1:
            ahead, behind, rider = lax.optimization_barrier((ahead, behind, rider))
        mine, theirs, ahead, behind = lax.optimization_barrier((mine, theirs, ahead, behind))
    swapped = lax.ppermute(theirs, "dp", [(i, i ^ 1) for i in range(group_count)])
    return slot_wanted % CORES == core, mine, swapped, rider


def on_device(
    tokens,
    lengths,
    group_prefix,
    prefix_cache,
    query_weight,
    key_weight,
    value_weight,
    out_weight,
    gate_up_weight,
    down_weight,
):
    tensor_count = lax.axis_size("tensor")
    tensor_rank = lax.axis_index("tensor")
    group_rank = lax.axis_index("dp")
    row_count = tokens.shape[0]
    group_tokens = row_count * tensor_count
    local_heads = query_weight.shape[1] // HD
    head_ratio = QH // KVH
    local_kv = max(1, local_heads // head_ratio)
    repeat_by = local_heads // local_kv
    kv_first = tensor_rank * local_heads // head_ratio
    kv_total = KVH * HD
    query_width = local_heads * HD
    kv_width = local_kv * HD
    scaling = 1.0 / math.sqrt(HD)
    positions, request = token_layout(lengths[0], group_tokens)
    cos_table, sin_table = rope_tables(positions)
    key_cols = lax.dynamic_slice_in_dim(key_weight, kv_first * HD, kv_width, 1)
    value_cols = lax.dynamic_slice_in_dim(value_weight, kv_first * HD, kv_width, 1)
    projection = jnp.concatenate([query_weight, key_cols, value_cols], axis=1)

    shard_rows = prefix_cache.shape[0]
    kv_groups = KVH // local_kv
    by_head = prefix_cache.reshape(shard_rows, 2, kv_groups, kv_width)
    by_head = jnp.transpose(by_head, (2, 0, 1, 3)).reshape(kv_groups, shard_rows, 2 * kv_width)
    on_core, mine, swapped, projection = fetch_slot(by_head, group_prefix, group_rank, projection)
    out_full = lax.all_gather(out_weight, "tensor", axis=0, tiled=True)
    outgoing = jnp.where(
        on_core,
        jnp.repeat(mine, tensor_count // kv_groups, axis=0),
        jnp.repeat(swapped, tensor_count // kv_groups, axis=0),
    )
    incoming = lax.all_to_all(outgoing, "tensor", 0, 0, tiled=True)
    seg_rows = tensor_count * shard_rows
    incoming = incoming.reshape(seg_rows, 2 * kv_width)
    keys_block = jnp.repeat(incoming[:, :kv_width].reshape(seg_rows, local_kv, HD), repeat_by, axis=1)
    values_block = jnp.repeat(incoming[:, kv_width:].reshape(seg_rows, local_kv, HD), repeat_by, axis=1)

    group_rows = gather_rows(tokens, "tensor")
    segment = norm_rows(group_rows)
    seg_rows = segment.shape[0]
    mapped = jnp.dot(segment, projection, preferred_element_type=jnp.float32)
    query_part = rotate(
        mapped[:, :query_width].reshape(seg_rows, local_heads, HD), cos_table, sin_table
    )
    key_part = rotate(
        mapped[:, query_width : query_width + kv_width].reshape(seg_rows, local_kv, HD),
        cos_table,
        sin_table,
    )
    projected = jnp.concatenate(
        [
            query_part.reshape(seg_rows, query_width),
            key_part.reshape(seg_rows, kv_width),
            mapped[:, query_width + kv_width :],
        ],
        axis=1,
    ).astype(jnp.bfloat16)
    queries = projected[:, :query_width].reshape(group_tokens, local_heads, HD)
    own_keys = jnp.repeat(
        projected[:, query_width : query_width + kv_width].reshape(group_tokens, local_kv, HD),
        repeat_by,
        axis=1,
    )
    own_values = jnp.repeat(
        projected[:, query_width + kv_width :].reshape(group_tokens, local_kv, HD),
        repeat_by,
        axis=1,
    )
    indices = jnp.arange(group_tokens, dtype=jnp.int32)
    allowed = (request[:, None] == request[None, :]) & (indices[None, :] <= indices[:, None])
    prefix_scores = (
        jnp.einsum("thd,nhd->thn", queries, keys_block, preferred_element_type=jnp.float32) * scaling
    )
    own_scores = (
        jnp.einsum("thd,nhd->thn", queries, own_keys, preferred_element_type=jnp.float32) * scaling
    )
    own_scores = jnp.where(allowed[:, None, :], own_scores, NEG_FILL)
    top_score = jnp.maximum(jnp.max(prefix_scores, axis=2), jnp.max(own_scores, axis=2))
    prefix_exp = jnp.exp(prefix_scores - top_score[:, :, None])
    own_exp = jnp.exp(own_scores - top_score[:, :, None])
    weight = jnp.sum(prefix_exp, axis=2) + jnp.sum(own_exp, axis=2)
    blended = jnp.einsum(
        "thn,nhd->thd", prefix_exp.astype(jnp.bfloat16), values_block, preferred_element_type=jnp.float32
    ) + jnp.einsum(
        "thn,nhd->thd", own_exp.astype(jnp.bfloat16), own_values, preferred_element_type=jnp.float32
    )
    attended = (blended / weight[:, :, None]).astype(jnp.bfloat16).reshape(group_tokens, query_width)
    every_head = gather_rows(jnp.transpose(attended)[None], "tensor")
    every_head = jnp.transpose(every_head.reshape(tensor_count * query_width, group_tokens))
    attn_sum = jnp.dot(every_head, out_full, preferred_element_type=jnp.float32)
    middle = (group_rows.astype(jnp.float32) + attn_sum).astype(jnp.bfloat16)
    segment = norm_rows(middle)
    gate_value = jnp.dot(segment, gate_up_weight[0], preferred_element_type=jnp.float32)
    upward = jnp.dot(segment, gate_up_weight[1], preferred_element_type=jnp.float32)
    hidden = (jax.nn.silu(gate_value) * upward).astype(jnp.bfloat16)
    ffn_sum = sum_scatter_rows(
        jnp.dot(hidden, down_weight, preferred_element_type=jnp.float32).astype(jnp.bfloat16),
        "tensor",
    )
    own_middle = lax.dynamic_slice_in_dim(middle, tensor_rank * row_count, row_count, 0)
    return (own_middle.astype(jnp.float32) + ffn_sum).astype(jnp.bfloat16)


def solution(mesh):
    return jax.shard_map(
        on_device,
        mesh=mesh,
        in_specs=(
            P(("dp", "tensor"), None),
            P("dp", None),
            P(),
            P(("dp", "tensor"), None),
            P(None, "tensor"),
            P(),
            P(),
            P("tensor", None),
            P(None, None, "tensor"),
            P("tensor", None),
        ),
        out_specs=P(("dp", "tensor"), None),
        check_vma=False,
    )
```

```python
import math

import jax
import jax.numpy as jnp
from jax import lax
from jax.sharding import PartitionSpec as P

QH = 16
KVH = 4
HD = 64
PLEN = 4096


NEG_FILL = -1e30


def token_layout(lengths, total_rows):
    ends_at = jnp.cumsum(lengths)
    starts_at = ends_at - lengths
    indices = jnp.arange(total_rows, dtype=jnp.int32)
    request = jnp.sum((indices[:, None] >= ends_at[None, :]).astype(jnp.int32), axis=1)
    begins = jnp.max(
        jnp.where(starts_at[None, :] <= indices[:, None], starts_at[None, :], 0), axis=1
    )
    return ((PLEN + indices - begins).astype(jnp.float32), request)


def rope_tables(positions):
    halves = HD // 2
    steps_float = jnp.arange(halves, dtype=jnp.float32)
    inverse = jnp.exp(steps_float * (-2.0 * math.log(10000.0) / HD))
    angles = positions[:, None] * inverse[None, :]
    return (jnp.cos(angles), jnp.sin(angles))


def rotate(values, cos_table, sin_table):
    halves = values.shape[-1] // 2
    former = values[..., :halves]
    latter = values[..., halves:]
    cos_rows = cos_table[:, None, :]
    sin_rows = sin_table[:, None, :]
    return jnp.concatenate(
        [former * cos_rows - latter * sin_rows, latter * cos_rows + former * sin_rows], axis=-1
    )


def norm_rows(inputs):
    floats = inputs.astype(jnp.float32)
    return (floats * lax.rsqrt(jnp.mean(floats * floats, axis=-1, keepdims=True) + 1e-05)).astype(
        jnp.bfloat16
    )


def softmax_block(queries, keys_block, values_block, scaling, allowed):
    scores = (
        jnp.einsum("thd,nhd->thn", queries, keys_block, preferred_element_type=jnp.float32)
        * scaling
    )
    if allowed is not None:
        scores = jnp.where(allowed, scores, NEG_FILL)
    top_score = jnp.max(scores, axis=2)
    exponent = jnp.exp(scores - top_score[:, :, None])
    weight = jnp.sum(exponent, axis=2)
    blended = jnp.einsum(
        "thn,nhd->thd",
        exponent.astype(jnp.bfloat16),
        values_block,
        preferred_element_type=jnp.float32,
    )
    return (top_score, weight, blended)


def merge_states(former, latter):
    top_one, weight_one, blend_one = former
    top_two, weight_two, blend_two = latter
    overall = jnp.maximum(top_one, top_two)
    factor_one = jnp.exp(top_one - overall)
    factor_two = jnp.exp(top_two - overall)
    return (
        overall,
        weight_one * factor_one + weight_two * factor_two,
        blend_one * factor_one[:, :, None] + blend_two * factor_two[:, :, None],
    )


def gather_rows(values, axis):
    count = lax.axis_size(axis)
    copies = jnp.broadcast_to(values[None], (count,) + values.shape)
    received = lax.all_to_all(copies, axis, 0, 0, tiled=True)
    return received.reshape((count * values.shape[0],) + values.shape[1:])


def sum_scatter_rows(values, axis):
    count = lax.axis_size(axis)
    parts = values.reshape((count, values.shape[0] // count) + values.shape[1:])
    received = lax.all_to_all(parts, axis, 0, 0, tiled=True)
    return jnp.sum(received.astype(jnp.float32), axis=0)


CORES = 2


def fetch_slot(prefix_cache, group_prefix, group_rank, rider):
    group_count = lax.axis_size("dp")
    chips = group_count // CORES
    chip = group_rank // CORES
    core = group_rank % CORES
    slot_wanted = group_prefix[group_rank]
    partner_slot = group_prefix[group_rank ^ 1]
    mine_at = (slot_wanted // CORES - chip) % chips
    theirs_at = (partner_slot // CORES - chip) % chips
    onward = [(i, (i + CORES) % group_count) for i in range(group_count)]
    backward = [(i, (i - CORES) % group_count) for i in range(group_count)]
    mine = prefix_cache
    theirs = prefix_cache
    ahead = prefix_cache
    behind = prefix_cache
    for step in range(1, chips // 2 + 1):
        ahead = lax.ppermute(ahead, "dp", onward)
        mine = jnp.where(mine_at == (chips - step) % chips, ahead, mine)
        theirs = jnp.where(theirs_at == (chips - step) % chips, ahead, theirs)
        if step < chips - step:
            behind = lax.ppermute(behind, "dp", backward)
            mine = jnp.where(mine_at == step, behind, mine)
            theirs = jnp.where(theirs_at == step, behind, theirs)
        if step == 3:
            ahead, behind, rider = lax.optimization_barrier((ahead, behind, rider))
        mine, theirs, ahead, behind = lax.optimization_barrier((mine, theirs, ahead, behind))
    swapped = lax.ppermute(theirs, "dp", [(i, i ^ 1) for i in range(group_count)])
    return slot_wanted % CORES == core, mine, swapped, rider


def on_device(
    tokens,
    lengths,
    group_prefix,
    prefix_cache,
    query_weight,
    key_weight,
    value_weight,
    out_weight,
    gate_up_weight,
    down_weight,
):
    tensor_count = lax.axis_size("tensor")
    tensor_rank = lax.axis_index("tensor")
    group_rank = lax.axis_index("dp")
    row_count = tokens.shape[0]
    group_tokens = row_count * tensor_count
    local_heads = query_weight.shape[1] // HD
    head_ratio = QH // KVH
    local_kv = max(1, local_heads // head_ratio)
    repeat_by = local_heads // local_kv
    kv_first = tensor_rank * local_heads // head_ratio
    kv_total = KVH * HD
    query_width = local_heads * HD
    kv_width = local_kv * HD
    scaling = 1.0 / math.sqrt(HD)
    positions, request = token_layout(lengths[0], group_tokens)
    cos_table, sin_table = rope_tables(positions)
    key_cols = lax.dynamic_slice_in_dim(key_weight, kv_first * HD, kv_width, 1)
    value_cols = lax.dynamic_slice_in_dim(value_weight, kv_first * HD, kv_width, 1)
    projection = jnp.concatenate([query_weight, key_cols, value_cols], axis=1)

    shard_rows = prefix_cache.shape[0]
    kv_groups = KVH // local_kv
    by_head = prefix_cache.reshape(shard_rows, 2, kv_groups, kv_width)
    by_head = jnp.transpose(by_head, (2, 0, 1, 3)).reshape(kv_groups, shard_rows, 2 * kv_width)
    on_core, mine, swapped, projection = fetch_slot(by_head, group_prefix, group_rank, projection)
    out_full = lax.all_gather(out_weight, "tensor", axis=0, tiled=True)
    outgoing = jnp.where(
        on_core,
        jnp.repeat(mine, tensor_count // kv_groups, axis=0),
        jnp.repeat(swapped, tensor_count // kv_groups, axis=0),
    )
    incoming = lax.all_to_all(outgoing, "tensor", 0, 0, tiled=True)
    seg_rows = tensor_count * shard_rows
    incoming = incoming.reshape(seg_rows, 2 * kv_width)
    keys_block = jnp.repeat(incoming[:, :kv_width].reshape(seg_rows, local_kv, HD), repeat_by, axis=1)
    values_block = jnp.repeat(incoming[:, kv_width:].reshape(seg_rows, local_kv, HD), repeat_by, axis=1)

    group_rows = gather_rows(tokens, "tensor")
    segment = norm_rows(group_rows)
    seg_rows = segment.shape[0]
    mapped = jnp.dot(segment, projection, preferred_element_type=jnp.float32)
    query_part = rotate(
        mapped[:, :query_width].reshape(seg_rows, local_heads, HD), cos_table, sin_table
    )
    key_part = rotate(
        mapped[:, query_width : query_width + kv_width].reshape(seg_rows, local_kv, HD),
        cos_table,
        sin_table,
    )
    projected = jnp.concatenate(
        [
            query_part.reshape(seg_rows, query_width),
            key_part.reshape(seg_rows, kv_width),
            mapped[:, query_width + kv_width :],
        ],
        axis=1,
    ).astype(jnp.bfloat16)
    queries = projected[:, :query_width].reshape(group_tokens, local_heads, HD)
    own_keys = jnp.repeat(
        projected[:, query_width : query_width + kv_width].reshape(group_tokens, local_kv, HD),
        repeat_by,
        axis=1,
    )
    own_values = jnp.repeat(
        projected[:, query_width + kv_width :].reshape(group_tokens, local_kv, HD),
        repeat_by,
        axis=1,
    )
    every_key = jnp.concatenate([keys_block, own_keys], axis=0)
    every_value = jnp.concatenate([values_block, own_values], axis=0)
    indices = jnp.arange(group_tokens, dtype=jnp.int32)
    allowed = (request[:, None] == request[None, :]) & (indices[None, :] <= indices[:, None])
    allowed = jnp.concatenate([jnp.ones((group_tokens, keys_block.shape[0]), bool), allowed], axis=1)
    top_score, weight, blended = softmax_block(
        queries, every_key, every_value, scaling, allowed[:, None, :]
    )
    attended = (blended / weight[:, :, None]).astype(jnp.bfloat16).reshape(group_tokens, query_width)
    every_head = gather_rows(jnp.transpose(attended)[None], "tensor")
    every_head = jnp.transpose(every_head.reshape(tensor_count * query_width, group_tokens))
    attn_sum = jnp.dot(every_head, out_full, preferred_element_type=jnp.float32)
    middle = (group_rows.astype(jnp.float32) + attn_sum).astype(jnp.bfloat16)
    segment = norm_rows(middle)
    gate_value = jnp.dot(segment, gate_up_weight[0], preferred_element_type=jnp.float32)
    upward = jnp.dot(segment, gate_up_weight[1], preferred_element_type=jnp.float32)
    hidden = (jax.nn.silu(gate_value) * upward).astype(jnp.bfloat16)
    ffn_sum = sum_scatter_rows(
        jnp.dot(hidden, down_weight, preferred_element_type=jnp.float32).astype(jnp.bfloat16),
        "tensor",
    )
    own_middle = lax.dynamic_slice_in_dim(middle, tensor_rank * row_count, row_count, 0)
    return (own_middle.astype(jnp.float32) + ffn_sum).astype(jnp.bfloat16)


def solution(mesh):
    return jax.shard_map(
        on_device,
        mesh=mesh,
        in_specs=(
            P(("dp", "tensor"), None),
            P("dp", None),
            P(),
            P(("dp", "tensor"), None),
            P(None, "tensor"),
            P(),
            P(),
            P("tensor", None),
            P(None, None, "tensor"),
            P("tensor", None),
        ),
        out_specs=P(("dp", "tensor"), None),
        check_vma=False,
    )
```

```python
import math

import jax
import jax.numpy as jnp
from jax import lax
from jax.sharding import PartitionSpec as P

QH = 16
KVH = 4
HD = 64
PLEN = 4096


NEG_FILL = -1e30


def token_layout(lengths, total_rows):
    ends_at = jnp.cumsum(lengths)
    starts_at = ends_at - lengths
    indices = jnp.arange(total_rows, dtype=jnp.int32)
    request = jnp.sum((indices[:, None] >= ends_at[None, :]).astype(jnp.int32), axis=1)
    begins = jnp.max(
        jnp.where(starts_at[None, :] <= indices[:, None], starts_at[None, :], 0), axis=1
    )
    return ((PLEN + indices - begins).astype(jnp.float32), request)


def rope_tables(positions):
    halves = HD // 2
    steps_float = jnp.arange(halves, dtype=jnp.float32)
    inverse = jnp.exp(steps_float * (-2.0 * math.log(10000.0) / HD))
    angles = positions[:, None] * inverse[None, :]
    return (jnp.cos(angles), jnp.sin(angles))


def rotate(values, cos_table, sin_table):
    halves = values.shape[-1] // 2
    former = values[..., :halves]
    latter = values[..., halves:]
    cos_rows = cos_table[:, None, :]
    sin_rows = sin_table[:, None, :]
    return jnp.concatenate(
        [former * cos_rows - latter * sin_rows, latter * cos_rows + former * sin_rows], axis=-1
    )


def norm_rows(inputs):
    floats = inputs.astype(jnp.float32)
    return (floats * lax.rsqrt(jnp.mean(floats * floats, axis=-1, keepdims=True) + 1e-05)).astype(
        jnp.bfloat16
    )


def softmax_block(queries, keys_block, values_block, scaling, allowed):
    scores = (
        jnp.einsum("thd,nhd->thn", queries, keys_block, preferred_element_type=jnp.float32)
        * scaling
    )
    if allowed is not None:
        scores = jnp.where(allowed, scores, NEG_FILL)
    top_score = jnp.max(scores, axis=2)
    exponent = jnp.exp(scores - top_score[:, :, None])
    weight = jnp.sum(exponent, axis=2)
    blended = jnp.einsum(
        "thn,nhd->thd",
        exponent.astype(jnp.bfloat16),
        values_block,
        preferred_element_type=jnp.float32,
    )
    return (top_score, weight, blended)


def merge_states(former, latter):
    top_one, weight_one, blend_one = former
    top_two, weight_two, blend_two = latter
    overall = jnp.maximum(top_one, top_two)
    factor_one = jnp.exp(top_one - overall)
    factor_two = jnp.exp(top_two - overall)
    return (
        overall,
        weight_one * factor_one + weight_two * factor_two,
        blend_one * factor_one[:, :, None] + blend_two * factor_two[:, :, None],
    )


def gather_rows(values, axis):
    count = lax.axis_size(axis)
    copies = jnp.broadcast_to(values[None], (count,) + values.shape)
    received = lax.all_to_all(copies, axis, 0, 0, tiled=True)
    return received.reshape((count * values.shape[0],) + values.shape[1:])


def sum_scatter_rows(values, axis):
    count = lax.axis_size(axis)
    parts = values.reshape((count, values.shape[0] // count) + values.shape[1:])
    received = lax.all_to_all(parts, axis, 0, 0, tiled=True)
    return jnp.sum(received.astype(jnp.float32), axis=0)


CORES = 2


def fetch_slot(prefix_cache, group_prefix, group_rank, rider):
    group_count = lax.axis_size("dp")
    chips = group_count // CORES
    chip = group_rank // CORES
    core = group_rank % CORES
    slot_wanted = group_prefix[group_rank]
    partner_slot = group_prefix[group_rank ^ 1]
    mine_at = (slot_wanted // CORES - chip) % chips
    theirs_at = (partner_slot // CORES - chip) % chips
    onward = [(i, (i + CORES) % group_count) for i in range(group_count)]
    backward = [(i, (i - CORES) % group_count) for i in range(group_count)]
    mine = prefix_cache
    theirs = prefix_cache
    ahead = prefix_cache
    behind = prefix_cache
    for step in range(1, chips // 2 + 1):
        ahead = lax.ppermute(ahead, "dp", onward)
        mine = jnp.where(mine_at == (chips - step) % chips, ahead, mine)
        theirs = jnp.where(theirs_at == (chips - step) % chips, ahead, theirs)
        if step < chips - step:
            behind = lax.ppermute(behind, "dp", backward)
            mine = jnp.where(mine_at == step, behind, mine)
            theirs = jnp.where(theirs_at == step, behind, theirs)
        if step == 1:
            ahead, behind, rider = lax.optimization_barrier((ahead, behind, rider))
        mine, theirs, ahead, behind = lax.optimization_barrier((mine, theirs, ahead, behind))
    swapped = lax.ppermute(theirs, "dp", [(i, i ^ 1) for i in range(group_count)])
    return slot_wanted % CORES == core, mine, swapped, rider


def on_device(
    tokens,
    lengths,
    group_prefix,
    prefix_cache,
    query_weight,
    key_weight,
    value_weight,
    out_weight,
    gate_up_weight,
    down_weight,
):
    tensor_count = lax.axis_size("tensor")
    tensor_rank = lax.axis_index("tensor")
    group_rank = lax.axis_index("dp")
    row_count = tokens.shape[0]
    group_tokens = row_count * tensor_count
    local_heads = query_weight.shape[1] // HD
    head_ratio = QH // KVH
    local_kv = max(1, local_heads // head_ratio)
    repeat_by = local_heads // local_kv
    kv_first = tensor_rank * local_heads // head_ratio
    kv_total = KVH * HD
    query_width = local_heads * HD
    kv_width = local_kv * HD
    scaling = 1.0 / math.sqrt(HD)
    positions, request = token_layout(lengths[0], group_tokens)
    cos_table, sin_table = rope_tables(positions)
    key_cols = lax.dynamic_slice_in_dim(key_weight, kv_first * HD, kv_width, 1)
    value_cols = lax.dynamic_slice_in_dim(value_weight, kv_first * HD, kv_width, 1)
    projection = jnp.concatenate([query_weight, key_cols, value_cols], axis=1)

    shard_rows = prefix_cache.shape[0]
    kv_groups = KVH // local_kv
    by_head = prefix_cache.reshape(shard_rows, 2, kv_groups, kv_width)
    by_head = jnp.transpose(by_head, (2, 0, 1, 3)).reshape(kv_groups, shard_rows, 2 * kv_width)
    on_core, mine, swapped, projection = fetch_slot(by_head, group_prefix, group_rank, projection)
    out_full = lax.all_gather(out_weight, "tensor", axis=0, tiled=True)
    outgoing = jnp.where(
        on_core,
        jnp.repeat(mine, tensor_count // kv_groups, axis=0),
        jnp.repeat(swapped, tensor_count // kv_groups, axis=0),
    )
    incoming = lax.all_to_all(outgoing, "tensor", 0, 0, tiled=True)
    seg_rows = tensor_count * shard_rows
    incoming = incoming.reshape(seg_rows, 2 * kv_width)
    keys_block = jnp.repeat(incoming[:, :kv_width].reshape(seg_rows, local_kv, HD), repeat_by, axis=1)
    values_block = jnp.repeat(incoming[:, kv_width:].reshape(seg_rows, local_kv, HD), repeat_by, axis=1)

    group_rows = gather_rows(tokens, "tensor")
    segment = norm_rows(group_rows)
    seg_rows = segment.shape[0]
    mapped = jnp.dot(segment, projection, preferred_element_type=jnp.float32)
    query_part = rotate(
        mapped[:, :query_width].reshape(seg_rows, local_heads, HD), cos_table, sin_table
    )
    key_part = rotate(
        mapped[:, query_width : query_width + kv_width].reshape(seg_rows, local_kv, HD),
        cos_table,
        sin_table,
    )
    projected = jnp.concatenate(
        [
            query_part.reshape(seg_rows, query_width),
            key_part.reshape(seg_rows, kv_width),
            mapped[:, query_width + kv_width :],
        ],
        axis=1,
    ).astype(jnp.bfloat16)
    queries = projected[:, :query_width].reshape(group_tokens, local_heads, HD)
    own_keys = jnp.repeat(
        projected[:, query_width : query_width + kv_width].reshape(group_tokens, local_kv, HD),
        repeat_by,
        axis=1,
    )
    own_values = jnp.repeat(
        projected[:, query_width + kv_width :].reshape(group_tokens, local_kv, HD),
        repeat_by,
        axis=1,
    )
    every_key = jnp.concatenate([keys_block, own_keys], axis=0)
    every_value = jnp.concatenate([values_block, own_values], axis=0)
    indices = jnp.arange(group_tokens, dtype=jnp.int32)
    allowed = (request[:, None] == request[None, :]) & (indices[None, :] <= indices[:, None])
    allowed = jnp.concatenate([jnp.ones((group_tokens, keys_block.shape[0]), bool), allowed], axis=1)
    top_score, weight, blended = softmax_block(
        queries, every_key, every_value, scaling, allowed[:, None, :]
    )
    attended = (blended / weight[:, :, None]).astype(jnp.bfloat16).reshape(group_tokens, query_width)
    every_head = gather_rows(jnp.transpose(attended)[None], "tensor")
    every_head = jnp.transpose(every_head.reshape(tensor_count * query_width, group_tokens))
    attn_sum = jnp.dot(every_head, out_full, preferred_element_type=jnp.float32)
    middle = (group_rows.astype(jnp.float32) + attn_sum).astype(jnp.bfloat16)
    segment = norm_rows(middle)
    gate_value, upward = jnp.einsum(
        "td,kdf->ktf", segment, gate_up_weight, preferred_element_type=jnp.float32
    )
    hidden = (jax.nn.silu(gate_value) * upward).astype(jnp.bfloat16)
    ffn_sum = sum_scatter_rows(
        jnp.dot(hidden, down_weight, preferred_element_type=jnp.float32).astype(jnp.bfloat16),
        "tensor",
    )
    own_middle = lax.dynamic_slice_in_dim(middle, tensor_rank * row_count, row_count, 0)
    return (own_middle.astype(jnp.float32) + ffn_sum).astype(jnp.bfloat16)


def solution(mesh):
    return jax.shard_map(
        on_device,
        mesh=mesh,
        in_specs=(
            P(("dp", "tensor"), None),
            P("dp", None),
            P(),
            P(("dp", "tensor"), None),
            P(None, "tensor"),
            P(),
            P(),
            P("tensor", None),
            P(None, None, "tensor"),
            P("tensor", None),
        ),
        out_specs=P(("dp", "tensor"), None),
        check_vma=False,
    )
```

```python
import math

import jax
import jax.numpy as jnp
from jax import lax
from jax.sharding import PartitionSpec as P

QH = 16
KVH = 4
HD = 64
PLEN = 4096


NEG_FILL = -1e30


def token_layout(lengths, total_rows):
    ends_at = jnp.cumsum(lengths)
    starts_at = ends_at - lengths
    indices = jnp.arange(total_rows, dtype=jnp.int32)
    request = jnp.sum((indices[:, None] >= ends_at[None, :]).astype(jnp.int32), axis=1)
    begins = jnp.max(
        jnp.where(starts_at[None, :] <= indices[:, None], starts_at[None, :], 0), axis=1
    )
    return ((PLEN + indices - begins).astype(jnp.float32), request)


def rope_tables(positions):
    halves = HD // 2
    steps_float = jnp.arange(halves, dtype=jnp.float32)
    inverse = jnp.exp(steps_float * (-2.0 * math.log(10000.0) / HD))
    angles = positions[:, None] * inverse[None, :]
    return (jnp.cos(angles), jnp.sin(angles))


def rotate(values, cos_table, sin_table):
    halves = values.shape[-1] // 2
    former = values[..., :halves]
    latter = values[..., halves:]
    cos_rows = cos_table[:, None, :]
    sin_rows = sin_table[:, None, :]
    return jnp.concatenate(
        [former * cos_rows - latter * sin_rows, latter * cos_rows + former * sin_rows], axis=-1
    )


def norm_rows(inputs):
    floats = inputs.astype(jnp.float32)
    return (floats * lax.rsqrt(jnp.mean(floats * floats, axis=-1, keepdims=True) + 1e-05)).astype(
        jnp.bfloat16
    )


def softmax_block(queries, keys_block, values_block, scaling, allowed):
    scores = (
        jnp.einsum("thd,nhd->thn", queries, keys_block, preferred_element_type=jnp.float32)
        * scaling
    )
    if allowed is not None:
        scores = jnp.where(allowed, scores, NEG_FILL)
    top_score = jnp.max(scores, axis=2)
    exponent = jnp.exp(scores - top_score[:, :, None])
    weight = jnp.sum(exponent, axis=2)
    blended = jnp.einsum(
        "thn,nhd->thd",
        exponent.astype(jnp.bfloat16),
        values_block,
        preferred_element_type=jnp.float32,
    )
    return (top_score, weight, blended)


def merge_states(former, latter):
    top_one, weight_one, blend_one = former
    top_two, weight_two, blend_two = latter
    overall = jnp.maximum(top_one, top_two)
    factor_one = jnp.exp(top_one - overall)
    factor_two = jnp.exp(top_two - overall)
    return (
        overall,
        weight_one * factor_one + weight_two * factor_two,
        blend_one * factor_one[:, :, None] + blend_two * factor_two[:, :, None],
    )


def gather_rows(values, axis):
    count = lax.axis_size(axis)
    copies = jnp.broadcast_to(values[None], (count,) + values.shape)
    received = lax.all_to_all(copies, axis, 0, 0, tiled=True)
    return received.reshape((count * values.shape[0],) + values.shape[1:])


def sum_scatter_rows(values, axis):
    count = lax.axis_size(axis)
    parts = values.reshape((count, values.shape[0] // count) + values.shape[1:])
    received = lax.all_to_all(parts, axis, 0, 0, tiled=True)
    return jnp.sum(received.astype(jnp.float32), axis=0)


CORES = 2


def fetch_slot(prefix_cache, group_prefix, group_rank, rider):
    group_count = lax.axis_size("dp")
    chips = group_count // CORES
    chip = group_rank // CORES
    core = group_rank % CORES
    slot_wanted = group_prefix[group_rank]
    partner_slot = group_prefix[group_rank ^ 1]
    mine_at = (slot_wanted // CORES - chip) % chips
    theirs_at = (partner_slot // CORES - chip) % chips
    onward = [(i, (i + CORES) % group_count) for i in range(group_count)]
    backward = [(i, (i - CORES) % group_count) for i in range(group_count)]
    mine = prefix_cache
    theirs = prefix_cache
    ahead = prefix_cache
    behind = prefix_cache
    for step in range(1, chips // 2 + 1):
        ahead = lax.ppermute(ahead, "dp", onward)
        mine = jnp.where(mine_at == (chips - step) % chips, ahead, mine)
        theirs = jnp.where(theirs_at == (chips - step) % chips, ahead, theirs)
        if step < chips - step:
            behind = lax.ppermute(behind, "dp", backward)
            mine = jnp.where(mine_at == step, behind, mine)
            theirs = jnp.where(theirs_at == step, behind, theirs)
        if step == 1:
            ahead, behind, rider = lax.optimization_barrier((ahead, behind, rider))
        mine, theirs, ahead, behind = lax.optimization_barrier((mine, theirs, ahead, behind))
    swapped = lax.ppermute(theirs, "dp", [(i, i ^ 1) for i in range(group_count)])
    return slot_wanted % CORES == core, mine, swapped, rider


def on_device(
    tokens,
    lengths,
    group_prefix,
    prefix_cache,
    query_weight,
    key_weight,
    value_weight,
    out_weight,
    gate_up_weight,
    down_weight,
):
    tensor_count = lax.axis_size("tensor")
    tensor_rank = lax.axis_index("tensor")
    group_rank = lax.axis_index("dp")
    row_count = tokens.shape[0]
    group_tokens = row_count * tensor_count
    local_heads = query_weight.shape[1] // HD
    head_ratio = QH // KVH
    local_kv = max(1, local_heads // head_ratio)
    repeat_by = local_heads // local_kv
    kv_first = tensor_rank * local_heads // head_ratio
    kv_total = KVH * HD
    query_width = local_heads * HD
    kv_width = local_kv * HD
    scaling = 1.0 / math.sqrt(HD)
    positions, request = token_layout(lengths[0], group_tokens)
    cos_table, sin_table = rope_tables(positions)
    key_cols = lax.dynamic_slice_in_dim(key_weight, kv_first * HD, kv_width, 1)
    value_cols = lax.dynamic_slice_in_dim(value_weight, kv_first * HD, kv_width, 1)
    projection = (query_weight, key_cols, value_cols)

    shard_rows = prefix_cache.shape[0]
    kv_groups = KVH // local_kv
    by_head = prefix_cache.reshape(shard_rows, 2, kv_groups, kv_width)
    by_head = jnp.transpose(by_head, (2, 0, 1, 3)).reshape(kv_groups, shard_rows, 2 * kv_width)
    on_core, mine, swapped, projection = fetch_slot(by_head, group_prefix, group_rank, projection)
    out_full = lax.all_gather(out_weight, "tensor", axis=0, tiled=True)
    outgoing = jnp.where(
        on_core,
        jnp.repeat(mine, tensor_count // kv_groups, axis=0),
        jnp.repeat(swapped, tensor_count // kv_groups, axis=0),
    )
    incoming = lax.all_to_all(outgoing, "tensor", 0, 0, tiled=True)
    seg_rows = tensor_count * shard_rows
    incoming = incoming.reshape(seg_rows, 2 * kv_width)
    keys_block = jnp.repeat(incoming[:, :kv_width].reshape(seg_rows, local_kv, HD), repeat_by, axis=1)
    values_block = jnp.repeat(incoming[:, kv_width:].reshape(seg_rows, local_kv, HD), repeat_by, axis=1)

    group_rows = gather_rows(tokens, "tensor")
    segment = norm_rows(group_rows)
    seg_rows = segment.shape[0]
    mapped = jnp.concatenate(
        [jnp.dot(segment, part, preferred_element_type=jnp.float32) for part in projection], axis=1
    )
    query_part = rotate(
        mapped[:, :query_width].reshape(seg_rows, local_heads, HD), cos_table, sin_table
    )
    key_part = rotate(
        mapped[:, query_width : query_width + kv_width].reshape(seg_rows, local_kv, HD),
        cos_table,
        sin_table,
    )
    projected = jnp.concatenate(
        [
            query_part.reshape(seg_rows, query_width),
            key_part.reshape(seg_rows, kv_width),
            mapped[:, query_width + kv_width :],
        ],
        axis=1,
    ).astype(jnp.bfloat16)
    queries = projected[:, :query_width].reshape(group_tokens, local_heads, HD)
    own_keys = jnp.repeat(
        projected[:, query_width : query_width + kv_width].reshape(group_tokens, local_kv, HD),
        repeat_by,
        axis=1,
    )
    own_values = jnp.repeat(
        projected[:, query_width + kv_width :].reshape(group_tokens, local_kv, HD),
        repeat_by,
        axis=1,
    )
    every_key = jnp.concatenate([keys_block, own_keys], axis=0)
    every_value = jnp.concatenate([values_block, own_values], axis=0)
    indices = jnp.arange(group_tokens, dtype=jnp.int32)
    allowed = (request[:, None] == request[None, :]) & (indices[None, :] <= indices[:, None])
    allowed = jnp.concatenate([jnp.ones((group_tokens, keys_block.shape[0]), bool), allowed], axis=1)
    top_score, weight, blended = softmax_block(
        queries, every_key, every_value, scaling, allowed[:, None, :]
    )
    attended = (blended / weight[:, :, None]).astype(jnp.bfloat16).reshape(group_tokens, query_width)
    every_head = gather_rows(jnp.transpose(attended)[None], "tensor")
    every_head = jnp.transpose(every_head.reshape(tensor_count * query_width, group_tokens))
    attn_sum = jnp.dot(every_head, out_full, preferred_element_type=jnp.float32)
    middle = (group_rows.astype(jnp.float32) + attn_sum).astype(jnp.bfloat16)
    segment = norm_rows(middle)
    gate_value, upward = jnp.einsum(
        "td,kdf->ktf", segment, gate_up_weight, preferred_element_type=jnp.float32
    )
    hidden = (jax.nn.silu(gate_value) * upward).astype(jnp.bfloat16)
    ffn_sum = sum_scatter_rows(
        jnp.dot(hidden, down_weight, preferred_element_type=jnp.float32).astype(jnp.bfloat16),
        "tensor",
    )
    own_middle = lax.dynamic_slice_in_dim(middle, tensor_rank * row_count, row_count, 0)
    return (own_middle.astype(jnp.float32) + ffn_sum).astype(jnp.bfloat16)


def solution(mesh):
    return jax.shard_map(
        on_device,
        mesh=mesh,
        in_specs=(
            P(("dp", "tensor"), None),
            P("dp", None),
            P(),
            P(("dp", "tensor"), None),
            P(None, "tensor"),
            P(),
            P(),
            P("tensor", None),
            P(None, None, "tensor"),
            P("tensor", None),
        ),
        out_specs=P(("dp", "tensor"), None),
        check_vma=False,
    )
```
